512 devices in a mesh: len: 32 (over z, core), xa: 4 (over y), xb: 4 (over x).
Axes of the slice: x: 4, y: 4, z: 16, core: 2. Of those that a mesh axis runs over, the one named last changes fastest.
Arguments:
- displacement: float32 [3, 4096, 4096], P(None, ('xa', 'xb'), 'len'), may hold values from -3 to 3
- velocity: float32 [3, 4096, 4096], P(None, ('xa', 'xb'), 'len'), may hold values from -6 to 6
- anchors: float32 [3, 4096], P(None, ('xa', 'xb')), may hold values from -0.5 to 0.5
- seg_live: int32 [4096, 32], P(('xa', 'xb'), 'len'), may hold values from 1 to 128
- pair_blocks: int32 [32, 16, 16, 32, 2], P('len', ('xa', 'xb')), may hold values from 0 to 255
- pair_count: int32 [32, 16, 16], P('len', ('xa', 'xb')), may hold values from 1 to 32, as said below
Outputs:
- new_velocity: float32 [3, 4096, 4096], P(None, ('xa', 'xb'), 'len')
- new_displacement: float32 [3, 4096, 4096], P(None, ('xa', 'xb'), 'len')
The draws below stay inside these ranges and needn't reach their ends.
Inputs may be any that keep to these rules, and one draw needn't show every extreme that they name: `seg_live`: the first that many segments of a block take part in contact. `pair_blocks`: block numbers local to the device that holds the block. `pair_count`: live pairs from a device to a peer stand in the first slots of that peer's row; slots at or beyond the count hold arbitrary block numbers and carry no pair; the count 32 is reached in every draw.
All inputs are finite; a program needn't handle non-finite values.
Results may differ from the reference program's by a relative error of at most 0.0003.
Values sent between devices are 32-bit elements; how exact they have to be, the bound alone decides.
No kernel may reach another device: no remote copies, remote signals or barrier semaphores. Data moves between devices by JAX's collectives and lax.ppermute only.
A program may use at most 64 MiB of HBM per device.

```python
import jax
import jax.numpy as jnp
from jax import lax

FIB_DEV = 256
SEG_DEV = 128
CAP = 32
PEERS = 16
SLABS = 32
FIBRES = 4096
SEGS = 4096
BLOCKS = 32
BLK_DEV = 256


def draw_pair_count(key, part):
    key_base = jax.random.fold_in(key, 11)
    first_key, second_key, third_key = jax.random.split(key_base, 3)
    spread = jax.random.randint(first_key, (SLABS, PEERS, PEERS), 1, CAP // 4 + 1)
    heavy = jax.random.randint(second_key, (SLABS, PEERS, 1), 0, 4)
    factor = jnp.where(heavy == 0, 4, 1)
    counts = spread * factor
    chosen = jax.random.randint(third_key, (SLABS, 1, 1), 0, PEERS * PEERS)
    position = jnp.arange(PEERS, dtype=jnp.int32)[:, None] * PEERS + jnp.arange(PEERS, dtype=jnp.int32)[None, :]
    counts = jnp.where(position[None] == chosen, CAP, counts)
    return counts.astype(jnp.int32)


def plant(drawn, key, least, high):
    place = [jax.random.randint(jax.random.fold_in(key, axis), (), 0, length) for axis, length in enumerate(drawn.shape)]
    main_axis = drawn.shape.index(max(drawn.shape))
    next_to = place[:main_axis] + [(place[main_axis] + 1) % drawn.shape[main_axis]] + place[main_axis + 1:]
    return drawn.at[tuple(place)].set(least).at[tuple(next_to)].set(high)


def block_scale(rng, shape, pieces, smallest, high):
    def one(axis_at, blocks):
        draws = jax.random.uniform(jax.random.fold_in(jax.random.fold_in(rng, 6), axis_at), (blocks,), jnp.float32, smallest / len(pieces), high / len(pieces))
        return jnp.repeat(jnp.exp(draws), shape[axis_at] // blocks).reshape((-1,) + (1,) * (len(shape) - axis_at - 1))

    level = one(*pieces[0])
    for cut in pieces[1:]:
        level = level * one(*cut)
    return level


def bell_draw(key, shape, width, bound, pieces=(), kind=jnp.bfloat16):
    values = width * jax.random.normal(key, shape, jnp.float32)
    if pieces:
        values = values * block_scale(key, shape, pieces, -0.22, 0.18)
    return jnp.clip(values, -bound, bound).astype(kind)


def setup_inputs(seed: int = 0) -> dict:
    keys = jax.random.split(jax.random.key(seed), 7)
    return {
        "displacement": bell_draw(keys[0], (3, FIBRES, SEGS), 1.0, 3.0, ((1, 16), (2, 32)), jnp.float32),
        "velocity": bell_draw(keys[1], (3, FIBRES, SEGS), 1.0, 6.0, ((1, 16), (2, 32)), jnp.float32),
        "anchors": jnp.clip(jax.random.uniform(keys[2], (3, FIBRES), jnp.float32, -0.5, 0.5) * block_scale(keys[2], (3, FIBRES), ((1, 16),), -0.4, 0.0), -0.5, 0.5),
        "seg_live": plant(jax.random.randint(keys[3], (FIBRES, BLOCKS), 1, 129), jax.random.fold_in(keys[3], 1), 1, 128).astype(jnp.int32),
        "pair_blocks": plant(jax.random.randint(keys[4], (SLABS, PEERS, PEERS, CAP, 2), 0, BLK_DEV), jax.random.fold_in(keys[4], 1), 0, BLK_DEV - 1).astype(jnp.int32),
        "pair_count": draw_pair_count(jax.random.fold_in(keys[6], 71), 0),
    }


spacing = 1.0 / 128.0
axial_stiff = 1.0
bend_stiff = 0.25
contact_stiff = 1.0 / 16.0
time_step = 0.2
damping = 0.9


def chain_force(padded):
    center = padded[:, :, 2:-2]
    next_one = padded[:, :, 3:-1]
    prev_one = padded[:, :, 1:-3]
    next_two = padded[:, :, 4:]
    prev_two = padded[:, :, :-4]
    axial = next_one - 2.0 * center + prev_one
    bending = next_two - 4.0 * next_one + 6.0 * center - 4.0 * prev_one + prev_two
    return axial_stiff * axial - bend_stiff * bending


def tile_forces(first, second, first_on, second_on):
    squared = jnp.zeros((first.shape[1], 128, 128), jnp.float32)
    for component in range(3):
        apart = first[component][:, :, None] - second[component][:, None, :]
        squared = squared + apart * apart
    weights = contact_stiff * jnp.exp(-squared) * first_on[:, :, None] * second_on[:, None, :]
    row_total = jnp.sum(weights, axis=2)
    col_total = jnp.sum(weights, axis=1)
    pulled_second = jnp.einsum("gij,cgj->cgi", weights, second, precision=lax.Precision.HIGHEST)
    pulled_first = jnp.einsum("gij,cgi->cgj", weights, first, precision=lax.Precision.HIGHEST)
    on_first = first * row_total[None] - pulled_second
    on_second = second * col_total[None] - pulled_first
    return on_first, on_second


def reference(displacement, velocity, anchors, seg_live, pair_blocks, pair_count):
    per_fibre = SEG_DEV // 128
    blocks_dev = FIB_DEV * per_fibre
    padded = jnp.pad(displacement, ((0, 0), (0, 0), (2, 2)))
    beam = chain_force(padded)
    seg_index = jnp.arange(SLABS * SEG_DEV, dtype=jnp.int32)
    height = seg_index.astype(jnp.float32) * spacing
    lift = jnp.stack([jnp.zeros_like(height), jnp.zeros_like(height), height])
    positions = displacement + anchors[:, :, None] + lift[:, None, :]
    grouped = positions.reshape(3, PEERS, FIB_DEV, SLABS, per_fibre, 128)
    grouped = grouped.transpose(3, 1, 0, 2, 4, 5).reshape(SLABS, PEERS, 3, blocks_dev, 128)
    counts_dev = seg_live.reshape(PEERS, FIB_DEV, SLABS, per_fibre)
    counts_dev = counts_dev.transpose(2, 0, 1, 3).reshape(SLABS, PEERS, blocks_dev)
    lanes = jnp.arange(128, dtype=jnp.int32)
    slots = jnp.arange(CAP, dtype=jnp.int32)

    def slab_forces(inputs):
        slab_pos, slab_counts, slab_pairs, slab_live = inputs

        def channel(forces, index):
            asker = index // PEERS
            holder = index % PEERS
            first_ids = slab_pairs[asker, holder, :, 0]
            second_ids = slab_pairs[asker, holder, :, 1]
            used = (slots < slab_live[asker, holder]).astype(jnp.float32)
            first = slab_pos[asker][:, first_ids, :]
            second = slab_pos[holder][:, second_ids, :]
            first_on = (lanes[None, :] < slab_counts[asker][first_ids][:, None]).astype(jnp.float32) * used[:, None]
            second_on = (lanes[None, :] < slab_counts[holder][second_ids][:, None]).astype(jnp.float32)
            on_first, on_second = tile_forces(first, second, first_on, second_on)
            asker_rows = jnp.zeros((CAP,), jnp.int32) + asker
            holder_rows = jnp.zeros((CAP,), jnp.int32) + holder
            forces = forces.at[asker_rows, :, first_ids, :].add(jnp.moveaxis(on_first, 1, 0))
            forces = forces.at[holder_rows, :, second_ids, :].add(jnp.moveaxis(on_second, 1, 0))
            return forces, None

        start_forces = jnp.zeros((PEERS, 3, blocks_dev, 128), jnp.float32)
        forces, unused = lax.scan(channel, start_forces, jnp.arange(PEERS * PEERS, dtype=jnp.int32))
        return forces

    contact = lax.map(slab_forces, (grouped, counts_dev, pair_blocks, pair_count))
    contact = contact.reshape(SLABS, PEERS, 3, FIB_DEV, per_fibre, 128)
    contact = contact.transpose(2, 1, 3, 0, 4, 5).reshape(3, PEERS * FIB_DEV, SLABS * SEG_DEV)
    new_velocity = damping * velocity + time_step * (beam + contact)
    new_displacement = displacement + time_step * new_velocity
    return new_velocity, new_displacement
```

```python
import jax
import jax.numpy as jnp
from jax import lax
from jax.experimental import pallas as pl
from jax.experimental.pallas import tpu as pltpu
from jax.sharding import PartitionSpec as P

spacing = 1.0 / 128.0
axial_stiff = 1.0
bend_stiff = 0.25
contact_stiff = 1.0 / 16.0
time_step = 0.2
damping = 0.9
masked_far = 1.0e4
HIGHEST = lax.Precision.HIGHEST


def padded_2(block, sides, width):
    for axis, dim in sides:
        count = lax.axis_size(axis)
        forward = [(i, i + 1) for i in range(count - 1)]
        backward = [(target, source) for source, target in forward]
        low = lax.ppermute(
            lax.slice_in_dim(block, block.shape[dim] - width, None, axis=dim), axis, forward
        )
        high = lax.ppermute(lax.slice_in_dim(block, 0, width, axis=dim), axis, backward)
        block = jnp.concatenate([low, block, high], axis=dim)
    return block


def chain_force(padded):
    center = padded[:, :, 2:-2]
    next_one = padded[:, :, 3:-1]
    prev_one = padded[:, :, 1:-3]
    next_two = padded[:, :, 4:]
    prev_two = padded[:, :, :-4]
    axial = next_one - 2.0 * center + prev_one
    bending = next_two - 4.0 * next_one + 6.0 * center - 4.0 * prev_one + prev_two
    return axial_stiff * axial - bend_stiff * bending


def pair_kernel(cnt_ref, mine_ref, m_ref, rd_ref, rq_ref, f1_ref, f2_ref):
    f1_ref[...] = jnp.zeros(f1_ref.shape, f1_ref.dtype)
    f2_ref[...] = jnp.zeros(f2_ref.shape, f2_ref.dtype)
    peers = cnt_ref.shape[0]
    cap = rd_ref.shape[0] // peers
    blocks = m_ref.shape[0]

    def peer(d, carry):
        live = jnp.clip(cnt_ref[d], 0, cap)

        def one(c, carry):
            slot = d * cap + c
            b = jnp.clip(mine_ref[slot], 0, blocks - 1)
            m = m_ref[b]
            rd = rd_ref[slot]
            rq = rq_ref[slot]
            dist = lax.dot_general(
                rd, m, (((0,), (0,)), ((), ())), precision=HIGHEST,
                preferred_element_type=jnp.float32,
            )
            w = jnp.exp(-dist) * contact_stiff
            f1 = lax.dot_general(
                rq, w, (((1,), (0,)), ((), ())), precision=HIGHEST,
                preferred_element_type=jnp.float32,
            )
            f2 = lax.dot_general(
                m, w, (((1,), (1,)), ((), ())), precision=HIGHEST,
                preferred_element_type=jnp.float32,
            )
            on_first = m * f1[3:4, :] - f1
            on_second = rq * f2[3:4, :] - f2
            f1_ref[b] = f1_ref[b] + on_first
            f2_ref[slot] = on_second[0:3, :]
            return carry

        return lax.fori_loop(0, live, one, carry)

    lax.fori_loop(0, peers, peer, 0)


def back_kernel(req_ref, f1_ref, ret_ref, out_ref):
    out_ref[...] = f1_ref[...]
    blocks = out_ref.shape[0]

    def one(s, carry):
        b = jnp.clip(req_ref[s], 0, blocks - 1)
        out_ref[b, 0:3, :] = out_ref[b, 0:3, :] + ret_ref[s]
        return carry

    lax.fori_loop(0, ret_ref.shape[0], one, 0)


def local(displacement, velocity, anchors, seg_live, pair_blocks, pair_count):
    seg_len = displacement.shape[2]
    fibre_count = displacement.shape[1]
    per_fibre = seg_len // 128
    block_total = fibre_count * per_fibre
    peer_total = pair_blocks.shape[2]
    slot_cap = pair_blocks.shape[3]
    slot_total = peer_total * slot_cap
    padded = padded_2(displacement, (("len", 2),), 2)
    beam = chain_force(padded)

    height = jnp.arange(seg_len, dtype=jnp.int32).astype(jnp.float32) * spacing
    lift = jnp.stack([jnp.zeros_like(height), jnp.zeros_like(height), height])
    positions = displacement + anchors[:, :, None] + lift[:, None, :]
    blocks = positions.reshape(3, block_total, 128).transpose(1, 0, 2)
    lanes = jnp.arange(128, dtype=jnp.int32)
    live = (lanes[None, :] < seg_live.reshape(block_total)[:, None]).astype(jnp.float32)
    norm = jnp.sum(blocks * blocks, axis=1)
    ones = jnp.ones_like(live)
    zero = jnp.zeros_like(live)
    mine_rows = jnp.stack(
        [blocks[:, 0], blocks[:, 1], blocks[:, 2], ones, norm, masked_far * (1.0 - live), ones, zero],
        axis=1,
    )
    lend_rows = jnp.stack([blocks[:, 0], blocks[:, 1], blocks[:, 2], live], axis=1)

    mine_ids = pair_blocks[0, 0, :, :, 0].reshape(slot_total)
    their_ids = pair_blocks[0, 0, :, :, 1]
    requested = lax.all_to_all(their_ids, ("xa", "xb"), split_axis=0, concat_axis=0, tiled=True)
    requested_flat = requested.reshape(slot_total)
    lent = lend_rows[requested_flat].reshape(peer_total, slot_cap, 4, 128)
    remote = lax.all_to_all(lent, ("xa", "xb"), split_axis=0, concat_axis=0, tiled=True)
    remote = remote.reshape(slot_total, 4, 128)
    q = remote[:, 0:3]
    rnorm = jnp.sum(q * q, axis=1)
    rlive = remote[:, 3]
    rones = jnp.ones_like(rlive)
    rzero = jnp.zeros_like(rlive)
    rd = jnp.stack(
        [-2.0 * q[:, 0], -2.0 * q[:, 1], -2.0 * q[:, 2], rnorm, rones, rones,
         masked_far * (1.0 - rlive), rzero],
        axis=1,
    )
    rq = jnp.stack([q[:, 0], q[:, 1], q[:, 2], rones, rzero, rzero, rzero, rzero], axis=1)

    smem = pl.BlockSpec(memory_space=pltpu.SMEM)
    vmem = pl.BlockSpec(memory_space=pltpu.VMEM)
    f1, f2 = pl.pallas_call(
        pair_kernel,
        out_shape=(
            jax.ShapeDtypeStruct((block_total, 8, 128), jnp.float32),
            jax.ShapeDtypeStruct((slot_total, 3, 128), jnp.float32),
        ),
        in_specs=[smem, smem, vmem, vmem, vmem],
        out_specs=(vmem, vmem),
    )(pair_count[0, 0], mine_ids, mine_rows, rd, rq)

    returned = lax.all_to_all(
        f2.reshape(peer_total, slot_cap, 3, 128), ("xa", "xb"), split_axis=0, concat_axis=0, tiled=True
    )
    acc = pl.pallas_call(
        back_kernel,
        out_shape=jax.ShapeDtypeStruct((block_total, 8, 128), jnp.float32),
        in_specs=[smem, vmem, vmem],
        out_specs=vmem,
    )(requested_flat, f1, returned.reshape(slot_total, 3, 128))
    contact = acc[:, 0:3, :].transpose(1, 0, 2).reshape(3, fibre_count, seg_len)
    new_velocity = damping * velocity + time_step * (beam + contact)
    new_displacement = displacement + time_step * new_velocity
    return (new_velocity, new_displacement)


def solution(mesh):
    in_specs = (
        P(None, ("xa", "xb"), "len"),
        P(None, ("xa", "xb"), "len"),
        P(None, ("xa", "xb")),
        P(("xa", "xb"), "len"),
        P("len", ("xa", "xb"), None, None, None),
        P("len", ("xa", "xb"), None),
    )
    out_specs = (P(None, ("xa", "xb"), "len"), P(None, ("xa", "xb"), "len"))
    return jax.shard_map(local, mesh=mesh, in_specs=in_specs, out_specs=out_specs, check_vma=False)
```

```python
import jax
import jax.numpy as jnp
from jax import lax
from jax.experimental import pallas as pl
from jax.experimental.pallas import tpu as pltpu
from jax.sharding import PartitionSpec as P

spacing = 1.0 / 128.0
axial_stiff = 1.0
bend_stiff = 0.25
contact_stiff = 1.0 / 16.0
time_step = 0.2
damping = 0.9
masked_far = 1.0e4
HIGHEST = lax.Precision.HIGHEST
HIGH = lax.Precision.HIGH
tile_group = 8


def padded_2(block, sides, width):
    for axis, dim in sides:
        count = lax.axis_size(axis)
        forward = [(i, i + 1) for i in range(count - 1)]
        backward = [(target, source) for source, target in forward]
        low = lax.ppermute(
            lax.slice_in_dim(block, block.shape[dim] - width, None, axis=dim), axis, forward
        )
        high = lax.ppermute(lax.slice_in_dim(block, 0, width, axis=dim), axis, backward)
        block = jnp.concatenate([low, block, high], axis=dim)
    return block


def chain_force(padded):
    center = padded[:, :, 2:-2]
    next_one = padded[:, :, 3:-1]
    prev_one = padded[:, :, 1:-3]
    next_two = padded[:, :, 4:]
    prev_two = padded[:, :, :-4]
    axial = next_one - 2.0 * center + prev_one
    bending = next_two - 4.0 * next_one + 6.0 * center - 4.0 * prev_one + prev_two
    return axial_stiff * axial - bend_stiff * bending


def tile_pair(m, rd, rq):
    dist = lax.dot_general(
        rd, m, (((0,), (0,)), ((), ())), precision=HIGHEST, preferred_element_type=jnp.float32
    )
    w = jnp.exp(-dist)
    f1 = lax.dot_general(
        rq, w, (((1,), (0,)), ((), ())), precision=HIGH, preferred_element_type=jnp.float32
    )
    f2 = lax.dot_general(
        m, w, (((1,), (1,)), ((), ())), precision=HIGH, preferred_element_type=jnp.float32
    )
    f1 = f1 * contact_stiff
    f2 = f2 * contact_stiff
    return m * f1[3:4, :] - f1, (rq * f2[3:4, :] - f2)[0:3, :]


def pair_kernel(cnt_ref, mine_ref, m_ref, rd_ref, rq_ref, f1_ref, f2_ref):
    f1_ref[...] = jnp.zeros(f1_ref.shape, f1_ref.dtype)
    f2_ref[...] = jnp.zeros(f2_ref.shape, f2_ref.dtype)
    peers = cnt_ref.shape[0]
    cap = rd_ref.shape[0] // peers
    blocks = m_ref.shape[0]

    def peer(d, carry):
        live = jnp.clip(cnt_ref[d], 0, cap)

        def group(g, carry):
            done = []
            for k in range(tile_group):
                c = g * tile_group + k
                slot = d * cap + c
                b = jnp.clip(mine_ref[slot], 0, blocks - 1)
                on_first, on_second = tile_pair(m_ref[b], rd_ref[slot], rq_ref[slot])
                ok = c < live
                done.append((b, slot, jnp.where(ok, on_first, 0.0), jnp.where(ok, on_second, 0.0)))
            for b, slot, on_first, on_second in done:
                f1_ref[b] = f1_ref[b] + on_first
                f2_ref[slot] = on_second
            return carry

        return lax.fori_loop(0, (live + tile_group - 1) // tile_group, group, carry)

    lax.fori_loop(0, peers, peer, 0)


def back_kernel(req_ref, f1_ref, ret_ref, out_ref):
    out_ref[...] = f1_ref[...]
    blocks = out_ref.shape[0]

    def one(s, carry):
        b = jnp.clip(req_ref[s], 0, blocks - 1)
        out_ref[b, 0:3, :] = out_ref[b, 0:3, :] + ret_ref[s]
        return carry

    lax.fori_loop(0, ret_ref.shape[0], one, 0)


def local(displacement, velocity, anchors, seg_live, pair_blocks, pair_count):
    seg_len = displacement.shape[2]
    fibre_count = displacement.shape[1]
    per_fibre = seg_len // 128
    block_total = fibre_count * per_fibre
    peer_total = pair_blocks.shape[2]
    slot_cap = pair_blocks.shape[3]
    slot_total = peer_total * slot_cap
    padded = padded_2(displacement, (("len", 2),), 2)
    beam = chain_force(padded)

    height = jnp.arange(seg_len, dtype=jnp.int32).astype(jnp.float32) * spacing
    lift = jnp.stack([jnp.zeros_like(height), jnp.zeros_like(height), height])
    positions = displacement + anchors[:, :, None] + lift[:, None, :]
    blocks = positions.reshape(3, block_total, 128).transpose(1, 0, 2)
    lanes = jnp.arange(128, dtype=jnp.int32)
    live = (lanes[None, :] < seg_live.reshape(block_total)[:, None]).astype(jnp.float32)
    norm = jnp.sum(blocks * blocks, axis=1)
    ones = jnp.ones_like(live)
    zero = jnp.zeros_like(live)
    mine_rows = jnp.stack(
        [blocks[:, 0], blocks[:, 1], blocks[:, 2], ones, norm, masked_far * (1.0 - live), ones, zero],
        axis=1,
    )
    lend_rows = jnp.stack([blocks[:, 0], blocks[:, 1], blocks[:, 2], live], axis=1)

    mine_ids = pair_blocks[0, 0, :, :, 0].reshape(slot_total)
    their_ids = pair_blocks[0, 0, :, :, 1]
    requested = lax.all_to_all(their_ids, ("xa", "xb"), split_axis=0, concat_axis=0, tiled=True)
    requested_flat = requested.reshape(slot_total)
    lent = lend_rows[requested_flat].reshape(peer_total, slot_cap, 4, 128)
    remote = lax.all_to_all(lent, ("xa", "xb"), split_axis=0, concat_axis=0, tiled=True)
    remote = remote.reshape(slot_total, 4, 128)
    q = remote[:, 0:3]
    rnorm = jnp.sum(q * q, axis=1)
    rlive = remote[:, 3]
    rones = jnp.ones_like(rlive)
    rzero = jnp.zeros_like(rlive)
    rd = jnp.stack(
        [-2.0 * q[:, 0], -2.0 * q[:, 1], -2.0 * q[:, 2], rnorm, rones, rones,
         masked_far * (1.0 - rlive), rzero],
        axis=1,
    )
    rq = jnp.stack([q[:, 0], q[:, 1], q[:, 2], rones, rzero, rzero, rzero, rzero], axis=1)

    smem = pl.BlockSpec(memory_space=pltpu.SMEM)
    vmem = pl.BlockSpec(memory_space=pltpu.VMEM)
    f1, f2 = pl.pallas_call(
        pair_kernel,
        out_shape=(
            jax.ShapeDtypeStruct((block_total, 8, 128), jnp.float32),
            jax.ShapeDtypeStruct((slot_total, 3, 128), jnp.float32),
        ),
        in_specs=[smem, smem, vmem, vmem, vmem],
        out_specs=(vmem, vmem),
    )(pair_count[0, 0], mine_ids, mine_rows, rd, rq)

    returned = lax.all_to_all(
        f2.reshape(peer_total, slot_cap, 3, 128), ("xa", "xb"), split_axis=0, concat_axis=0, tiled=True
    )
    acc = pl.pallas_call(
        back_kernel,
        out_shape=jax.ShapeDtypeStruct((block_total, 8, 128), jnp.float32),
        in_specs=[smem, vmem, vmem],
        out_specs=vmem,
    )(requested_flat, f1, returned.reshape(slot_total, 3, 128))
    contact = acc[:, 0:3, :].transpose(1, 0, 2).reshape(3, fibre_count, seg_len)
    new_velocity = damping * velocity + time_step * (beam + contact)
    new_displacement = displacement + time_step * new_velocity
    return (new_velocity, new_displacement)


def solution(mesh):
    in_specs = (
        P(None, ("xa", "xb"), "len"),
        P(None, ("xa", "xb"), "len"),
        P(None, ("xa", "xb")),
        P(("xa", "xb"), "len"),
        P("len", ("xa", "xb"), None, None, None),
        P("len", ("xa", "xb"), None),
    )
    out_specs = (P(None, ("xa", "xb"), "len"), P(None, ("xa", "xb"), "len"))
    return jax.shard_map(local, mesh=mesh, in_specs=in_specs, out_specs=out_specs, check_vma=False)
```

```python
import jax
import jax.numpy as jnp
from jax import lax
from jax.experimental import pallas as pl
from jax.experimental.pallas import tpu as pltpu
from jax.sharding import PartitionSpec as P

spacing = 1.0 / 128.0
axial_stiff = 1.0
bend_stiff = 0.25
contact_stiff = 1.0 / 16.0
time_step = 0.2
damping = 0.9
masked_far = 1.0e4
HIGHEST = lax.Precision.HIGHEST
HIGH = lax.Precision.HIGH
tile_group = 8
balance_rounds = 3


def padded_2(block, sides, width):
    for axis, dim in sides:
        count = lax.axis_size(axis)
        forward = [(i, i + 1) for i in range(count - 1)]
        backward = [(target, source) for source, target in forward]
        low = lax.ppermute(
            lax.slice_in_dim(block, block.shape[dim] - width, None, axis=dim), axis, forward
        )
        high = lax.ppermute(lax.slice_in_dim(block, 0, width, axis=dim), axis, backward)
        block = jnp.concatenate([low, block, high], axis=dim)
    return block


def chain_force(padded):
    center = padded[:, :, 2:-2]
    next_one = padded[:, :, 3:-1]
    prev_one = padded[:, :, 1:-3]
    next_two = padded[:, :, 4:]
    prev_two = padded[:, :, :-4]
    axial = next_one - 2.0 * center + prev_one
    bending = next_two - 4.0 * next_one + 6.0 * center - 4.0 * prev_one + prev_two
    return axial_stiff * axial - bend_stiff * bending


def tile_pair(m, rd, rq):
    dist = lax.dot_general(
        rd, m, (((0,), (0,)), ((), ())), precision=HIGHEST, preferred_element_type=jnp.float32
    )
    w = jnp.exp(-dist)
    f1 = lax.dot_general(
        rq, w, (((1,), (0,)), ((), ())), precision=HIGH, preferred_element_type=jnp.float32
    )
    f2 = lax.dot_general(
        m, w, (((1,), (1,)), ((), ())), precision=HIGH, preferred_element_type=jnp.float32
    )
    f1 = f1 * contact_stiff
    f2 = f2 * contact_stiff
    return m * f1[3:4, :] - f1, (rq * f2[3:4, :] - f2)[0:3, :]


def pair_kernel(
    ka_ref, hl_ref, hh_ref, mine_ref, req_ref, m_ref, rd_ref, rq_ref, f1_ref, f2_ref, lb_ref, ls_ref
):
    f1_ref[...] = jnp.zeros(f1_ref.shape, f1_ref.dtype)
    f2_ref[...] = jnp.zeros(f2_ref.shape, f2_ref.dtype)
    peers = ka_ref.shape[0]
    cap = mine_ref.shape[0] // peers
    blocks = m_ref.shape[0]

    def listed(d, n):
        def asked(c, n):
            lb_ref[n] = jnp.clip(mine_ref[d * cap + c], 0, blocks - 1)
            ls_ref[n] = d * 2 * cap + c
            return n + 1

        def held(c, n):
            lb_ref[n] = jnp.clip(req_ref[d * cap + c], 0, blocks - 1)
            ls_ref[n] = d * 2 * cap + cap + c
            return n + 1

        n = lax.fori_loop(0, jnp.clip(ka_ref[d], 0, cap), asked, n)
        low = jnp.clip(hl_ref[d], 0, cap)
        return lax.fori_loop(low, jnp.clip(hh_ref[d], low, cap), held, n)

    total = lax.fori_loop(0, peers, listed, 0)
    last = jnp.maximum(total - 1, 0)

    def group(g, carry):
        done = []
        for k in range(tile_group):
            t = g * tile_group + k
            at = jnp.minimum(t, last)
            b = lb_ref[at]
            slot = ls_ref[at]
            on_first, on_second = tile_pair(m_ref[b], rd_ref[slot], rq_ref[slot])
            done.append((b, slot, jnp.where(t < total, on_first, 0.0), on_second))
        for b, slot, on_first, on_second in done:
            f1_ref[b] = f1_ref[b] + on_first
            f2_ref[slot] = on_second
        return carry

    lax.fori_loop(0, (total + tile_group - 1) // tile_group, group, 0)


def split_pairs(counts, cap):
    peers = counts.shape[0]
    whole = jnp.clip(counts, 0, cap)
    share = whole.astype(jnp.float32)
    eye = jnp.eye(peers, dtype=jnp.float32)
    off = share * (1.0 - eye)
    own = jnp.sum(share * eye, axis=1)
    off_row = jnp.sum(off, axis=1)
    level = jnp.sum(share) / peers
    keep = jnp.ones((peers,), jnp.float32)
    for _ in range(balance_rounds):
        incoming = jnp.sum((1.0 - keep)[:, None] * off, axis=0)
        target = jnp.maximum(level - incoming, 0.0)
        keep = jnp.clip((target - own) / jnp.maximum(off_row, 1.0), 0.0, 1.0)
    split = jnp.floor(keep[:, None] * share + 0.5).astype(jnp.int32)
    split = jnp.clip(split, 0, whole)
    diag = jnp.eye(peers, dtype=jnp.bool_)
    return jnp.where(diag, whole, split), whole


def back_kernel(req_ref, f1_ref, ret_ref, out_ref):
    out_ref[...] = f1_ref[...]
    blocks = out_ref.shape[0]

    def one(s, carry):
        b = jnp.clip(req_ref[s], 0, blocks - 1)
        out_ref[b, 0:3, :] = out_ref[b, 0:3, :] + ret_ref[s]
        return carry

    lax.fori_loop(0, ret_ref.shape[0], one, 0)


def local(displacement, velocity, anchors, seg_live, pair_blocks, pair_count):
    seg_len = displacement.shape[2]
    fibre_count = displacement.shape[1]
    per_fibre = seg_len // 128
    block_total = fibre_count * per_fibre
    peer_total = pair_blocks.shape[2]
    slot_cap = pair_blocks.shape[3]
    slot_total = peer_total * slot_cap
    padded = padded_2(displacement, (("len", 2),), 2)
    beam = chain_force(padded)

    height = jnp.arange(seg_len, dtype=jnp.int32).astype(jnp.float32) * spacing
    lift = jnp.stack([jnp.zeros_like(height), jnp.zeros_like(height), height])
    positions = displacement + anchors[:, :, None] + lift[:, None, :]
    blocks = positions.reshape(3, block_total, 128).transpose(1, 0, 2)
    lanes = jnp.arange(128, dtype=jnp.int32)
    live = (lanes[None, :] < seg_live.reshape(block_total)[:, None]).astype(jnp.float32)
    norm = jnp.sum(blocks * blocks, axis=1)
    ones = jnp.ones_like(live)
    zero = jnp.zeros_like(live)
    mine_rows = jnp.stack(
        [blocks[:, 0], blocks[:, 1], blocks[:, 2], ones, norm, masked_far * (1.0 - live), ones, zero],
        axis=1,
    )
    lend_rows = jnp.stack([blocks[:, 0], blocks[:, 1], blocks[:, 2], live], axis=1)

    mine_ids = pair_blocks[0, 0, :, :, 0]
    their_ids = pair_blocks[0, 0, :, :, 1]
    requested = lax.all_to_all(their_ids, ("xa", "xb"), split_axis=0, concat_axis=0, tiled=True)
    lend_ids = jnp.concatenate([requested, mine_ids], axis=1).reshape(2 * slot_total)
    lent = lend_rows[lend_ids].reshape(peer_total, 2 * slot_cap, 4, 128)
    remote = lax.all_to_all(lent, ("xa", "xb"), split_axis=0, concat_axis=0, tiled=True)
    remote = remote.reshape(2 * slot_total, 4, 128)
    q = remote[:, 0:3]
    rnorm = jnp.sum(q * q, axis=1)
    rlive = remote[:, 3]
    rones = jnp.ones_like(rlive)
    rzero = jnp.zeros_like(rlive)
    rd = jnp.stack(
        [-2.0 * q[:, 0], -2.0 * q[:, 1], -2.0 * q[:, 2], rnorm, rones, rones,
         masked_far * (1.0 - rlive), rzero],
        axis=1,
    )
    rq = jnp.stack([q[:, 0], q[:, 1], q[:, 2], rones, rzero, rzero, rzero, rzero], axis=1)

    counts = lax.all_gather(pair_count[0, 0], ("xa", "xb"), axis=0, tiled=False)
    split, whole = split_pairs(counts, slot_cap)
    me = lax.axis_index(("xa", "xb"))
    ask_keep = split[me]
    hold_low = split[:, me]
    hold_high = whole[:, me]

    smem = pl.BlockSpec(memory_space=pltpu.SMEM)
    vmem = pl.BlockSpec(memory_space=pltpu.VMEM)
    f1, f2 = pl.pallas_call(
        pair_kernel,
        out_shape=(
            jax.ShapeDtypeStruct((block_total, 8, 128), jnp.float32),
            jax.ShapeDtypeStruct((2 * slot_total, 3, 128), jnp.float32),
        ),
        in_specs=[smem, smem, smem, smem, smem, vmem, vmem, vmem],
        out_specs=(vmem, vmem),
        scratch_shapes=[pltpu.SMEM((2 * slot_total,), jnp.int32), pltpu.SMEM((2 * slot_total,), jnp.int32)],
    )(ask_keep, hold_low, hold_high, mine_ids.reshape(slot_total), requested.reshape(slot_total),
      mine_rows, rd, rq)

    returned = lax.all_to_all(
        f2.reshape(peer_total, 2 * slot_cap, 3, 128), ("xa", "xb"), split_axis=0, concat_axis=0,
        tiled=True,
    )
    acc = pl.pallas_call(
        back_kernel,
        out_shape=jax.ShapeDtypeStruct((block_total, 8, 128), jnp.float32),
        in_specs=[smem, vmem, vmem],
        out_specs=vmem,
    )(lend_ids, f1, returned.reshape(2 * slot_total, 3, 128))
    contact = acc[:, 0:3, :].transpose(1, 0, 2).reshape(3, fibre_count, seg_len)
    new_velocity = damping * velocity + time_step * (beam + contact)
    new_displacement = displacement + time_step * new_velocity
    return (new_velocity, new_displacement)


def solution(mesh):
    in_specs = (
        P(None, ("xa", "xb"), "len"),
        P(None, ("xa", "xb"), "len"),
        P(None, ("xa", "xb")),
        P(("xa", "xb"), "len"),
        P("len", ("xa", "xb"), None, None, None),
        P("len", ("xa", "xb"), None),
    )
    out_specs = (P(None, ("xa", "xb"), "len"), P(None, ("xa", "xb"), "len"))
    return jax.shard_map(local, mesh=mesh, in_specs=in_specs, out_specs=out_specs, check_vma=False)
```

```python
import jax
import jax.numpy as jnp
from jax import lax
from jax.experimental import pallas as pl
from jax.experimental.pallas import tpu as pltpu
from jax.sharding import PartitionSpec as P

spacing = 1.0 / 128.0
axial_stiff = 1.0
bend_stiff = 0.25
contact_stiff = 1.0 / 16.0
time_step = 0.2
damping = 0.9
masked_far = 1.0e4
HIGHEST = lax.Precision.HIGHEST
HIGH = lax.Precision.HIGH
tile_group = 8
balance_rounds = 3


def halos(block, axis, dim, width):
    count = lax.axis_size(axis)
    forward = [(i, i + 1) for i in range(count - 1)]
    backward = [(target, source) for source, target in forward]
    low = lax.ppermute(
        lax.slice_in_dim(block, block.shape[dim] - width, None, axis=dim), axis, forward
    )
    high = lax.ppermute(lax.slice_in_dim(block, 0, width, axis=dim), axis, backward)
    return low, high


def chain_force(padded):
    center = padded[:, :, 2:-2]
    next_one = padded[:, :, 3:-1]
    prev_one = padded[:, :, 1:-3]
    next_two = padded[:, :, 4:]
    prev_two = padded[:, :, :-4]
    axial = next_one - 2.0 * center + prev_one
    bending = next_two - 4.0 * next_one + 6.0 * center - 4.0 * prev_one + prev_two
    return axial_stiff * axial - bend_stiff * bending


def rows_of(x, near):
    row = lax.broadcasted_iota(jnp.int32, (8, 128), 0)
    v0, v1, v2, on = x[0:1], x[1:2], x[2:3], x[3:4]
    norm = v0 * v0 + v1 * v1 + v2 * v2
    far = masked_far * (1.0 - on)
    pick = lambda r, v: jnp.where(row == r, jnp.broadcast_to(v, (8, 128)), 0.0)
    if near:
        return (pick(0, v0) + pick(1, v1) + pick(2, v2) + jnp.where((row == 3) | (row == 6), 1.0, 0.0)
                + pick(4, norm) + pick(5, far))
    rd = (pick(0, -2.0 * v0) + pick(1, -2.0 * v1) + pick(2, -2.0 * v2) + pick(3, norm)
          + jnp.where((row == 4) | (row == 5), 1.0, 0.0) + pick(6, far))
    rq = pick(0, v0) + pick(1, v1) + pick(2, v2) + jnp.where(row == 3, 1.0, 0.0)
    return rd, rq


def tile_pair(m, rd, rq):
    dist = lax.dot_general(
        rd, m, (((0,), (0,)), ((), ())), precision=HIGHEST, preferred_element_type=jnp.float32
    )
    w = jnp.exp(-dist)
    f1 = lax.dot_general(
        rq, w, (((1,), (0,)), ((), ())), precision=HIGH, preferred_element_type=jnp.float32
    )
    f2 = lax.dot_general(
        m, w, (((1,), (1,)), ((), ())), precision=HIGH, preferred_element_type=jnp.float32
    )
    f1 = f1 * contact_stiff
    f2 = f2 * contact_stiff
    return m * f1[3:4, :] - f1, (rq * f2[3:4, :] - f2)[0:3, :]


def pair_kernel(
    ka_ref, hl_ref, hh_ref, mine_ref, req_ref, m_ref, rem_ref, low_ref, high_ref, f1_ref, f2_ref, lb_ref,
    ls_ref,
):
    f1_ref[...] = jnp.zeros(f1_ref.shape, f1_ref.dtype)
    f2_ref[...] = jnp.zeros(f2_ref.shape, f2_ref.dtype)
    peers = ka_ref.shape[0]
    cap = mine_ref.shape[0] // peers
    blocks = m_ref.shape[0]

    def listed(d, n):
        def asked(c, n):
            lb_ref[n] = jnp.clip(mine_ref[d * cap + c], 0, blocks - 1)
            ls_ref[n] = d * 2 * cap + c
            return n + 1

        def held(c, n):
            lb_ref[n] = jnp.clip(req_ref[d * cap + c], 0, blocks - 1)
            ls_ref[n] = d * 2 * cap + cap + c
            return n + 1

        n = lax.fori_loop(0, jnp.clip(ka_ref[d], 0, cap), asked, n)
        low = jnp.clip(hl_ref[d], 0, cap)
        return lax.fori_loop(low, jnp.clip(hh_ref[d], low, cap), held, n)

    total = lax.fori_loop(0, peers, listed, 0)
    last = jnp.maximum(total - 1, 0)

    def group(g, carry):
        done = []
        for k in range(tile_group):
            t = g * tile_group + k
            at = jnp.minimum(t, last)
            b = lb_ref[at]
            slot = ls_ref[at]
            rd, rq = rows_of(rem_ref[slot], False)
            on_first, on_second = tile_pair(rows_of(m_ref[b], True), rd, rq)
            done.append((b, slot, jnp.where(t < total, on_first, 0.0), on_second))
        for b, slot, on_first, on_second in done:
            f1_ref[b] = f1_ref[b] + on_first
            f2_ref[slot] = on_second
        return carry

    lax.fori_loop(0, (total + tile_group - 1) // tile_group, group, 0)


def split_pairs(counts, cap):
    peers = counts.shape[0]
    whole = jnp.clip(counts, 0, cap)
    share = whole.astype(jnp.float32)
    eye = jnp.eye(peers, dtype=jnp.float32)
    off = share * (1.0 - eye)
    own = jnp.sum(share * eye, axis=1)
    off_row = jnp.sum(off, axis=1)
    level = jnp.sum(share) / peers
    keep = jnp.ones((peers,), jnp.float32)
    for _ in range(balance_rounds):
        incoming = jnp.sum((1.0 - keep)[:, None] * off, axis=0)
        target = jnp.maximum(level - incoming, 0.0)
        keep = jnp.clip((target - own) / jnp.maximum(off_row, 1.0), 0.0, 1.0)
    split = jnp.floor(keep[:, None] * share + 0.5).astype(jnp.int32)
    split = jnp.clip(split, 0, whole)
    diag = jnp.eye(peers, dtype=jnp.bool_)
    return jnp.where(diag, whole, split), whole


def back_kernel(req_ref, f1_ref, ret_ref, out_ref):
    out_ref[...] = f1_ref[...]
    blocks = out_ref.shape[0]

    def one(s, carry):
        b = jnp.clip(req_ref[s], 0, blocks - 1)
        out_ref[b, 0:3, :] = out_ref[b, 0:3, :] + ret_ref[s]
        return carry

    lax.fori_loop(0, ret_ref.shape[0], one, 0, unroll=8)


def local(displacement, velocity, anchors, seg_live, pair_blocks, pair_count):
    seg_len = displacement.shape[2]
    fibre_count = displacement.shape[1]
    per_fibre = seg_len // 128
    block_total = fibre_count * per_fibre
    peer_total = pair_blocks.shape[2]
    slot_cap = pair_blocks.shape[3]
    slot_total = peer_total * slot_cap
    halo_low, halo_high = halos(displacement, "len", 2, 2)
    beam = chain_force(jnp.concatenate([halo_low, displacement, halo_high], axis=2))

    height = jnp.arange(seg_len, dtype=jnp.int32).astype(jnp.float32) * spacing
    lift = jnp.stack([jnp.zeros_like(height), jnp.zeros_like(height), height])
    positions = displacement + anchors[:, :, None] + lift[:, None, :]
    blocks = positions.reshape(3, block_total, 128).transpose(1, 0, 2)
    lanes = jnp.arange(128, dtype=jnp.int32)
    live = (lanes[None, :] < seg_live.reshape(block_total)[:, None]).astype(jnp.float32)
    lend_rows = jnp.stack([blocks[:, 0], blocks[:, 1], blocks[:, 2], live], axis=1)

    mine_ids = pair_blocks[0, 0, :, :, 0]
    their_ids = pair_blocks[0, 0, :, :, 1]
    own_counts = jnp.broadcast_to(pair_count[0, 0][None, :], (peer_total, peer_total))
    asked = lax.all_to_all(
        jnp.concatenate([their_ids, own_counts], axis=1), ("xa", "xb"), split_axis=0, concat_axis=0,
        tiled=True,
    )
    requested = asked[:, :slot_cap]
    counts = asked[:, slot_cap:]
    lend_ids = jnp.concatenate([requested, mine_ids], axis=1).reshape(2 * slot_total)
    lent = lend_rows[lend_ids].reshape(peer_total, 2 * slot_cap, 4, 128)
    remote = lax.all_to_all(lent, ("xa", "xb"), split_axis=0, concat_axis=0, tiled=True)
    remote = remote.reshape(2 * slot_total, 4, 128)
    split, whole = split_pairs(counts, slot_cap)
    me = lax.axis_index(("xa", "xb"))
    ask_keep = split[me]
    hold_low = split[:, me]
    hold_high = whole[:, me]

    smem = pl.BlockSpec(memory_space=pltpu.SMEM)
    vmem = pl.BlockSpec(memory_space=pltpu.VMEM)
    f1, f2 = pl.pallas_call(
        pair_kernel,
        out_shape=(
            jax.ShapeDtypeStruct((block_total, 8, 128), jnp.float32),
            jax.ShapeDtypeStruct((2 * slot_total, 3, 128), jnp.float32),
        ),
        in_specs=[smem, smem, smem, smem, smem, vmem, vmem, vmem, vmem],
        out_specs=(vmem, vmem),
        scratch_shapes=[pltpu.SMEM((2 * slot_total,), jnp.int32), pltpu.SMEM((2 * slot_total,), jnp.int32)],
    )(ask_keep, hold_low, hold_high, mine_ids.reshape(slot_total), requested.reshape(slot_total),
      lend_rows, remote, halo_low, halo_high)

    returned = lax.all_to_all(
        f2.reshape(peer_total, 2 * slot_cap, 3, 128), ("xa", "xb"), split_axis=0, concat_axis=0,
        tiled=True,
    )
    acc = pl.pallas_call(
        back_kernel,
        out_shape=jax.ShapeDtypeStruct((block_total, 8, 128), jnp.float32),
        in_specs=[smem, vmem, vmem],
        out_specs=vmem,
    )(lend_ids, f1, returned.reshape(2 * slot_total, 3, 128))
    contact = acc[:, 0:3, :].transpose(1, 0, 2).reshape(3, fibre_count, seg_len)
    new_velocity = damping * velocity + time_step * (beam + contact)
    new_displacement = displacement + time_step * new_velocity
    return (new_velocity, new_displacement)


def solution(mesh):
    in_specs = (
        P(None, ("xa", "xb"), "len"),
        P(None, ("xa", "xb"), "len"),
        P(None, ("xa", "xb")),
        P(("xa", "xb"), "len"),
        P("len", ("xa", "xb"), None, None, None),
        P("len", ("xa", "xb"), None),
    )
    out_specs = (P(None, ("xa", "xb"), "len"), P(None, ("xa", "xb"), "len"))
    return jax.shard_map(local, mesh=mesh, in_specs=in_specs, out_specs=out_specs, check_vma=False)
```

```python
import jax
import jax.numpy as jnp
from jax import lax
from jax.experimental import pallas as pl
from jax.experimental.pallas import tpu as pltpu
from jax.sharding import PartitionSpec as P

spacing = 1.0 / 128.0
axial_stiff = 1.0
bend_stiff = 0.25
contact_stiff = 1.0 / 16.0
time_step = 0.2
damping = 0.9
masked_far = 1.0e4
HIGHEST = lax.Precision.HIGHEST
HIGH = lax.Precision.HIGH
tile_group = 8


def halos(block, axis, dim, width):
    count = lax.axis_size(axis)
    forward = [(i, i + 1) for i in range(count - 1)]
    backward = [(target, source) for source, target in forward]
    low = lax.ppermute(
        lax.slice_in_dim(block, block.shape[dim] - width, None, axis=dim), axis, forward
    )
    high = lax.ppermute(lax.slice_in_dim(block, 0, width, axis=dim), axis, backward)
    return low, high


def chain_force(padded):
    center = padded[:, :, 2:-2]
    next_one = padded[:, :, 3:-1]
    prev_one = padded[:, :, 1:-3]
    next_two = padded[:, :, 4:]
    prev_two = padded[:, :, :-4]
    axial = next_one - 2.0 * center + prev_one
    bending = next_two - 4.0 * next_one + 6.0 * center - 4.0 * prev_one + prev_two
    return axial_stiff * axial - bend_stiff * bending


def rows_of(x, near):
    row = lax.broadcasted_iota(jnp.int32, (8, 128), 0)
    lane = lax.broadcasted_iota(jnp.int32, (1, 128), 1).astype(jnp.float32)
    v0, v1, v2 = x[0:1], x[1:2], x[2:3]
    on = jnp.where(lane < x[3:4, 0:1], 1.0, 0.0)
    norm = v0 * v0 + v1 * v1 + v2 * v2
    far = masked_far * (1.0 - on)
    pick = lambda r, v: jnp.where(row == r, jnp.broadcast_to(v, (8, 128)), 0.0)
    if near:
        return (pick(0, v0) + pick(1, v1) + pick(2, v2) + jnp.where((row == 3) | (row == 6), 1.0, 0.0)
                + pick(4, norm) + pick(5, far))
    rd = (pick(0, -2.0 * v0) + pick(1, -2.0 * v1) + pick(2, -2.0 * v2) + pick(3, norm)
          + jnp.where((row == 4) | (row == 5), 1.0, 0.0) + pick(6, far))
    rq = pick(0, v0) + pick(1, v1) + pick(2, v2) + jnp.where(row == 3, 1.0, 0.0)
    return rd, rq


def tile_pair(m, rd, rq):
    dist = lax.dot_general(
        rd, m, (((0,), (0,)), ((), ())), precision=HIGHEST, preferred_element_type=jnp.float32
    )
    w = jnp.exp(-dist)
    f1 = lax.dot_general(
        rq, w, (((1,), (0,)), ((), ())), precision=HIGH, preferred_element_type=jnp.float32
    )
    f2 = lax.dot_general(
        m, w, (((1,), (1,)), ((), ())), precision=HIGH, preferred_element_type=jnp.float32
    )
    f1 = f1 * contact_stiff
    f2 = f2 * contact_stiff
    return m * f1[3:4, :] - f1, (rq * f2[3:4, :] - f2)[0:3, :]


def pair_kernel(cnt_ref, req_ref, m_ref, rem_ref, low_ref, high_ref, f1_ref, f2_ref, lb_ref, ls_ref):
    f1_ref[...] = jnp.zeros(f1_ref.shape, f1_ref.dtype)
    f2_ref[...] = jnp.zeros(f2_ref.shape, f2_ref.dtype)
    peers = cnt_ref.shape[0]
    cap = req_ref.shape[0] // peers
    blocks = m_ref.shape[0]

    def listed(d, n):
        def held(c, n):
            lb_ref[n] = jnp.clip(req_ref[d * cap + c], 0, blocks - 1)
            ls_ref[n] = d * cap + c
            return n + 1

        return lax.fori_loop(0, jnp.clip(cnt_ref[d], 0, cap), held, n)

    total = lax.fori_loop(0, peers, listed, 0)
    last = jnp.maximum(total - 1, 0)

    def group(g, carry):
        done = []
        for k in range(tile_group):
            t = g * tile_group + k
            at = jnp.minimum(t, last)
            b = lb_ref[at]
            slot = ls_ref[at]
            rd, rq = rows_of(rem_ref[slot], False)
            on_first, on_second = tile_pair(rows_of(m_ref[b], True), rd, rq)
            done.append((b, slot, jnp.where(t < total, on_first, 0.0), on_second))
        for b, slot, on_first, on_second in done:
            f1_ref[b] = f1_ref[b] + on_first
            f2_ref[slot] = on_second
        return carry

    lax.fori_loop(0, (total + tile_group - 1) // tile_group, group, 0)


def back_kernel(req_ref, f1_ref, ret_ref, out_ref):
    out_ref[...] = f1_ref[...]
    blocks = out_ref.shape[0]

    def one(s, carry):
        b = jnp.clip(req_ref[s], 0, blocks - 1)
        out_ref[b, 0:3, :] = out_ref[b, 0:3, :] + ret_ref[s]
        return carry

    lax.fori_loop(0, ret_ref.shape[0], one, 0, unroll=8)


def local(displacement, velocity, anchors, seg_live, pair_blocks, pair_count):
    seg_len = displacement.shape[2]
    fibre_count = displacement.shape[1]
    per_fibre = seg_len // 128
    block_total = fibre_count * per_fibre
    peer_total = pair_blocks.shape[2]
    slot_cap = pair_blocks.shape[3]
    slot_total = peer_total * slot_cap
    halo_low, halo_high = halos(displacement, "len", 2, 2)
    beam = chain_force(jnp.concatenate([halo_low, displacement, halo_high], axis=2))

    height = jnp.arange(seg_len, dtype=jnp.int32).astype(jnp.float32) * spacing
    lift = jnp.stack([jnp.zeros_like(height), jnp.zeros_like(height), height])
    positions = displacement + anchors[:, :, None] + lift[:, None, :]
    blocks = positions.reshape(3, block_total, 128).transpose(1, 0, 2)
    lanes = jnp.arange(128, dtype=jnp.int32)
    seg_count = seg_live.reshape(block_total).astype(jnp.float32)
    meta = jnp.where(lanes[None, :] == 0, seg_count[:, None], 0.0)
    my_rows = jnp.concatenate([blocks, meta[:, None, :]], axis=1)

    mine_ids = pair_blocks[0, 0, :, :, 0]
    their_ids = pair_blocks[0, 0, :, :, 1].astype(jnp.float32)
    live_to = jnp.broadcast_to(pair_count[0, 0].astype(jnp.float32)[:, None], their_ids.shape)
    mine_flat = mine_ids.reshape(slot_total)
    sent_meta = jnp.where(
        lanes == 0, seg_count[mine_flat][:, None],
        jnp.where(lanes == 1, their_ids.reshape(slot_total)[:, None],
                  jnp.where(lanes == 2, live_to.reshape(slot_total)[:, None], 0.0)),
    )
    lent = jnp.concatenate([blocks[mine_flat], sent_meta[:, None, :]], axis=1)
    remote = lax.all_to_all(
        lent.reshape(peer_total, slot_cap, 4, 128), ("xa", "xb"), split_axis=0, concat_axis=0, tiled=True
    )
    req_ids = remote[:, :, 3, 1].astype(jnp.int32).reshape(slot_total)
    live_from = remote[:, 0, 3, 2].astype(jnp.int32)

    smem = pl.BlockSpec(memory_space=pltpu.SMEM)
    vmem = pl.BlockSpec(memory_space=pltpu.VMEM)
    f1, f2 = pl.pallas_call(
        pair_kernel,
        out_shape=(
            jax.ShapeDtypeStruct((block_total, 8, 128), jnp.float32),
            jax.ShapeDtypeStruct((slot_total, 3, 128), jnp.float32),
        ),
        in_specs=[smem, smem, vmem, vmem, vmem, vmem],
        out_specs=(vmem, vmem),
        scratch_shapes=[pltpu.SMEM((slot_total,), jnp.int32), pltpu.SMEM((slot_total,), jnp.int32)],
    )(live_from, req_ids, my_rows, remote.reshape(slot_total, 4, 128), halo_low, halo_high)

    returned = lax.all_to_all(
        f2.reshape(peer_total, slot_cap, 3, 128), ("xa", "xb"), split_axis=0, concat_axis=0, tiled=True
    )
    acc = pl.pallas_call(
        back_kernel,
        out_shape=jax.ShapeDtypeStruct((block_total, 8, 128), jnp.float32),
        in_specs=[smem, vmem, vmem],
        out_specs=vmem,
    )(mine_flat, f1, returned.reshape(slot_total, 3, 128))
    contact = acc[:, 0:3, :].transpose(1, 0, 2).reshape(3, fibre_count, seg_len)
    new_velocity = damping * velocity + time_step * (beam + contact)
    new_displacement = displacement + time_step * new_velocity
    return (new_velocity, new_displacement)


def solution(mesh):
    in_specs = (
        P(None, ("xa", "xb"), "len"),
        P(None, ("xa", "xb"), "len"),
        P(None, ("xa", "xb")),
        P(("xa", "xb"), "len"),
        P("len", ("xa", "xb"), None, None, None),
        P("len", ("xa", "xb"), None),
    )
    out_specs = (P(None, ("xa", "xb"), "len"), P(None, ("xa", "xb"), "len"))
    return jax.shard_map(local, mesh=mesh, in_specs=in_specs, out_specs=out_specs, check_vma=False)
```

```python
import jax
import jax.numpy as jnp
from jax import lax
from jax.experimental import pallas as pl
from jax.experimental.pallas import tpu as pltpu
from jax.sharding import PartitionSpec as P

spacing = 1.0 / 128.0
axial_stiff = 1.0
bend_stiff = 0.25
contact_stiff = 1.0 / 16.0
time_step = 0.2
damping = 0.9
masked_far = 1.0e4
HIGH = lax.Precision.HIGH
tile_group = 8


def halos(block, axis, dim, width):
    count = lax.axis_size(axis)
    forward = [(i, i + 1) for i in range(count - 1)]
    backward = [(target, source) for source, target in forward]
    low = lax.ppermute(
        lax.slice_in_dim(block, block.shape[dim] - width, None, axis=dim), axis, forward
    )
    high = lax.ppermute(lax.slice_in_dim(block, 0, width, axis=dim), axis, backward)
    return low, high


def chain_force(padded):
    center = padded[:, :, 2:-2]
    next_one = padded[:, :, 3:-1]
    prev_one = padded[:, :, 1:-3]
    next_two = padded[:, :, 4:]
    prev_two = padded[:, :, :-4]
    axial = next_one - 2.0 * center + prev_one
    bending = next_two - 4.0 * next_one + 6.0 * center - 4.0 * prev_one + prev_two
    return axial_stiff * axial - bend_stiff * bending


def rows_of(x, near):
    row = lax.broadcasted_iota(jnp.int32, (8, 128), 0)
    lane = lax.broadcasted_iota(jnp.int32, (1, 128), 1).astype(jnp.float32)
    v0, v1, v2 = x[0:1], x[1:2], x[2:3]
    on = jnp.where(lane < x[3:4, 0:1], 1.0, 0.0)
    norm = v0 * v0 + v1 * v1 + v2 * v2
    far = masked_far * (1.0 - on)
    pick = lambda r, v: jnp.where(row == r, jnp.broadcast_to(v, (8, 128)), 0.0)
    if near:
        return (pick(0, v0) + pick(1, v1) + pick(2, v2) + jnp.where((row == 3) | (row == 6), 1.0, 0.0)
                + pick(4, norm) + pick(5, far))
    rd = (pick(0, -2.0 * v0) + pick(1, -2.0 * v1) + pick(2, -2.0 * v2) + pick(3, norm)
          + jnp.where((row == 4) | (row == 5), 1.0, 0.0) + pick(6, far))
    rq = pick(0, v0) + pick(1, v1) + pick(2, v2) + jnp.where(row == 3, 1.0, 0.0)
    return rd, rq


def tile_two(m_a, m_b, rd_a, rd_b, rq_a, rq_b):
    zero = jnp.zeros((8, 128), jnp.float32)
    mine = jnp.concatenate(
        [jnp.concatenate([m_a, zero], axis=1), jnp.concatenate([zero, m_b], axis=1)], axis=0
    )
    dist = lax.dot_general(
        jnp.concatenate([rd_a, rd_b], axis=0), mine, (((0,), (0,)), ((), ())), precision=HIGH,
        preferred_element_type=jnp.float32,
    )
    w = jnp.exp(-dist)
    f1 = lax.dot_general(
        jnp.concatenate([rq_a, rq_b], axis=0), w, (((1,), (0,)), ((), ())), precision=HIGH,
        preferred_element_type=jnp.float32,
    )
    f2 = lax.dot_general(
        mine, w, (((1,), (1,)), ((), ())), precision=HIGH, preferred_element_type=jnp.float32
    )
    f1 = f1 * contact_stiff
    f2 = f2 * contact_stiff
    out = []
    for m, rq, g1, g2 in ((m_a, rq_a, f1[0:8, 0:128], f2[0:8]), (m_b, rq_b, f1[8:16, 128:256], f2[8:16])):
        out.append((m * g1[3:4, :] - g1, (rq * g2[3:4, :] - g2)[0:3, :]))
    return out


def pair_kernel(cnt_ref, req_ref, m_ref, rem_ref, low_ref, high_ref, f1_ref, f2_ref, lb_ref, ls_ref):
    f1_ref[...] = jnp.zeros(f1_ref.shape, f1_ref.dtype)
    f2_ref[...] = jnp.zeros(f2_ref.shape, f2_ref.dtype)
    peers = cnt_ref.shape[0]
    cap = req_ref.shape[0] // peers
    blocks = m_ref.shape[0]

    def listed(d, n):
        def held(c, n):
            lb_ref[n] = jnp.clip(req_ref[d * cap + c], 0, blocks - 1)
            ls_ref[n] = d * cap + c
            return n + 1

        return lax.fori_loop(0, jnp.clip(cnt_ref[d], 0, cap), held, n)

    total = lax.fori_loop(0, peers, listed, 0)
    last = jnp.maximum(total - 1, 0)

    def group(g, carry):
        done = []
        for k in range(0, tile_group, 2):
            picked = []
            for t in (g * tile_group + k, g * tile_group + k + 1):
                at = jnp.minimum(t, last)
                picked.append((t, lb_ref[at], ls_ref[at]))
            (t_a, b_a, s_a), (t_b, b_b, s_b) = picked
            rd_a, rq_a = rows_of(rem_ref[s_a], False)
            rd_b, rq_b = rows_of(rem_ref[s_b], False)
            pair = tile_two(rows_of(m_ref[b_a], True), rows_of(m_ref[b_b], True), rd_a, rd_b, rq_a, rq_b)
            for (t, b, slot), (on_first, on_second) in zip(picked, pair):
                done.append((b, slot, jnp.where(t < total, on_first, 0.0), on_second))
        for b, slot, on_first, on_second in done:
            f1_ref[b] = f1_ref[b] + on_first
            f2_ref[slot] = on_second
        return carry

    lax.fori_loop(0, (total + tile_group - 1) // tile_group, group, 0)


def back_kernel(req_ref, f1_ref, ret_ref, out_ref):
    out_ref[...] = f1_ref[...]
    blocks = out_ref.shape[0]

    def one(s, carry):
        b = jnp.clip(req_ref[s], 0, blocks - 1)
        out_ref[b, 0:3, :] = out_ref[b, 0:3, :] + ret_ref[s]
        return carry

    lax.fori_loop(0, ret_ref.shape[0], one, 0, unroll=8)


def local(displacement, velocity, anchors, seg_live, pair_blocks, pair_count):
    seg_len = displacement.shape[2]
    fibre_count = displacement.shape[1]
    per_fibre = seg_len // 128
    block_total = fibre_count * per_fibre
    peer_total = pair_blocks.shape[2]
    slot_cap = pair_blocks.shape[3]
    slot_total = peer_total * slot_cap
    halo_low, halo_high = halos(displacement, "len", 2, 2)
    beam = chain_force(jnp.concatenate([halo_low, displacement, halo_high], axis=2))

    height = jnp.arange(seg_len, dtype=jnp.int32).astype(jnp.float32) * spacing
    lift = jnp.stack([jnp.zeros_like(height), jnp.zeros_like(height), height])
    positions = displacement + anchors[:, :, None] + lift[:, None, :]
    blocks = positions.reshape(3, block_total, 128).transpose(1, 0, 2)
    lanes = jnp.arange(128, dtype=jnp.int32)
    seg_count = seg_live.reshape(block_total).astype(jnp.float32)
    meta = jnp.where(lanes[None, :] == 0, seg_count[:, None], 0.0)
    my_rows = jnp.concatenate([blocks, meta[:, None, :]], axis=1)

    mine_ids = pair_blocks[0, 0, :, :, 0]
    their_ids = pair_blocks[0, 0, :, :, 1].astype(jnp.float32)
    live_to = jnp.broadcast_to(pair_count[0, 0].astype(jnp.float32)[:, None], their_ids.shape)
    mine_flat = mine_ids.reshape(slot_total)
    sent_meta = jnp.where(
        lanes == 0, seg_count[mine_flat][:, None],
        jnp.where(lanes == 1, their_ids.reshape(slot_total)[:, None],
                  jnp.where(lanes == 2, live_to.reshape(slot_total)[:, None], 0.0)),
    )
    lent = jnp.concatenate([blocks[mine_flat], sent_meta[:, None, :]], axis=1)
    remote = lax.all_to_all(
        lent.reshape(peer_total, slot_cap, 4, 128), ("xa", "xb"), split_axis=0, concat_axis=0, tiled=True
    )
    req_ids = remote[:, :, 3, 1].astype(jnp.int32).reshape(slot_total)
    live_from = remote[:, 0, 3, 2].astype(jnp.int32)

    smem = pl.BlockSpec(memory_space=pltpu.SMEM)
    vmem = pl.BlockSpec(memory_space=pltpu.VMEM)
    f1, f2 = pl.pallas_call(
        pair_kernel,
        out_shape=(
            jax.ShapeDtypeStruct((block_total, 8, 128), jnp.float32),
            jax.ShapeDtypeStruct((slot_total, 3, 128), jnp.float32),
        ),
        in_specs=[smem, smem, vmem, vmem, vmem, vmem],
        out_specs=(vmem, vmem),
        scratch_shapes=[pltpu.SMEM((slot_total,), jnp.int32), pltpu.SMEM((slot_total,), jnp.int32)],
    )(live_from, req_ids, my_rows, remote.reshape(slot_total, 4, 128), halo_low, halo_high)

    returned = lax.all_to_all(
        f2.reshape(peer_total, slot_cap, 3, 128), ("xa", "xb"), split_axis=0, concat_axis=0, tiled=True
    )
    acc = pl.pallas_call(
        back_kernel,
        out_shape=jax.ShapeDtypeStruct((block_total, 8, 128), jnp.float32),
        in_specs=[smem, vmem, vmem],
        out_specs=vmem,
    )(mine_flat, f1, returned.reshape(slot_total, 3, 128))
    contact = acc[:, 0:3, :].transpose(1, 0, 2).reshape(3, fibre_count, seg_len)
    new_velocity = damping * velocity + time_step * (beam + contact)
    new_displacement = displacement + time_step * new_velocity
    return (new_velocity, new_displacement)


def solution(mesh):
    in_specs = (
        P(None, ("xa", "xb"), "len"),
        P(None, ("xa", "xb"), "len"),
        P(None, ("xa", "xb")),
        P(("xa", "xb"), "len"),
        P("len", ("xa", "xb"), None, None, None),
        P("len", ("xa", "xb"), None),
    )
    out_specs = (P(None, ("xa", "xb"), "len"), P(None, ("xa", "xb"), "len"))
    return jax.shard_map(local, mesh=mesh, in_specs=in_specs, out_specs=out_specs, check_vma=False)
```

```python
import functools

import jax
import jax.numpy as jnp
from jax import lax
from jax.experimental import pallas as pl
from jax.experimental.pallas import tpu as pltpu
from jax.sharding import PartitionSpec as P

spacing = 1.0 / 128.0
axial_stiff = 1.0
bend_stiff = 0.25
contact_stiff = 1.0 / 16.0
time_step = 0.2
damping = 0.9
masked_far = 1.0e4
HIGH = lax.Precision.HIGH
tile_group = 8


def halos(block, axis, dim, width):
    count = lax.axis_size(axis)
    forward = [(i, i + 1) for i in range(count - 1)]
    backward = [(target, source) for source, target in forward]
    low = lax.ppermute(
        lax.slice_in_dim(block, block.shape[dim] - width, None, axis=dim), axis, forward
    )
    high = lax.ppermute(lax.slice_in_dim(block, 0, width, axis=dim), axis, backward)
    return low, high


def chain_force(padded):
    center = padded[:, :, 2:-2]
    next_one = padded[:, :, 3:-1]
    prev_one = padded[:, :, 1:-3]
    next_two = padded[:, :, 4:]
    prev_two = padded[:, :, :-4]
    axial = next_one - 2.0 * center + prev_one
    bending = next_two - 4.0 * next_one + 6.0 * center - 4.0 * prev_one + prev_two
    return axial_stiff * axial - bend_stiff * bending


def rows_of(x, near):
    row = lax.broadcasted_iota(jnp.int32, (8, 128), 0)
    lane = lax.broadcasted_iota(jnp.int32, (1, 128), 1).astype(jnp.float32)
    v0, v1, v2 = x[0:1], x[1:2], x[2:3]
    on = jnp.where(lane < x[3:4, 0:1], 1.0, 0.0)
    norm = v0 * v0 + v1 * v1 + v2 * v2
    far = masked_far * (1.0 - on)
    pick = lambda r, v: jnp.where(row == r, jnp.broadcast_to(v, (8, 128)), 0.0)
    if near:
        return (pick(0, v0) + pick(1, v1) + pick(2, v2) + jnp.where((row == 3) | (row == 6), 1.0, 0.0)
                + pick(4, norm) + pick(5, far))
    rd = (pick(0, -2.0 * v0) + pick(1, -2.0 * v1) + pick(2, -2.0 * v2) + pick(3, norm)
          + jnp.where((row == 4) | (row == 5), 1.0, 0.0) + pick(6, far))
    rq = pick(0, v0) + pick(1, v1) + pick(2, v2) + jnp.where(row == 3, 1.0, 0.0)
    return rd, rq


def tile_two(m_a, m_b, rd_a, rd_b, rq_a, rq_b):
    zero = jnp.zeros((8, 128), jnp.float32)
    mine = jnp.concatenate(
        [jnp.concatenate([m_a, zero], axis=1), jnp.concatenate([zero, m_b], axis=1)], axis=0
    )
    dist = lax.dot_general(
        jnp.concatenate([rd_a, rd_b], axis=0), mine, (((0,), (0,)), ((), ())), precision=HIGH,
        preferred_element_type=jnp.float32,
    )
    w = jnp.exp(-dist)
    f1 = lax.dot_general(
        jnp.concatenate([rq_a, rq_b], axis=0), w, (((1,), (0,)), ((), ())), precision=HIGH,
        preferred_element_type=jnp.float32,
    )
    f2 = lax.dot_general(
        mine, w, (((1,), (1,)), ((), ())), precision=HIGH, preferred_element_type=jnp.float32
    )
    f1 = f1 * contact_stiff
    f2 = f2 * contact_stiff
    out = []
    for m, rq, g1, g2 in ((m_a, rq_a, f1[0:8, 0:128], f2[0:8]), (m_b, rq_b, f1[8:16, 128:256], f2[8:16])):
        out.append((m * g1[3:4, :] - g1, (rq * g2[3:4, :] - g2)[0:3, :]))
    return out


def peer_row(slot, rows, cap):
    return (slot // cap) * rows * cap + slot % cap


def pack_kernel(mine_ref, their_ref, cnt_ref, rows_ref, lent_ref):
    peers = cnt_ref.shape[0]
    cap = mine_ref.shape[0] // peers
    blocks = rows_ref.shape[0]
    row = lax.broadcasted_iota(jnp.int32, (4, 128), 0)
    lane = lax.broadcasted_iota(jnp.int32, (4, 128), 1)

    def one(s, carry):
        x = rows_ref[jnp.clip(mine_ref[s], 0, blocks - 1)]
        theirs = their_ref[s].astype(jnp.float32)
        live = cnt_ref[s // cap].astype(jnp.float32)
        x = jnp.where((row == 3) & (lane == 1), theirs, x)
        x = jnp.where((row == 3) & (lane == 2), live, x)
        lent_ref[pl.ds(peer_row(s, 4, cap), 4, stride=cap), :] = x
        return carry

    lax.fori_loop(0, mine_ref.shape[0], one, 0, unroll=8)


def pair_kernel(cnt_ref, req_ref, m_ref, rem_ref, low_ref, high_ref, f1_ref, f2_ref, lb_ref, ls_ref):
    f1_ref[...] = jnp.zeros(f1_ref.shape, f1_ref.dtype)
    f2_ref[...] = jnp.zeros(f2_ref.shape, f2_ref.dtype)
    peers = cnt_ref.shape[0]
    cap = req_ref.shape[0] // peers
    blocks = m_ref.shape[0]

    def listed(d, n):
        def held(c, n):
            lb_ref[n] = jnp.clip(req_ref[d * cap + c], 0, blocks - 1)
            ls_ref[n] = d * cap + c
            return n + 1

        return lax.fori_loop(0, jnp.clip(cnt_ref[d], 0, cap), held, n)

    total = lax.fori_loop(0, peers, listed, 0)
    last = jnp.maximum(total - 1, 0)

    def group(g, carry):
        done = []
        for k in range(0, tile_group, 2):
            picked = []
            for t in (g * tile_group + k, g * tile_group + k + 1):
                at = jnp.minimum(t, last)
                picked.append((t, lb_ref[at], ls_ref[at]))
            (t_a, b_a, s_a), (t_b, b_b, s_b) = picked
            rd_a, rq_a = rows_of(rem_ref[pl.ds(peer_row(s_a, 4, cap), 4, stride=cap), :], False)
            rd_b, rq_b = rows_of(rem_ref[pl.ds(peer_row(s_b, 4, cap), 4, stride=cap), :], False)
            pair = tile_two(rows_of(m_ref[b_a], True), rows_of(m_ref[b_b], True), rd_a, rd_b, rq_a, rq_b)
            for (t, b, slot), (on_first, on_second) in zip(picked, pair):
                done.append((b, slot, jnp.where(t < total, on_first, 0.0), on_second))
        for b, slot, on_first, on_second in done:
            f1_ref[b] = f1_ref[b] + on_first
            f2_ref[pl.ds(peer_row(slot, 3, cap), 3, stride=cap), :] = on_second
        return carry

    lax.fori_loop(0, (total + tile_group - 1) // tile_group, group, 0)


def back_kernel(cap, mine_ref, f1_ref, ret_ref, vel_ref, disp_ref, beam_ref, nv_ref, nd_ref, acc_ref):
    acc_ref[...] = f1_ref[...]
    blocks = vel_ref.shape[1]

    def one(s, carry):
        b = jnp.clip(mine_ref[s], 0, blocks - 1)
        start = pl.multiple_of(b * 8, 8)
        acc_ref[pl.ds(start, 3), :] = acc_ref[pl.ds(start, 3), :] + ret_ref[pl.ds(peer_row(s, 3, cap), 3, stride=cap), :]
        return carry

    lax.fori_loop(0, mine_ref.shape[0], one, 0, unroll=8)
    for c in range(3):
        contact = acc_ref[pl.ds(c, blocks, stride=8), :]
        new_velocity = damping * vel_ref[c] + time_step * (beam_ref[c] + contact)
        nv_ref[c] = new_velocity
        nd_ref[c] = disp_ref[c] + time_step * new_velocity


def local(displacement, velocity, anchors, seg_live, pair_blocks, pair_count):
    seg_len = displacement.shape[2]
    fibre_count = displacement.shape[1]
    per_fibre = seg_len // 128
    block_total = fibre_count * per_fibre
    peer_total = pair_blocks.shape[2]
    slot_cap = pair_blocks.shape[3]
    slot_total = peer_total * slot_cap
    halo_low, halo_high = halos(displacement, "len", 2, 2)
    beam = chain_force(jnp.concatenate([halo_low, displacement, halo_high], axis=2))

    height = jnp.arange(seg_len, dtype=jnp.int32).astype(jnp.float32) * spacing
    lift = jnp.stack([jnp.zeros_like(height), jnp.zeros_like(height), height])
    positions = displacement + anchors[:, :, None] + lift[:, None, :]
    blocks = positions.reshape(3, block_total, 128).transpose(1, 0, 2)
    lanes = jnp.arange(128, dtype=jnp.int32)
    seg_count = seg_live.reshape(block_total).astype(jnp.float32)
    meta = jnp.where(lanes[None, :] == 0, seg_count[:, None], 0.0)
    my_rows = jnp.concatenate([blocks, meta[:, None, :]], axis=1)

    mine_flat = pair_blocks[0, 0, :, :, 0].reshape(slot_total)
    their_flat = pair_blocks[0, 0, :, :, 1].reshape(slot_total)
    smem = pl.BlockSpec(memory_space=pltpu.SMEM)
    vmem = pl.BlockSpec(memory_space=pltpu.VMEM)
    lent = pl.pallas_call(
        pack_kernel,
        out_shape=jax.ShapeDtypeStruct((peer_total * 4 * slot_cap, 128), jnp.float32),
        in_specs=[smem, smem, smem, vmem],
        out_specs=vmem,
    )(mine_flat, their_flat, pair_count[0, 0], my_rows)
    remote = lax.all_to_all(
        lent.reshape(peer_total, 4, slot_cap, 128), ("xa", "xb"), split_axis=0, concat_axis=0, tiled=True
    )
    req_ids = remote[:, 3, :, 1].astype(jnp.int32).reshape(slot_total)
    live_from = remote[:, 3, 0, 2].astype(jnp.int32)

    f1, f2 = pl.pallas_call(
        pair_kernel,
        out_shape=(
            jax.ShapeDtypeStruct((block_total, 8, 128), jnp.float32),
            jax.ShapeDtypeStruct((peer_total * 3 * slot_cap, 128), jnp.float32),
        ),
        in_specs=[smem, smem, vmem, vmem, vmem, vmem],
        out_specs=(vmem, vmem),
        scratch_shapes=[pltpu.SMEM((slot_total,), jnp.int32), pltpu.SMEM((slot_total,), jnp.int32)],
    )(live_from, req_ids, my_rows, remote.reshape(peer_total * 4 * slot_cap, 128), halo_low, halo_high)

    returned = lax.all_to_all(
        f2.reshape(peer_total, 3, slot_cap, 128), ("xa", "xb"), split_axis=0, concat_axis=0, tiled=True
    )
    new_velocity, new_displacement = pl.pallas_call(
        functools.partial(back_kernel, slot_cap),
        out_shape=(
            jax.ShapeDtypeStruct(velocity.shape, jnp.float32),
            jax.ShapeDtypeStruct(displacement.shape, jnp.float32),
        ),
        in_specs=[smem, vmem, vmem, vmem, vmem, vmem],
        out_specs=(vmem, vmem),
        scratch_shapes=[pltpu.VMEM((block_total * 8, 128), jnp.float32)],
    )(mine_flat, f1.reshape(block_total * 8, 128), returned.reshape(peer_total * 3 * slot_cap, 128),
      velocity, displacement, beam)
    return (new_velocity, new_displacement)


def solution(mesh):
    in_specs = (
        P(None, ("xa", "xb"), "len"),
        P(None, ("xa", "xb"), "len"),
        P(None, ("xa", "xb")),
        P(("xa", "xb"), "len"),
        P("len", ("xa", "xb"), None, None, None),
        P("len", ("xa", "xb"), None),
    )
    out_specs = (P(None, ("xa", "xb"), "len"), P(None, ("xa", "xb"), "len"))
    return jax.shard_map(local, mesh=mesh, in_specs=in_specs, out_specs=out_specs, check_vma=False)
```

```python
import functools

import jax
import jax.numpy as jnp
from jax import lax
from jax.experimental import pallas as pl
from jax.experimental.pallas import tpu as pltpu
from jax.sharding import PartitionSpec as P

spacing = 1.0 / 128.0
axial_stiff = 1.0
bend_stiff = 0.25
contact_stiff = 1.0 / 16.0
time_step = 0.2
damping = 0.9
masked_far = 1.0e4
HIGH = lax.Precision.HIGH
tile_group = 8


def halos(block, axis, dim, width):
    count = lax.axis_size(axis)
    forward = [(i, i + 1) for i in range(count - 1)]
    backward = [(target, source) for source, target in forward]
    low = lax.ppermute(
        lax.slice_in_dim(block, block.shape[dim] - width, None, axis=dim), axis, forward
    )
    high = lax.ppermute(lax.slice_in_dim(block, 0, width, axis=dim), axis, backward)
    return low, high


def chain_force(padded):
    center = padded[:, :, 2:-2]
    next_one = padded[:, :, 3:-1]
    prev_one = padded[:, :, 1:-3]
    next_two = padded[:, :, 4:]
    prev_two = padded[:, :, :-4]
    axial = next_one - 2.0 * center + prev_one
    bending = next_two - 4.0 * next_one + 6.0 * center - 4.0 * prev_one + prev_two
    return axial_stiff * axial - bend_stiff * bending


def rows_of(x, near):
    row = lax.broadcasted_iota(jnp.int32, (8, 128), 0)
    lane = lax.broadcasted_iota(jnp.int32, (1, 128), 1).astype(jnp.float32)
    v0, v1, v2 = x[0:1], x[1:2], x[2:3]
    on = jnp.where(lane < x[3:4, 0:1], 1.0, 0.0)
    norm = v0 * v0 + v1 * v1 + v2 * v2
    far = masked_far * (1.0 - on)
    pick = lambda r, v: jnp.where(row == r, jnp.broadcast_to(v, (8, 128)), 0.0)
    if near:
        return (pick(0, v0) + pick(1, v1) + pick(2, v2) + jnp.where((row == 3) | (row == 6), 1.0, 0.0)
                + pick(4, norm) + pick(5, far))
    rd = (pick(0, -2.0 * v0) + pick(1, -2.0 * v1) + pick(2, -2.0 * v2) + pick(3, norm)
          + jnp.where((row == 4) | (row == 5), 1.0, 0.0) + pick(6, far))
    rq = pick(0, v0) + pick(1, v1) + pick(2, v2) + jnp.where(row == 3, 1.0, 0.0)
    return rd, rq


def tile_two(m_a, m_b, rd_a, rd_b, rq_a, rq_b):
    zero = jnp.zeros((8, 128), jnp.float32)
    mine = jnp.concatenate(
        [jnp.concatenate([m_a, zero], axis=1), jnp.concatenate([zero, m_b], axis=1)], axis=0
    )
    dist = lax.dot_general(
        jnp.concatenate([rd_a, rd_b], axis=0), mine, (((0,), (0,)), ((), ())), precision=HIGH,
        preferred_element_type=jnp.float32,
    )
    w = jnp.exp(-dist)
    f1 = lax.dot_general(
        jnp.concatenate([rq_a, rq_b], axis=0), w, (((1,), (0,)), ((), ())), precision=HIGH,
        preferred_element_type=jnp.float32,
    )
    f2 = lax.dot_general(
        mine, w, (((1,), (1,)), ((), ())), precision=HIGH, preferred_element_type=jnp.float32
    )
    f1 = f1 * contact_stiff
    f2 = f2 * contact_stiff
    out = []
    for m, rq, g1, g2 in ((m_a, rq_a, f1[0:8, 0:128], f2[0:8]), (m_b, rq_b, f1[8:16, 128:256], f2[8:16])):
        out.append((m * g1[3:4, :] - g1, (rq * g2[3:4, :] - g2)[0:3, :]))
    return out


def peer_row(slot, rows, cap):
    return (slot // cap) * rows * cap + slot % cap


def pack_kernel(mine_ref, their_ref, cnt_ref, rows_ref, lent_ref):
    peers = cnt_ref.shape[0]
    cap = mine_ref.shape[0] // peers
    blocks = rows_ref.shape[0]
    row = lax.broadcasted_iota(jnp.int32, (4, 128), 0)
    lane = lax.broadcasted_iota(jnp.int32, (4, 128), 1)

    lent_ref[...] = jnp.zeros(lent_ref.shape, lent_ref.dtype)

    def peer(d, carry):
        live = cnt_ref[d]

        def one(c, carry):
            s = d * cap + c
            x = rows_ref[jnp.clip(mine_ref[s], 0, blocks - 1)]
            x = jnp.where((row == 3) & (lane == 1), their_ref[s].astype(jnp.float32), x)
            x = jnp.where((row == 3) & (lane == 2), live.astype(jnp.float32), x)
            lent_ref[pl.ds(d * 4 * cap + c, 4, stride=cap), :] = x
            return carry

        return lax.fori_loop(0, jnp.clip(live, 1, cap), one, carry)

    lax.fori_loop(0, peers, peer, 0)


def pair_kernel(cnt_ref, req_ref, m_ref, rem_ref, low_ref, high_ref, f1_ref, f2_ref, lb_ref, ls_ref):
    f1_ref[...] = jnp.zeros(f1_ref.shape, f1_ref.dtype)
    f2_ref[...] = jnp.zeros(f2_ref.shape, f2_ref.dtype)
    peers = cnt_ref.shape[0]
    cap = req_ref.shape[0] // peers
    blocks = m_ref.shape[0]

    def listed(d, n):
        def held(c, n):
            lb_ref[n] = jnp.clip(req_ref[d * cap + c], 0, blocks - 1)
            ls_ref[n] = d * cap + c
            return n + 1

        return lax.fori_loop(0, jnp.clip(cnt_ref[d], 0, cap), held, n)

    total = lax.fori_loop(0, peers, listed, 0)
    last = jnp.maximum(total - 1, 0)

    def group(g, carry):
        done = []
        for k in range(0, tile_group, 2):
            picked = []
            for t in (g * tile_group + k, g * tile_group + k + 1):
                at = jnp.minimum(t, last)
                picked.append((t, lb_ref[at], ls_ref[at]))
            (t_a, b_a, s_a), (t_b, b_b, s_b) = picked
            rd_a, rq_a = rows_of(rem_ref[pl.ds(peer_row(s_a, 4, cap), 4, stride=cap), :], False)
            rd_b, rq_b = rows_of(rem_ref[pl.ds(peer_row(s_b, 4, cap), 4, stride=cap), :], False)
            pair = tile_two(rows_of(m_ref[b_a], True), rows_of(m_ref[b_b], True), rd_a, rd_b, rq_a, rq_b)
            for (t, b, slot), (on_first, on_second) in zip(picked, pair):
                done.append((b, slot, jnp.where(t < total, on_first, 0.0), on_second))
        for b, slot, on_first, on_second in done:
            f1_ref[b] = f1_ref[b] + on_first
            f2_ref[pl.ds(peer_row(slot, 3, cap), 3, stride=cap), :] = on_second
        return carry

    lax.fori_loop(0, (total + tile_group - 1) // tile_group, group, 0)


def back_kernel(cap, mine_ref, cnt_ref, f1_ref, ret_ref, vel_ref, disp_ref, beam_ref, nv_ref, nd_ref, acc_ref):
    acc_ref[...] = f1_ref[...]
    blocks = vel_ref.shape[1]

    def peer(d, carry):
        def one(c, carry):
            s = d * cap + c
            b = jnp.clip(mine_ref[s], 0, blocks - 1)
            start = pl.multiple_of(b * 8, 8)
            acc_ref[pl.ds(start, 3), :] = (
                acc_ref[pl.ds(start, 3), :] + ret_ref[pl.ds(d * 3 * cap + c, 3, stride=cap), :]
            )
            return carry

        return lax.fori_loop(0, jnp.clip(cnt_ref[d], 0, cap), one, carry)

    lax.fori_loop(0, cnt_ref.shape[0], peer, 0)
    for c in range(3):
        contact = acc_ref[pl.ds(c, blocks, stride=8), :]
        new_velocity = damping * vel_ref[c] + time_step * (beam_ref[c] + contact)
        nv_ref[c] = new_velocity
        nd_ref[c] = disp_ref[c] + time_step * new_velocity


def local(displacement, velocity, anchors, seg_live, pair_blocks, pair_count):
    seg_len = displacement.shape[2]
    fibre_count = displacement.shape[1]
    per_fibre = seg_len // 128
    block_total = fibre_count * per_fibre
    peer_total = pair_blocks.shape[2]
    slot_cap = pair_blocks.shape[3]
    slot_total = peer_total * slot_cap
    halo_low, halo_high = halos(displacement, "len", 2, 2)
    beam = chain_force(jnp.concatenate([halo_low, displacement, halo_high], axis=2))

    height = jnp.arange(seg_len, dtype=jnp.int32).astype(jnp.float32) * spacing
    lift = jnp.stack([jnp.zeros_like(height), jnp.zeros_like(height), height])
    positions = displacement + anchors[:, :, None] + lift[:, None, :]
    blocks = positions.reshape(3, block_total, 128).transpose(1, 0, 2)
    lanes = jnp.arange(128, dtype=jnp.int32)
    seg_count = seg_live.reshape(block_total).astype(jnp.float32)
    meta = jnp.where(lanes[None, :] == 0, seg_count[:, None], 0.0)
    my_rows = jnp.concatenate([blocks, meta[:, None, :]], axis=1)

    mine_flat = pair_blocks[0, 0, :, :, 0].reshape(slot_total)
    their_flat = pair_blocks[0, 0, :, :, 1].reshape(slot_total)
    smem = pl.BlockSpec(memory_space=pltpu.SMEM)
    vmem = pl.BlockSpec(memory_space=pltpu.VMEM)
    lent = pl.pallas_call(
        pack_kernel,
        out_shape=jax.ShapeDtypeStruct((peer_total * 4 * slot_cap, 128), jnp.float32),
        in_specs=[smem, smem, smem, vmem],
        out_specs=vmem,
    )(mine_flat, their_flat, pair_count[0, 0], my_rows)
    remote = lax.all_to_all(
        lent.reshape(peer_total, 4, slot_cap, 128), ("xa", "xb"), split_axis=0, concat_axis=0, tiled=True
    )
    req_ids = remote[:, 3, :, 1].astype(jnp.int32).reshape(slot_total)
    live_from = remote[:, 3, 0, 2].astype(jnp.int32)

    f1, f2 = pl.pallas_call(
        pair_kernel,
        out_shape=(
            jax.ShapeDtypeStruct((block_total, 8, 128), jnp.float32),
            jax.ShapeDtypeStruct((peer_total * 3 * slot_cap, 128), jnp.float32),
        ),
        in_specs=[smem, smem, vmem, vmem, vmem, vmem],
        out_specs=(vmem, vmem),
        scratch_shapes=[pltpu.SMEM((slot_total,), jnp.int32), pltpu.SMEM((slot_total,), jnp.int32)],
    )(live_from, req_ids, my_rows, remote.reshape(peer_total * 4 * slot_cap, 128), halo_low, halo_high)

    returned = lax.all_to_all(
        f2.reshape(peer_total, 3, slot_cap, 128), ("xa", "xb"), split_axis=0, concat_axis=0, tiled=True
    )
    new_velocity, new_displacement = pl.pallas_call(
        functools.partial(back_kernel, slot_cap),
        out_shape=(
            jax.ShapeDtypeStruct(velocity.shape, jnp.float32),
            jax.ShapeDtypeStruct(displacement.shape, jnp.float32),
        ),
        in_specs=[smem, smem, vmem, vmem, vmem, vmem, vmem],
        out_specs=(vmem, vmem),
        scratch_shapes=[pltpu.VMEM((block_total * 8, 128), jnp.float32)],
    )(mine_flat, pair_count[0, 0], f1.reshape(block_total * 8, 128), returned.reshape(peer_total * 3 * slot_cap, 128),
      velocity, displacement, beam)
    return (new_velocity, new_displacement)


def solution(mesh):
    in_specs = (
        P(None, ("xa", "xb"), "len"),
        P(None, ("xa", "xb"), "len"),
        P(None, ("xa", "xb")),
        P(("xa", "xb"), "len"),
        P("len", ("xa", "xb"), None, None, None),
        P("len", ("xa", "xb"), None),
    )
    out_specs = (P(None, ("xa", "xb"), "len"), P(None, ("xa", "xb"), "len"))
    return jax.shard_map(local, mesh=mesh, in_specs=in_specs, out_specs=out_specs, check_vma=False)
```

```python
import functools

import jax
import jax.numpy as jnp
from jax import lax
from jax.experimental import pallas as pl
from jax.experimental.pallas import tpu as pltpu
from jax.sharding import PartitionSpec as P

spacing = 1.0 / 128.0
axial_stiff = 1.0
bend_stiff = 0.25
contact_stiff = 1.0 / 16.0
time_step = 0.2
damping = 0.9
masked_far = 1.0e4
HIGH = lax.Precision.HIGH
tile_group = 16
slot_step = 4


def halos(block, axis, dim, width):
    count = lax.axis_size(axis)
    forward = [(i, i + 1) for i in range(count - 1)]
    backward = [(target, source) for source, target in forward]
    low = lax.ppermute(
        lax.slice_in_dim(block, block.shape[dim] - width, None, axis=dim), axis, forward
    )
    high = lax.ppermute(lax.slice_in_dim(block, 0, width, axis=dim), axis, backward)
    return low, high


def chain_force(padded):
    center = padded[:, :, 2:-2]
    next_one = padded[:, :, 3:-1]
    prev_one = padded[:, :, 1:-3]
    next_two = padded[:, :, 4:]
    prev_two = padded[:, :, :-4]
    axial = next_one - 2.0 * center + prev_one
    bending = next_two - 4.0 * next_one + 6.0 * center - 4.0 * prev_one + prev_two
    return axial_stiff * axial - bend_stiff * bending


def rows_of(x, near):
    row = lax.broadcasted_iota(jnp.int32, (8, 128), 0)
    lane = lax.broadcasted_iota(jnp.int32, (1, 128), 1).astype(jnp.float32)
    v0, v1, v2 = x[0:1], x[1:2], x[2:3]
    on = jnp.where(lane < x[3:4, 0:1], 1.0, 0.0)
    norm = v0 * v0 + v1 * v1 + v2 * v2
    far = masked_far * (1.0 - on)
    pick = lambda r, v: jnp.where(row == r, jnp.broadcast_to(v, (8, 128)), 0.0)
    if near:
        return (pick(0, v0) + pick(1, v1) + pick(2, v2) + jnp.where((row == 3) | (row == 6), 1.0, 0.0)
                + pick(4, norm) + pick(5, far))
    rd = (pick(0, -2.0 * v0) + pick(1, -2.0 * v1) + pick(2, -2.0 * v2) + pick(3, norm)
          + jnp.where((row == 4) | (row == 5), 1.0, 0.0) + pick(6, far))
    rq = pick(0, v0) + pick(1, v1) + pick(2, v2) + jnp.where(row == 3, 1.0, 0.0)
    return rd, rq


def tile_two(m_a, m_b, rd_a, rd_b, rq_a, rq_b):
    zero = jnp.zeros((8, 128), jnp.float32)
    mine = jnp.concatenate(
        [jnp.concatenate([m_a, zero], axis=1), jnp.concatenate([zero, m_b], axis=1)], axis=0
    )
    dist = lax.dot_general(
        jnp.concatenate([rd_a, rd_b], axis=0), mine, (((0,), (0,)), ((), ())), precision=HIGH,
        preferred_element_type=jnp.float32,
    )
    w = jnp.exp(-dist)
    f1 = lax.dot_general(
        jnp.concatenate([rq_a, rq_b], axis=0), w, (((1,), (0,)), ((), ())), precision=HIGH,
        preferred_element_type=jnp.float32,
    )
    f2 = lax.dot_general(
        mine, w, (((1,), (1,)), ((), ())), precision=HIGH, preferred_element_type=jnp.float32
    )
    f1 = f1 * contact_stiff
    f2 = f2 * contact_stiff
    out = []
    for m, rq, g1, g2 in ((m_a, rq_a, f1[0:8, 0:128], f2[0:8]), (m_b, rq_b, f1[8:16, 128:256], f2[8:16])):
        out.append((m * g1[3:4, :] - g1, (rq * g2[3:4, :] - g2)[0:3, :]))
    return out


def peer_row(slot, rows, cap):
    return (slot // cap) * rows * cap + slot % cap


def pack_kernel(mine_ref, their_ref, cnt_ref, rows_ref, lent_ref):
    peers = cnt_ref.shape[0]
    cap = mine_ref.shape[0] // peers
    blocks = rows_ref.shape[0]
    row = lax.broadcasted_iota(jnp.int32, (4, 128), 0)
    lane = lax.broadcasted_iota(jnp.int32, (4, 128), 1)

    lent_ref[...] = jnp.zeros(lent_ref.shape, lent_ref.dtype)

    def peer(d, carry):
        live = cnt_ref[d]

        sent = jnp.clip(live, 1, cap)

        def step(g, carry):
            for k in range(slot_step):
                c = jnp.minimum(g * slot_step + k, sent - 1)
                s = d * cap + c
                x = rows_ref[jnp.clip(mine_ref[s], 0, blocks - 1)]
                x = jnp.where((row == 3) & (lane == 1), their_ref[s].astype(jnp.float32), x)
                x = jnp.where((row == 3) & (lane == 2), live.astype(jnp.float32), x)
                lent_ref[pl.ds(d * 4 * cap + c, 4, stride=cap), :] = x
            return carry

        return lax.fori_loop(0, (sent + slot_step - 1) // slot_step, step, carry)

    lax.fori_loop(0, peers, peer, 0)


def pair_kernel(cnt_ref, req_ref, m_ref, rem_ref, low_ref, high_ref, f1_ref, f2_ref, lb_ref, ls_ref):
    f1_ref[...] = jnp.zeros(f1_ref.shape, f1_ref.dtype)
    f2_ref[...] = jnp.zeros(f2_ref.shape, f2_ref.dtype)
    peers = cnt_ref.shape[0]
    cap = req_ref.shape[0] // peers
    blocks = m_ref.shape[0]

    def listed(d, n):
        def held(c, n):
            lb_ref[n] = jnp.clip(req_ref[d * cap + c], 0, blocks - 1)
            ls_ref[n] = d * cap + c
            return n + 1

        return lax.fori_loop(0, jnp.clip(cnt_ref[d], 0, cap), held, n)

    total = lax.fori_loop(0, peers, listed, 0)
    last = jnp.maximum(total - 1, 0)

    def group(g, carry):
        done = []
        for k in range(0, tile_group, 2):
            picked = []
            for t in (g * tile_group + k, g * tile_group + k + 1):
                at = jnp.minimum(t, last)
                picked.append((t, lb_ref[at], ls_ref[at]))
            (t_a, b_a, s_a), (t_b, b_b, s_b) = picked
            rd_a, rq_a = rows_of(rem_ref[pl.ds(peer_row(s_a, 4, cap), 4, stride=cap), :], False)
            rd_b, rq_b = rows_of(rem_ref[pl.ds(peer_row(s_b, 4, cap), 4, stride=cap), :], False)
            pair = tile_two(rows_of(m_ref[b_a], True), rows_of(m_ref[b_b], True), rd_a, rd_b, rq_a, rq_b)
            for (t, b, slot), (on_first, on_second) in zip(picked, pair):
                done.append((b, slot, jnp.where(t < total, on_first, 0.0), on_second))
        for b, slot, on_first, on_second in done:
            f1_ref[b] = f1_ref[b] + on_first
            f2_ref[pl.ds(peer_row(slot, 3, cap), 3, stride=cap), :] = on_second
        return carry

    lax.fori_loop(0, (total + tile_group - 1) // tile_group, group, 0)


def back_kernel(cap, mine_ref, cnt_ref, f1_ref, ret_ref, vel_ref, disp_ref, beam_ref, nv_ref, nd_ref, acc_ref):
    acc_ref[...] = f1_ref[...]
    blocks = vel_ref.shape[1]

    def peer(d, carry):
        live = jnp.clip(cnt_ref[d], 0, cap)

        def step(g, carry):
            for k in range(slot_step):
                c = g * slot_step + k
                at = jnp.minimum(c, live - 1)
                b = jnp.clip(mine_ref[d * cap + at], 0, blocks - 1)
                start = pl.multiple_of(b * 8, 8)
                got = ret_ref[pl.ds(d * 3 * cap + at, 3, stride=cap), :]
                acc_ref[pl.ds(start, 3), :] = acc_ref[pl.ds(start, 3), :] + jnp.where(c < live, got, 0.0)
            return carry

        return lax.fori_loop(0, (live + slot_step - 1) // slot_step, step, carry)

    lax.fori_loop(0, cnt_ref.shape[0], peer, 0)
    for c in range(3):
        contact = acc_ref[pl.ds(c, blocks, stride=8), :]
        new_velocity = damping * vel_ref[c] + time_step * (beam_ref[c] + contact)
        nv_ref[c] = new_velocity
        nd_ref[c] = disp_ref[c] + time_step * new_velocity


def local(displacement, velocity, anchors, seg_live, pair_blocks, pair_count):
    seg_len = displacement.shape[2]
    fibre_count = displacement.shape[1]
    per_fibre = seg_len // 128
    block_total = fibre_count * per_fibre
    peer_total = pair_blocks.shape[2]
    slot_cap = pair_blocks.shape[3]
    slot_total = peer_total * slot_cap
    halo_low, halo_high = halos(displacement, "len", 2, 2)
    beam = chain_force(jnp.concatenate([halo_low, displacement, halo_high], axis=2))

    height = jnp.arange(seg_len, dtype=jnp.int32).astype(jnp.float32) * spacing
    lift = jnp.stack([jnp.zeros_like(height), jnp.zeros_like(height), height])
    positions = displacement + anchors[:, :, None] + lift[:, None, :]
    blocks = positions.reshape(3, block_total, 128).transpose(1, 0, 2)
    lanes = jnp.arange(128, dtype=jnp.int32)
    seg_count = seg_live.reshape(block_total).astype(jnp.float32)
    meta = jnp.where(lanes[None, :] == 0, seg_count[:, None], 0.0)
    my_rows = jnp.concatenate([blocks, meta[:, None, :]], axis=1)

    mine_flat = pair_blocks[0, 0, :, :, 0].reshape(slot_total)
    their_flat = pair_blocks[0, 0, :, :, 1].reshape(slot_total)
    smem = pl.BlockSpec(memory_space=pltpu.SMEM)
    vmem = pl.BlockSpec(memory_space=pltpu.VMEM)
    lent = pl.pallas_call(
        pack_kernel,
        out_shape=jax.ShapeDtypeStruct((peer_total * 4 * slot_cap, 128), jnp.float32),
        in_specs=[smem, smem, smem, vmem],
        out_specs=vmem,
    )(mine_flat, their_flat, pair_count[0, 0], my_rows)
    remote = lax.all_to_all(
        lent.reshape(peer_total, 4, slot_cap, 128), ("xa", "xb"), split_axis=0, concat_axis=0, tiled=True
    )
    req_ids = remote[:, 3, :, 1].astype(jnp.int32).reshape(slot_total)
    live_from = remote[:, 3, 0, 2].astype(jnp.int32)

    f1, f2 = pl.pallas_call(
        pair_kernel,
        out_shape=(
            jax.ShapeDtypeStruct((block_total, 8, 128), jnp.float32),
            jax.ShapeDtypeStruct((peer_total * 3 * slot_cap, 128), jnp.float32),
        ),
        in_specs=[smem, smem, vmem, vmem, vmem, vmem],
        out_specs=(vmem, vmem),
        scratch_shapes=[pltpu.SMEM((slot_total,), jnp.int32), pltpu.SMEM((slot_total,), jnp.int32)],
    )(live_from, req_ids, my_rows, remote.reshape(peer_total * 4 * slot_cap, 128), halo_low, halo_high)

    returned = lax.all_to_all(
        f2.reshape(peer_total, 3, slot_cap, 128), ("xa", "xb"), split_axis=0, concat_axis=0, tiled=True
    )
    new_velocity, new_displacement = pl.pallas_call(
        functools.partial(back_kernel, slot_cap),
        out_shape=(
            jax.ShapeDtypeStruct(velocity.shape, jnp.float32),
            jax.ShapeDtypeStruct(displacement.shape, jnp.float32),
        ),
        in_specs=[smem, smem, vmem, vmem, vmem, vmem, vmem],
        out_specs=(vmem, vmem),
        scratch_shapes=[pltpu.VMEM((block_total * 8, 128), jnp.float32)],
    )(mine_flat, pair_count[0, 0], f1.reshape(block_total * 8, 128), returned.reshape(peer_total * 3 * slot_cap, 128),
      velocity, displacement, beam)
    return (new_velocity, new_displacement)


def solution(mesh):
    in_specs = (
        P(None, ("xa", "xb"), "len"),
        P(None, ("xa", "xb"), "len"),
        P(None, ("xa", "xb")),
        P(("xa", "xb"), "len"),
        P("len", ("xa", "xb"), None, None, None),
        P("len", ("xa", "xb"), None),
    )
    out_specs = (P(None, ("xa", "xb"), "len"), P(None, ("xa", "xb"), "len"))
    return jax.shard_map(local, mesh=mesh, in_specs=in_specs, out_specs=out_specs, check_vma=False)
```

```python
import functools

import jax
import jax.numpy as jnp
from jax import lax
from jax.experimental import pallas as pl
from jax.experimental.pallas import tpu as pltpu
from jax.sharding import PartitionSpec as P

spacing = 1.0 / 128.0
axial_stiff = 1.0
bend_stiff = 0.25
contact_stiff = 1.0 / 16.0
time_step = 0.2
damping = 0.9
masked_far = 1.0e4
HIGH = lax.Precision.HIGH
tile_group = 16
slot_step = 4


def halos(block, axis, dim, width):
    count = lax.axis_size(axis)
    forward = [(i, i + 1) for i in range(count - 1)]
    backward = [(target, source) for source, target in forward]
    low = lax.ppermute(
        lax.slice_in_dim(block, block.shape[dim] - width, None, axis=dim), axis, forward
    )
    high = lax.ppermute(lax.slice_in_dim(block, 0, width, axis=dim), axis, backward)
    return low, high


def chain_force(padded):
    center = padded[:, :, 2:-2]
    next_one = padded[:, :, 3:-1]
    prev_one = padded[:, :, 1:-3]
    next_two = padded[:, :, 4:]
    prev_two = padded[:, :, :-4]
    axial = next_one - 2.0 * center + prev_one
    bending = next_two - 4.0 * next_one + 6.0 * center - 4.0 * prev_one + prev_two
    return axial_stiff * axial - bend_stiff * bending


def rows_of(x, near):
    row = lax.broadcasted_iota(jnp.int32, (8, 128), 0)
    lane = lax.broadcasted_iota(jnp.int32, (1, 128), 1).astype(jnp.float32)
    v0, v1, v2 = x[0:1], x[1:2], x[2:3]
    on = jnp.where(lane < x[3:4, 0:1], 1.0, 0.0)
    norm = v0 * v0 + v1 * v1 + v2 * v2
    far = masked_far * (1.0 - on)
    pick = lambda r, v: jnp.where(row == r, jnp.broadcast_to(v, (8, 128)), 0.0)
    if near:
        return (pick(0, v0) + pick(1, v1) + pick(2, v2) + jnp.where((row == 3) | (row == 6), 1.0, 0.0)
                + pick(4, norm) + pick(5, far))
    rd = (pick(0, -2.0 * v0) + pick(1, -2.0 * v1) + pick(2, -2.0 * v2) + pick(3, norm)
          + jnp.where((row == 4) | (row == 5), 1.0, 0.0) + pick(6, far))
    rq = pick(0, v0) + pick(1, v1) + pick(2, v2) + jnp.where(row == 3, 1.0, 0.0)
    return rd, rq


def tile_two(m_a, m_b, rd_a, rd_b, rq_a, rq_b):
    zero = jnp.zeros((8, 128), jnp.float32)
    mine = jnp.concatenate(
        [jnp.concatenate([m_a, zero], axis=1), jnp.concatenate([zero, m_b], axis=1)], axis=0
    )
    dist = lax.dot_general(
        jnp.concatenate([rd_a, rd_b], axis=0), mine, (((0,), (0,)), ((), ())), precision=HIGH,
        preferred_element_type=jnp.float32,
    )
    w = jnp.exp(-dist)
    f1 = lax.dot_general(
        jnp.concatenate([rq_a, rq_b], axis=0), w, (((1,), (0,)), ((), ())), precision=HIGH,
        preferred_element_type=jnp.float32,
    )
    f2 = lax.dot_general(
        mine, w, (((1,), (1,)), ((), ())), precision=HIGH, preferred_element_type=jnp.float32
    )
    f1 = f1 * contact_stiff
    f2 = f2 * contact_stiff
    out = []
    for m, rq, g1, g2 in ((m_a, rq_a, f1[0:8, 0:128], f2[0:8]), (m_b, rq_b, f1[8:16, 128:256], f2[8:16])):
        out.append((m * g1[3:4, :] - g1, (rq * g2[3:4, :] - g2)[0:3, :]))
    return out


def peer_row(slot, rows, cap):
    return (slot // cap) * rows * cap + slot % cap


def pack_kernel(anc_ref, seg_ref, mine_ref, their_ref, cnt_ref, disp_ref, rows_ref, lent_ref):
    peers = cnt_ref.shape[0]
    cap = mine_ref.shape[0] // peers
    blocks = rows_ref.shape[0]
    row = lax.broadcasted_iota(jnp.int32, (4, 128), 0)
    lane = lax.broadcasted_iota(jnp.int32, (4, 128), 1)
    height = lax.broadcasted_iota(jnp.int32, (1, 128), 1).astype(jnp.float32) * spacing

    def block(g, carry):
        for k in range(slot_step):
            b = g * slot_step + k
            x = jnp.where((row == 3) & (lane == 0), seg_ref[b].astype(jnp.float32), 0.0)
            for c in range(3):
                v = disp_ref[c, pl.ds(b, 1), :] + anc_ref[c * blocks + b]
                if c == 2:
                    v = v + height
                x = jnp.where(row == c, jnp.broadcast_to(v, (4, 128)), x)
            rows_ref[b] = x
        return carry

    lax.fori_loop(0, blocks // slot_step, block, 0)

    lent_ref[...] = jnp.zeros(lent_ref.shape, lent_ref.dtype)

    def peer(d, carry):
        live = cnt_ref[d]

        sent = jnp.clip(live, 1, cap)

        def step(g, carry):
            for k in range(slot_step):
                c = jnp.minimum(g * slot_step + k, sent - 1)
                s = d * cap + c
                x = rows_ref[jnp.clip(mine_ref[s], 0, blocks - 1)]
                x = jnp.where((row == 3) & (lane == 1), their_ref[s].astype(jnp.float32), x)
                x = jnp.where((row == 3) & (lane == 2), live.astype(jnp.float32), x)
                lent_ref[pl.ds(d * 4 * cap + c, 4, stride=cap), :] = x
            return carry

        return lax.fori_loop(0, (sent + slot_step - 1) // slot_step, step, carry)

    lax.fori_loop(0, peers, peer, 0)


def pair_kernel(cnt_ref, req_ref, m_ref, rem_ref, low_ref, high_ref, f1_ref, f2_ref, lb_ref, ls_ref):
    f1_ref[...] = jnp.zeros(f1_ref.shape, f1_ref.dtype)
    f2_ref[...] = jnp.zeros(f2_ref.shape, f2_ref.dtype)
    peers = cnt_ref.shape[0]
    cap = req_ref.shape[0] // peers
    blocks = m_ref.shape[0]

    def listed(d, n):
        live = jnp.clip(cnt_ref[d], 0, cap)

        def held(g, n):
            for k in range(slot_step):
                c = jnp.minimum(g * slot_step + k, cap - 1)
                lb_ref[n + k] = jnp.clip(req_ref[d * cap + c], 0, blocks - 1)
                ls_ref[n + k] = d * cap + c
            return n + jnp.minimum(slot_step, live - g * slot_step)

        return lax.fori_loop(0, (live + slot_step - 1) // slot_step, held, n)

    total = lax.fori_loop(0, peers, listed, 0)
    last = jnp.maximum(total - 1, 0)

    def group(g, carry):
        done = []
        for k in range(0, tile_group, 2):
            picked = []
            for t in (g * tile_group + k, g * tile_group + k + 1):
                at = jnp.minimum(t, last)
                picked.append((t, lb_ref[at], ls_ref[at]))
            (t_a, b_a, s_a), (t_b, b_b, s_b) = picked
            rd_a, rq_a = rows_of(rem_ref[pl.ds(peer_row(s_a, 4, cap), 4, stride=cap), :], False)
            rd_b, rq_b = rows_of(rem_ref[pl.ds(peer_row(s_b, 4, cap), 4, stride=cap), :], False)
            pair = tile_two(rows_of(m_ref[b_a], True), rows_of(m_ref[b_b], True), rd_a, rd_b, rq_a, rq_b)
            for (t, b, slot), (on_first, on_second) in zip(picked, pair):
                done.append((b, slot, jnp.where(t < total, on_first, 0.0), on_second))
        for b, slot, on_first, on_second in done:
            f1_ref[b] = f1_ref[b] + on_first
            f2_ref[pl.ds(peer_row(slot, 3, cap), 3, stride=cap), :] = on_second
        return carry

    lax.fori_loop(0, (total + tile_group - 1) // tile_group, group, 0)


def back_kernel(cap, mine_ref, cnt_ref, f1_ref, ret_ref, vel_ref, disp_ref, beam_ref, nv_ref, nd_ref, acc_ref):
    acc_ref[...] = f1_ref[...]
    blocks = vel_ref.shape[1]

    def peer(d, carry):
        live = jnp.clip(cnt_ref[d], 0, cap)

        def step(g, carry):
            for k in range(slot_step):
                c = g * slot_step + k
                at = jnp.minimum(c, live - 1)
                b = jnp.clip(mine_ref[d * cap + at], 0, blocks - 1)
                start = pl.multiple_of(b * 8, 8)
                got = ret_ref[pl.ds(d * 3 * cap + at, 3, stride=cap), :]
                acc_ref[pl.ds(start, 3), :] = acc_ref[pl.ds(start, 3), :] + jnp.where(c < live, got, 0.0)
            return carry

        return lax.fori_loop(0, (live + slot_step - 1) // slot_step, step, carry)

    lax.fori_loop(0, cnt_ref.shape[0], peer, 0)
    for c in range(3):
        contact = acc_ref[pl.ds(c, blocks, stride=8), :]
        new_velocity = damping * vel_ref[c] + time_step * (beam_ref[c] + contact)
        nv_ref[c] = new_velocity
        nd_ref[c] = disp_ref[c] + time_step * new_velocity


def local(displacement, velocity, anchors, seg_live, pair_blocks, pair_count):
    seg_len = displacement.shape[2]
    fibre_count = displacement.shape[1]
    per_fibre = seg_len // 128
    block_total = fibre_count * per_fibre
    peer_total = pair_blocks.shape[2]
    slot_cap = pair_blocks.shape[3]
    slot_total = peer_total * slot_cap
    halo_low, halo_high = halos(displacement, "len", 2, 2)
    beam = chain_force(jnp.concatenate([halo_low, displacement, halo_high], axis=2))

    mine_flat = pair_blocks[0, 0, :, :, 0].reshape(slot_total)
    their_flat = pair_blocks[0, 0, :, :, 1].reshape(slot_total)
    smem = pl.BlockSpec(memory_space=pltpu.SMEM)
    vmem = pl.BlockSpec(memory_space=pltpu.VMEM)
    my_rows, lent = pl.pallas_call(
        pack_kernel,
        out_shape=(
            jax.ShapeDtypeStruct((block_total, 4, 128), jnp.float32),
            jax.ShapeDtypeStruct((peer_total * 4 * slot_cap, 128), jnp.float32),
        ),
        in_specs=[smem, smem, smem, smem, smem, vmem],
        out_specs=(vmem, vmem),
    )(anchors.reshape(3 * block_total), seg_live.reshape(block_total), mine_flat, their_flat,
      pair_count[0, 0], displacement)
    remote = lax.all_to_all(
        lent.reshape(peer_total, 4, slot_cap, 128), ("xa", "xb"), split_axis=0, concat_axis=0, tiled=True
    )
    req_ids = remote[:, 3, :, 1].astype(jnp.int32).reshape(slot_total)
    live_from = remote[:, 3, 0, 2].astype(jnp.int32)

    f1, f2 = pl.pallas_call(
        pair_kernel,
        out_shape=(
            jax.ShapeDtypeStruct((block_total, 8, 128), jnp.float32),
            jax.ShapeDtypeStruct((peer_total * 3 * slot_cap, 128), jnp.float32),
        ),
        in_specs=[smem, smem, vmem, vmem, vmem, vmem],
        out_specs=(vmem, vmem),
        scratch_shapes=[pltpu.SMEM((slot_total + slot_step,), jnp.int32)] * 2,
    )(live_from, req_ids, my_rows, remote.reshape(peer_total * 4 * slot_cap, 128), halo_low, halo_high)

    returned = lax.all_to_all(
        f2.reshape(peer_total, 3, slot_cap, 128), ("xa", "xb"), split_axis=0, concat_axis=0, tiled=True
    )
    new_velocity, new_displacement = pl.pallas_call(
        functools.partial(back_kernel, slot_cap),
        out_shape=(
            jax.ShapeDtypeStruct(velocity.shape, jnp.float32),
            jax.ShapeDtypeStruct(displacement.shape, jnp.float32),
        ),
        in_specs=[smem, smem, vmem, vmem, vmem, vmem, vmem],
        out_specs=(vmem, vmem),
        scratch_shapes=[pltpu.VMEM((block_total * 8, 128), jnp.float32)],
    )(mine_flat, pair_count[0, 0], f1.reshape(block_total * 8, 128), returned.reshape(peer_total * 3 * slot_cap, 128),
      velocity, displacement, beam)
    return (new_velocity, new_displacement)


def solution(mesh):
    in_specs = (
        P(None, ("xa", "xb"), "len"),
        P(None, ("xa", "xb"), "len"),
        P(None, ("xa", "xb")),
        P(("xa", "xb"), "len"),
        P("len", ("xa", "xb"), None, None, None),
        P("len", ("xa", "xb"), None),
    )
    out_specs = (P(None, ("xa", "xb"), "len"), P(None, ("xa", "xb"), "len"))
    return jax.shard_map(local, mesh=mesh, in_specs=in_specs, out_specs=out_specs, check_vma=False)
```

```python
import functools

import jax
import jax.numpy as jnp
from jax import lax
from jax.experimental import pallas as pl
from jax.experimental.pallas import tpu as pltpu
from jax.sharding import PartitionSpec as P

spacing = 1.0 / 128.0
axial_stiff = 1.0
bend_stiff = 0.25
contact_stiff = 1.0 / 16.0
time_step = 0.2
damping = 0.9
masked_far = 1.0e4
HIGH = lax.Precision.HIGH
tile_group = 16
slot_step = 4


def halos(block, axis, dim, width):
    count = lax.axis_size(axis)
    forward = [(i, i + 1) for i in range(count - 1)]
    backward = [(target, source) for source, target in forward]
    low = lax.ppermute(
        lax.slice_in_dim(block, block.shape[dim] - width, None, axis=dim), axis, forward
    )
    high = lax.ppermute(lax.slice_in_dim(block, 0, width, axis=dim), axis, backward)
    return low, high


def chain_force(padded):
    center = padded[:, :, 2:-2]
    next_one = padded[:, :, 3:-1]
    prev_one = padded[:, :, 1:-3]
    next_two = padded[:, :, 4:]
    prev_two = padded[:, :, :-4]
    axial = next_one - 2.0 * center + prev_one
    bending = next_two - 4.0 * next_one + 6.0 * center - 4.0 * prev_one + prev_two
    return axial_stiff * axial - bend_stiff * bending


def split3(v):
    hi = v.astype(jnp.bfloat16).astype(jnp.float32)
    rest = v - hi
    mid = rest.astype(jnp.bfloat16).astype(jnp.float32)
    lo = (rest - mid).astype(jnp.bfloat16).astype(jnp.float32)
    return hi, mid, lo


def stack_rows(rows):
    row = lax.broadcasted_iota(jnp.int32, (8, 128), 0)
    groups = []
    for g in range(4):
        acc = jnp.zeros((8, 128), jnp.float32)
        for r, v in enumerate(rows[8 * g:8 * g + 8]):
            acc = acc + jnp.where(row == r, jnp.broadcast_to(v, (8, 128)), 0.0)
        groups.append(acc)
    return jnp.concatenate(groups, axis=0)


def rows_of(x, near):
    lane = lax.broadcasted_iota(jnp.int32, (1, 128), 1).astype(jnp.float32)
    v = [x[0:1], x[1:2], x[2:3]]
    on = jnp.where(lane < x[3:4, 0:1], 1.0, 0.0)
    norm = v[0] * v[0] + v[1] * v[1] + v[2] * v[2]
    far = masked_far * (1.0 - on)
    one = jnp.ones((1, 128), jnp.float32)
    rows = []
    if near:
        for c in range(3):
            hi, mid, lo = split3(v[c])
            rows += [hi, mid, hi, mid, lo, hi]
        rows += [one, one, one] + list(split3(norm)) + [one, far]
        return stack_rows(rows), None
    for c in range(3):
        hi, mid, lo = split3(-2.0 * v[c])
        rows += [hi, hi, mid, mid, hi, lo]
    rows += list(split3(norm)) + [one, one, one] + [far, one]
    row = lax.broadcasted_iota(jnp.int32, (8, 128), 0)
    rq = (jnp.where(row == 0, jnp.broadcast_to(v[0], (8, 128)), 0.0)
          + jnp.where(row == 1, jnp.broadcast_to(v[1], (8, 128)), 0.0)
          + jnp.where(row == 2, jnp.broadcast_to(v[2], (8, 128)), 0.0) + jnp.where(row == 3, 1.0, 0.0))
    return stack_rows(rows), rq


def side_rows(x):
    row = lax.broadcasted_iota(jnp.int32, (8, 128), 0)
    return (jnp.where(row == 0, jnp.broadcast_to(x[0:1], (8, 128)), 0.0)
            + jnp.where(row == 1, jnp.broadcast_to(x[1:2], (8, 128)), 0.0)
            + jnp.where(row == 2, jnp.broadcast_to(x[2:3], (8, 128)), 0.0) + jnp.where(row == 3, 1.0, 0.0))


def tile_two(m_a, m_b, s_a, s_b, rd_a, rd_b, rq_a, rq_b):
    zero = jnp.zeros(m_a.shape, jnp.float32)
    mine = jnp.concatenate(
        [jnp.concatenate([m_a, zero], axis=1), jnp.concatenate([zero, m_b], axis=1)], axis=0
    )
    dist = lax.dot_general(
        jnp.concatenate([rd_a, rd_b], axis=0), mine, (((0,), (0,)), ((), ())),
        preferred_element_type=jnp.float32,
    )
    w = jnp.exp(-dist)
    zero = jnp.zeros((8, 128), jnp.float32)
    side = jnp.concatenate(
        [jnp.concatenate([s_a, zero], axis=1), jnp.concatenate([zero, s_b], axis=1)], axis=0
    )
    f1 = lax.dot_general(
        jnp.concatenate([rq_a, rq_b], axis=0), w, (((1,), (0,)), ((), ())), precision=HIGH,
        preferred_element_type=jnp.float32,
    )
    f2 = lax.dot_general(
        side, w, (((1,), (1,)), ((), ())), precision=HIGH, preferred_element_type=jnp.float32
    )
    f1 = f1 * contact_stiff
    f2 = f2 * contact_stiff
    out = []
    for m, rq, g1, g2 in ((s_a, rq_a, f1[0:8, 0:128], f2[0:8]), (s_b, rq_b, f1[8:16, 128:256], f2[8:16])):
        out.append((m * g1[3:4, :] - g1, (rq * g2[3:4, :] - g2)[0:3, :]))
    return out


def peer_row(slot, rows, cap):
    return (slot // cap) * rows * cap + slot % cap


def pack_kernel(anc_ref, seg_ref, mine_ref, their_ref, cnt_ref, disp_ref, rows_ref, lent_ref):
    peers = cnt_ref.shape[0]
    cap = mine_ref.shape[0] // peers
    blocks = rows_ref.shape[0]
    row = lax.broadcasted_iota(jnp.int32, (4, 128), 0)
    lane = lax.broadcasted_iota(jnp.int32, (4, 128), 1)
    height = lax.broadcasted_iota(jnp.int32, (1, 128), 1).astype(jnp.float32) * spacing

    def block(g, carry):
        for k in range(slot_step):
            b = g * slot_step + k
            x = jnp.where((row == 3) & (lane == 0), seg_ref[b].astype(jnp.float32), 0.0)
            for c in range(3):
                v = disp_ref[c, pl.ds(b, 1), :] + anc_ref[c * blocks + b]
                if c == 2:
                    v = v + height
                x = jnp.where(row == c, jnp.broadcast_to(v, (4, 128)), x)
            rows_ref[b] = x
        return carry

    lax.fori_loop(0, blocks // slot_step, block, 0)

    lent_ref[...] = jnp.zeros(lent_ref.shape, lent_ref.dtype)

    def peer(d, carry):
        live = cnt_ref[d]

        sent = jnp.clip(live, 1, cap)

        def step(g, carry):
            for k in range(slot_step):
                c = jnp.minimum(g * slot_step + k, sent - 1)
                s = d * cap + c
                x = rows_ref[jnp.clip(mine_ref[s], 0, blocks - 1)]
                x = jnp.where((row == 3) & (lane == 1), their_ref[s].astype(jnp.float32), x)
                x = jnp.where((row == 3) & (lane == 2), live.astype(jnp.float32), x)
                lent_ref[pl.ds(d * 4 * cap + c, 4, stride=cap), :] = x
            return carry

        return lax.fori_loop(0, (sent + slot_step - 1) // slot_step, step, carry)

    lax.fori_loop(0, peers, peer, 0)


def pair_kernel(cnt_ref, req_ref, m_ref, rem_ref, low_ref, high_ref, f1_ref, f2_ref, lb_ref, ls_ref):
    f1_ref[...] = jnp.zeros(f1_ref.shape, f1_ref.dtype)
    f2_ref[...] = jnp.zeros(f2_ref.shape, f2_ref.dtype)
    peers = cnt_ref.shape[0]
    cap = req_ref.shape[0] // peers
    blocks = m_ref.shape[0]

    def listed(d, n):
        live = jnp.clip(cnt_ref[d], 0, cap)

        def held(g, n):
            for k in range(slot_step):
                c = jnp.minimum(g * slot_step + k, cap - 1)
                lb_ref[n + k] = jnp.clip(req_ref[d * cap + c], 0, blocks - 1)
                ls_ref[n + k] = d * cap + c
            return n + jnp.minimum(slot_step, live - g * slot_step)

        return lax.fori_loop(0, (live + slot_step - 1) // slot_step, held, n)

    total = lax.fori_loop(0, peers, listed, 0)
    last = jnp.maximum(total - 1, 0)

    def group(g, carry):
        done = []
        for k in range(0, tile_group, 2):
            picked = []
            for t in (g * tile_group + k, g * tile_group + k + 1):
                at = jnp.minimum(t, last)
                picked.append((t, lb_ref[at], ls_ref[at]))
            (t_a, b_a, s_a), (t_b, b_b, s_b) = picked
            rd_a, rq_a = rows_of(rem_ref[pl.ds(peer_row(s_a, 4, cap), 4, stride=cap), :], False)
            rd_b, rq_b = rows_of(rem_ref[pl.ds(peer_row(s_b, 4, cap), 4, stride=cap), :], False)
            x_a = m_ref[b_a]
            x_b = m_ref[b_b]
            pair = tile_two(
                rows_of(x_a, True)[0], rows_of(x_b, True)[0], side_rows(x_a), side_rows(x_b),
                rd_a, rd_b, rq_a, rq_b,
            )
            for (t, b, slot), (on_first, on_second) in zip(picked, pair):
                done.append((b, slot, jnp.where(t < total, on_first, 0.0), on_second))
        for b, slot, on_first, on_second in done:
            f1_ref[b] = f1_ref[b] + on_first
            f2_ref[pl.ds(peer_row(slot, 3, cap), 3, stride=cap), :] = on_second
        return carry

    lax.fori_loop(0, (total + tile_group - 1) // tile_group, group, 0)


def back_kernel(cap, mine_ref, cnt_ref, f1_ref, ret_ref, vel_ref, disp_ref, beam_ref, nv_ref, nd_ref, acc_ref):
    acc_ref[...] = f1_ref[...]
    blocks = vel_ref.shape[1]

    def peer(d, carry):
        live = jnp.clip(cnt_ref[d], 0, cap)

        def step(g, carry):
            for k in range(slot_step):
                c = g * slot_step + k
                at = jnp.minimum(c, live - 1)
                b = jnp.clip(mine_ref[d * cap + at], 0, blocks - 1)
                start = pl.multiple_of(b * 8, 8)
                got = ret_ref[pl.ds(d * 3 * cap + at, 3, stride=cap), :]
                acc_ref[pl.ds(start, 3), :] = acc_ref[pl.ds(start, 3), :] + jnp.where(c < live, got, 0.0)
            return carry

        return lax.fori_loop(0, (live + slot_step - 1) // slot_step, step, carry)

    lax.fori_loop(0, cnt_ref.shape[0], peer, 0)
    for c in range(3):
        contact = acc_ref[pl.ds(c, blocks, stride=8), :]
        new_velocity = damping * vel_ref[c] + time_step * (beam_ref[c] + contact)
        nv_ref[c] = new_velocity
        nd_ref[c] = disp_ref[c] + time_step * new_velocity


def local(displacement, velocity, anchors, seg_live, pair_blocks, pair_count):
    seg_len = displacement.shape[2]
    fibre_count = displacement.shape[1]
    per_fibre = seg_len // 128
    block_total = fibre_count * per_fibre
    peer_total = pair_blocks.shape[2]
    slot_cap = pair_blocks.shape[3]
    slot_total = peer_total * slot_cap
    halo_low, halo_high = halos(displacement, "len", 2, 2)
    beam = chain_force(jnp.concatenate([halo_low, displacement, halo_high], axis=2))

    mine_flat = pair_blocks[0, 0, :, :, 0].reshape(slot_total)
    their_flat = pair_blocks[0, 0, :, :, 1].reshape(slot_total)
    smem = pl.BlockSpec(memory_space=pltpu.SMEM)
    vmem = pl.BlockSpec(memory_space=pltpu.VMEM)
    my_rows, lent = pl.pallas_call(
        pack_kernel,
        out_shape=(
            jax.ShapeDtypeStruct((block_total, 4, 128), jnp.float32),
            jax.ShapeDtypeStruct((peer_total * 4 * slot_cap, 128), jnp.float32),
        ),
        in_specs=[smem, smem, smem, smem, smem, vmem],
        out_specs=(vmem, vmem),
    )(anchors.reshape(3 * block_total), seg_live.reshape(block_total), mine_flat, their_flat,
      pair_count[0, 0], displacement)
    remote = lax.all_to_all(
        lent.reshape(peer_total, 4, slot_cap, 128), ("xa", "xb"), split_axis=0, concat_axis=0, tiled=True
    )
    req_ids = remote[:, 3, :, 1].astype(jnp.int32).reshape(slot_total)
    live_from = remote[:, 3, 0, 2].astype(jnp.int32)

    f1, f2 = pl.pallas_call(
        pair_kernel,
        out_shape=(
            jax.ShapeDtypeStruct((block_total, 8, 128), jnp.float32),
            jax.ShapeDtypeStruct((peer_total * 3 * slot_cap, 128), jnp.float32),
        ),
        in_specs=[smem, smem, vmem, vmem, vmem, vmem],
        out_specs=(vmem, vmem),
        scratch_shapes=[pltpu.SMEM((slot_total + slot_step,), jnp.int32)] * 2,
    )(live_from, req_ids, my_rows, remote.reshape(peer_total * 4 * slot_cap, 128), halo_low, halo_high)

    returned = lax.all_to_all(
        f2.reshape(peer_total, 3, slot_cap, 128), ("xa", "xb"), split_axis=0, concat_axis=0, tiled=True
    )
    new_velocity, new_displacement = pl.pallas_call(
        functools.partial(back_kernel, slot_cap),
        out_shape=(
            jax.ShapeDtypeStruct(velocity.shape, jnp.float32),
            jax.ShapeDtypeStruct(displacement.shape, jnp.float32),
        ),
        in_specs=[smem, smem, vmem, vmem, vmem, vmem, vmem],
        out_specs=(vmem, vmem),
        scratch_shapes=[pltpu.VMEM((block_total * 8, 128), jnp.float32)],
    )(mine_flat, pair_count[0, 0], f1.reshape(block_total * 8, 128), returned.reshape(peer_total * 3 * slot_cap, 128),
      velocity, displacement, beam)
    return (new_velocity, new_displacement)


def solution(mesh):
    in_specs = (
        P(None, ("xa", "xb"), "len"),
        P(None, ("xa", "xb"), "len"),
        P(None, ("xa", "xb")),
        P(("xa", "xb"), "len"),
        P("len", ("xa", "xb"), None, None, None),
        P("len", ("xa", "xb"), None),
    )
    out_specs = (P(None, ("xa", "xb"), "len"), P(None, ("xa", "xb"), "len"))
    return jax.shard_map(local, mesh=mesh, in_specs=in_specs, out_specs=out_specs, check_vma=False)
```

```python
import functools

import jax
import jax.numpy as jnp
from jax import lax
from jax.experimental import pallas as pl
from jax.experimental.pallas import tpu as pltpu
from jax.sharding import PartitionSpec as P

spacing = 1.0 / 128.0
axial_stiff = 1.0
bend_stiff = 0.25
contact_stiff = 1.0 / 16.0
time_step = 0.2
damping = 0.9
masked_far = 1.0e4
HIGH = lax.Precision.HIGH
tile_group = 16
slot_step = 4


def halos(block, axis, dim, width):
    count = lax.axis_size(axis)
    forward = [(i, i + 1) for i in range(count - 1)]
    backward = [(target, source) for source, target in forward]
    low = lax.ppermute(
        lax.slice_in_dim(block, block.shape[dim] - width, None, axis=dim), axis, forward
    )
    high = lax.ppermute(lax.slice_in_dim(block, 0, width, axis=dim), axis, backward)
    return low, high


def chain_force(padded):
    center = padded[:, :, 2:-2]
    next_one = padded[:, :, 3:-1]
    prev_one = padded[:, :, 1:-3]
    next_two = padded[:, :, 4:]
    prev_two = padded[:, :, :-4]
    axial = next_one - 2.0 * center + prev_one
    bending = next_two - 4.0 * next_one + 6.0 * center - 4.0 * prev_one + prev_two
    return axial_stiff * axial - bend_stiff * bending


def split3(v):
    hi = v.astype(jnp.bfloat16).astype(jnp.float32)
    rest = v - hi
    mid = rest.astype(jnp.bfloat16).astype(jnp.float32)
    lo = (rest - mid).astype(jnp.bfloat16).astype(jnp.float32)
    return hi, mid, lo


def stack_rows(rows):
    row = lax.broadcasted_iota(jnp.int32, (8, 128), 0)
    groups = []
    for g in range(4):
        acc = jnp.zeros((8, 128), jnp.float32)
        for r, v in enumerate(rows[8 * g:8 * g + 8]):
            acc = acc + jnp.where(row == r, jnp.broadcast_to(v, (8, 128)), 0.0)
        groups.append(acc)
    return jnp.concatenate(groups, axis=0)


def rows_of(x, near):
    lane = lax.broadcasted_iota(jnp.int32, (1, 128), 1).astype(jnp.float32)
    v = [x[0:1], x[1:2], x[2:3]]
    on = jnp.where(lane < x[3:4, 0:1], 1.0, 0.0)
    norm = v[0] * v[0] + v[1] * v[1] + v[2] * v[2]
    far = masked_far * (1.0 - on)
    one = jnp.ones((1, 128), jnp.float32)
    rows = []
    if near:
        for c in range(3):
            hi, mid, lo = split3(v[c])
            rows += [hi, mid, hi, mid, lo, hi]
        rows += [one, one, one] + list(split3(norm)) + [one, far]
        return stack_rows(rows), None
    for c in range(3):
        hi, mid, lo = split3(-2.0 * v[c])
        rows += [hi, hi, mid, mid, hi, lo]
    rows += list(split3(norm)) + [one, one, one] + [far, one]
    row = lax.broadcasted_iota(jnp.int32, (8, 128), 0)
    rq = (jnp.where(row == 0, jnp.broadcast_to(v[0], (8, 128)), 0.0)
          + jnp.where(row == 1, jnp.broadcast_to(v[1], (8, 128)), 0.0)
          + jnp.where(row == 2, jnp.broadcast_to(v[2], (8, 128)), 0.0) + jnp.where(row == 3, 1.0, 0.0))
    return stack_rows(rows), rq


def side_rows(x):
    row = lax.broadcasted_iota(jnp.int32, (8, 128), 0)
    return (jnp.where(row == 0, jnp.broadcast_to(x[0:1], (8, 128)), 0.0)
            + jnp.where(row == 1, jnp.broadcast_to(x[1:2], (8, 128)), 0.0)
            + jnp.where(row == 2, jnp.broadcast_to(x[2:3], (8, 128)), 0.0) + jnp.where(row == 3, 1.0, 0.0))


def piece_sums(rows, w_hi, w_lo, axis):
    hi, mid, lo = split3(rows)
    count = rows.shape[0]
    dims = (((1,), (axis,)), ((), ()))
    by_hi = lax.dot_general(
        jnp.concatenate([hi, mid, lo], axis=0), w_hi, dims, preferred_element_type=jnp.float32
    )
    by_lo = lax.dot_general(
        jnp.concatenate([hi, mid], axis=0), w_lo, dims, preferred_element_type=jnp.float32
    )
    return (by_hi[0:count] + by_hi[count:2 * count] + by_hi[2 * count:]) + (
        by_lo[0:count] + by_lo[count:]
    )


def tile_two(m_a, m_b, s_a, s_b, rd_a, rd_b, rq_a, rq_b):
    zero = jnp.zeros(m_a.shape, jnp.float32)
    mine = jnp.concatenate(
        [jnp.concatenate([m_a, zero], axis=1), jnp.concatenate([zero, m_b], axis=1)], axis=0
    )
    dist = lax.dot_general(
        jnp.concatenate([rd_a, rd_b], axis=0), mine, (((0,), (0,)), ((), ())),
        preferred_element_type=jnp.float32,
    )
    w = jnp.exp(-dist)
    zero = jnp.zeros((8, 128), jnp.float32)
    side = jnp.concatenate(
        [jnp.concatenate([s_a, zero], axis=1), jnp.concatenate([zero, s_b], axis=1)], axis=0
    )
    w_hi = w.astype(jnp.bfloat16).astype(jnp.float32)
    w_lo = (w - w_hi).astype(jnp.bfloat16).astype(jnp.float32)
    f1 = piece_sums(jnp.concatenate([rq_a, rq_b], axis=0), w_hi, w_lo, 0)
    f2 = piece_sums(side, w_hi, w_lo, 1)
    f1 = f1 * contact_stiff
    f2 = f2 * contact_stiff
    out = []
    for m, rq, g1, g2 in ((s_a, rq_a, f1[0:8, 0:128], f2[0:8]), (s_b, rq_b, f1[8:16, 128:256], f2[8:16])):
        out.append((m * g1[3:4, :] - g1, (rq * g2[3:4, :] - g2)[0:3, :]))
    return out


def peer_row(slot, rows, cap):
    return (slot // cap) * rows * cap + slot % cap


def pack_kernel(anc_ref, seg_ref, mine_ref, their_ref, cnt_ref, disp_ref, rows_ref, lent_ref):
    peers = cnt_ref.shape[0]
    cap = mine_ref.shape[0] // peers
    blocks = rows_ref.shape[0]
    row = lax.broadcasted_iota(jnp.int32, (4, 128), 0)
    lane = lax.broadcasted_iota(jnp.int32, (4, 128), 1)
    height = lax.broadcasted_iota(jnp.int32, (1, 128), 1).astype(jnp.float32) * spacing

    def block(g, carry):
        for k in range(slot_step):
            b = g * slot_step + k
            x = jnp.where((row == 3) & (lane == 0), seg_ref[b].astype(jnp.float32), 0.0)
            for c in range(3):
                v = disp_ref[c, pl.ds(b, 1), :] + anc_ref[c * blocks + b]
                if c == 2:
                    v = v + height
                x = jnp.where(row == c, jnp.broadcast_to(v, (4, 128)), x)
            rows_ref[b] = x
        return carry

    lax.fori_loop(0, blocks // slot_step, block, 0)

    lent_ref[...] = jnp.zeros(lent_ref.shape, lent_ref.dtype)

    def peer(d, carry):
        live = cnt_ref[d]

        sent = jnp.clip(live, 1, cap)

        def step(g, carry):
            for k in range(slot_step):
                c = jnp.minimum(g * slot_step + k, sent - 1)
                s = d * cap + c
                x = rows_ref[jnp.clip(mine_ref[s], 0, blocks - 1)]
                x = jnp.where((row == 3) & (lane == 1), their_ref[s].astype(jnp.float32), x)
                x = jnp.where((row == 3) & (lane == 2), live.astype(jnp.float32), x)
                lent_ref[pl.ds(d * 4 * cap + c, 4, stride=cap), :] = x
            return carry

        return lax.fori_loop(0, (sent + slot_step - 1) // slot_step, step, carry)

    lax.fori_loop(0, peers, peer, 0)


def pair_kernel(cnt_ref, req_ref, m_ref, rem_ref, low_ref, high_ref, f1_ref, f2_ref, lb_ref, ls_ref):
    f1_ref[...] = jnp.zeros(f1_ref.shape, f1_ref.dtype)
    f2_ref[...] = jnp.zeros(f2_ref.shape, f2_ref.dtype)
    peers = cnt_ref.shape[0]
    cap = req_ref.shape[0] // peers
    blocks = m_ref.shape[0]

    def listed(d, n):
        live = jnp.clip(cnt_ref[d], 0, cap)

        def held(g, n):
            for k in range(slot_step):
                c = jnp.minimum(g * slot_step + k, cap - 1)
                lb_ref[n + k] = jnp.clip(req_ref[d * cap + c], 0, blocks - 1)
                ls_ref[n + k] = d * cap + c
            return n + jnp.minimum(slot_step, live - g * slot_step)

        return lax.fori_loop(0, (live + slot_step - 1) // slot_step, held, n)

    total = lax.fori_loop(0, peers, listed, 0)
    last = jnp.maximum(total - 1, 0)

    def group(g, carry):
        done = []
        for k in range(0, tile_group, 2):
            picked = []
            for t in (g * tile_group + k, g * tile_group + k + 1):
                at = jnp.minimum(t, last)
                picked.append((t, lb_ref[at], ls_ref[at]))
            (t_a, b_a, s_a), (t_b, b_b, s_b) = picked
            rd_a, rq_a = rows_of(rem_ref[pl.ds(peer_row(s_a, 4, cap), 4, stride=cap), :], False)
            rd_b, rq_b = rows_of(rem_ref[pl.ds(peer_row(s_b, 4, cap), 4, stride=cap), :], False)
            x_a = m_ref[b_a]
            x_b = m_ref[b_b]
            pair = tile_two(
                rows_of(x_a, True)[0], rows_of(x_b, True)[0], side_rows(x_a), side_rows(x_b),
                rd_a, rd_b, rq_a, rq_b,
            )
            for (t, b, slot), (on_first, on_second) in zip(picked, pair):
                done.append((b, slot, jnp.where(t < total, on_first, 0.0), on_second))
        for b, slot, on_first, on_second in done:
            f1_ref[b] = f1_ref[b] + on_first
            f2_ref[pl.ds(peer_row(slot, 3, cap), 3, stride=cap), :] = on_second
        return carry

    lax.fori_loop(0, (total + tile_group - 1) // tile_group, group, 0)


def back_kernel(cap, mine_ref, cnt_ref, f1_ref, ret_ref, vel_ref, disp_ref, beam_ref, nv_ref, nd_ref, acc_ref):
    acc_ref[...] = f1_ref[...]
    blocks = vel_ref.shape[1]

    def peer(d, carry):
        live = jnp.clip(cnt_ref[d], 0, cap)

        def step(g, carry):
            for k in range(slot_step):
                c = g * slot_step + k
                at = jnp.minimum(c, live - 1)
                b = jnp.clip(mine_ref[d * cap + at], 0, blocks - 1)
                start = pl.multiple_of(b * 8, 8)
                got = ret_ref[pl.ds(d * 3 * cap + at, 3, stride=cap), :]
                acc_ref[pl.ds(start, 3), :] = acc_ref[pl.ds(start, 3), :] + jnp.where(c < live, got, 0.0)
            return carry

        return lax.fori_loop(0, (live + slot_step - 1) // slot_step, step, carry)

    lax.fori_loop(0, cnt_ref.shape[0], peer, 0)
    for c in range(3):
        contact = acc_ref[pl.ds(c, blocks, stride=8), :]
        new_velocity = damping * vel_ref[c] + time_step * (beam_ref[c] + contact)
        nv_ref[c] = new_velocity
        nd_ref[c] = disp_ref[c] + time_step * new_velocity


def local(displacement, velocity, anchors, seg_live, pair_blocks, pair_count):
    seg_len = displacement.shape[2]
    fibre_count = displacement.shape[1]
    per_fibre = seg_len // 128
    block_total = fibre_count * per_fibre
    peer_total = pair_blocks.shape[2]
    slot_cap = pair_blocks.shape[3]
    slot_total = peer_total * slot_cap
    halo_low, halo_high = halos(displacement, "len", 2, 2)
    beam = chain_force(jnp.concatenate([halo_low, displacement, halo_high], axis=2))

    mine_flat = pair_blocks[0, 0, :, :, 0].reshape(slot_total)
    their_flat = pair_blocks[0, 0, :, :, 1].reshape(slot_total)
    smem = pl.BlockSpec(memory_space=pltpu.SMEM)
    vmem = pl.BlockSpec(memory_space=pltpu.VMEM)
    my_rows, lent = pl.pallas_call(
        pack_kernel,
        out_shape=(
            jax.ShapeDtypeStruct((block_total, 4, 128), jnp.float32),
            jax.ShapeDtypeStruct((peer_total * 4 * slot_cap, 128), jnp.float32),
        ),
        in_specs=[smem, smem, smem, smem, smem, vmem],
        out_specs=(vmem, vmem),
    )(anchors.reshape(3 * block_total), seg_live.reshape(block_total), mine_flat, their_flat,
      pair_count[0, 0], displacement)
    remote = lax.all_to_all(
        lent.reshape(peer_total, 4, slot_cap, 128), ("xa", "xb"), split_axis=0, concat_axis=0, tiled=True
    )
    req_ids = remote[:, 3, :, 1].astype(jnp.int32).reshape(slot_total)
    live_from = remote[:, 3, 0, 2].astype(jnp.int32)

    f1, f2 = pl.pallas_call(
        pair_kernel,
        out_shape=(
            jax.ShapeDtypeStruct((block_total, 8, 128), jnp.float32),
            jax.ShapeDtypeStruct((peer_total * 3 * slot_cap, 128), jnp.float32),
        ),
        in_specs=[smem, smem, vmem, vmem, vmem, vmem],
        out_specs=(vmem, vmem),
        scratch_shapes=[pltpu.SMEM((slot_total + slot_step,), jnp.int32)] * 2,
    )(live_from, req_ids, my_rows, remote.reshape(peer_total * 4 * slot_cap, 128), halo_low, halo_high)

    returned = lax.all_to_all(
        f2.reshape(peer_total, 3, slot_cap, 128), ("xa", "xb"), split_axis=0, concat_axis=0, tiled=True
    )
    new_velocity, new_displacement = pl.pallas_call(
        functools.partial(back_kernel, slot_cap),
        out_shape=(
            jax.ShapeDtypeStruct(velocity.shape, jnp.float32),
            jax.ShapeDtypeStruct(displacement.shape, jnp.float32),
        ),
        in_specs=[smem, smem, vmem, vmem, vmem, vmem, vmem],
        out_specs=(vmem, vmem),
        scratch_shapes=[pltpu.VMEM((block_total * 8, 128), jnp.float32)],
    )(mine_flat, pair_count[0, 0], f1.reshape(block_total * 8, 128), returned.reshape(peer_total * 3 * slot_cap, 128),
      velocity, displacement, beam)
    return (new_velocity, new_displacement)


def solution(mesh):
    in_specs = (
        P(None, ("xa", "xb"), "len"),
        P(None, ("xa", "xb"), "len"),
        P(None, ("xa", "xb")),
        P(("xa", "xb"), "len"),
        P("len", ("xa", "xb"), None, None, None),
        P("len", ("xa", "xb"), None),
    )
    out_specs = (P(None, ("xa", "xb"), "len"), P(None, ("xa", "xb"), "len"))
    return jax.shard_map(local, mesh=mesh, in_specs=in_specs, out_specs=out_specs, check_vma=False)
```

```python
import functools

import jax
import jax.numpy as jnp
from jax import lax
from jax.experimental import pallas as pl
from jax.experimental.pallas import tpu as pltpu
from jax.sharding import PartitionSpec as P

spacing = 1.0 / 128.0
axial_stiff = 1.0
bend_stiff = 0.25
contact_stiff = 1.0 / 16.0
time_step = 0.2
damping = 0.9
masked_far = 1.0e4
HIGH = lax.Precision.HIGH
tile_group = 32
slot_step = 4


def halos(block, axis, dim, width):
    count = lax.axis_size(axis)
    forward = [(i, i + 1) for i in range(count - 1)]
    backward = [(target, source) for source, target in forward]
    low = lax.ppermute(
        lax.slice_in_dim(block, block.shape[dim] - width, None, axis=dim), axis, forward
    )
    high = lax.ppermute(lax.slice_in_dim(block, 0, width, axis=dim), axis, backward)
    return low, high


def chain_force(padded):
    center = padded[:, :, 2:-2]
    next_one = padded[:, :, 3:-1]
    prev_one = padded[:, :, 1:-3]
    next_two = padded[:, :, 4:]
    prev_two = padded[:, :, :-4]
    axial = next_one - 2.0 * center + prev_one
    bending = next_two - 4.0 * next_one + 6.0 * center - 4.0 * prev_one + prev_two
    return axial_stiff * axial - bend_stiff * bending


def split3(v):
    hi = v.astype(jnp.bfloat16).astype(jnp.float32)
    rest = v - hi
    mid = rest.astype(jnp.bfloat16).astype(jnp.float32)
    lo = (rest - mid).astype(jnp.bfloat16).astype(jnp.float32)
    return hi, mid, lo


def stack_rows(rows):
    row = lax.broadcasted_iota(jnp.int32, (8, 128), 0)
    groups = []
    for g in range(4):
        acc = jnp.zeros((8, 128), jnp.float32)
        for r, v in enumerate(rows[8 * g:8 * g + 8]):
            acc = acc + jnp.where(row == r, jnp.broadcast_to(v, (8, 128)), 0.0)
        groups.append(acc)
    return jnp.concatenate(groups, axis=0)


def rows_of(x, near):
    lane = lax.broadcasted_iota(jnp.int32, (1, 128), 1).astype(jnp.float32)
    v = [x[0:1], x[1:2], x[2:3]]
    on = jnp.where(lane < x[3:4, 0:1], 1.0, 0.0)
    norm = v[0] * v[0] + v[1] * v[1] + v[2] * v[2]
    far = masked_far * (1.0 - on)
    one = jnp.ones((1, 128), jnp.float32)
    rows = []
    if near:
        for c in range(3):
            hi, mid, lo = split3(v[c])
            rows += [hi, mid, hi, mid, lo, hi]
        rows += [one, one, one] + list(split3(norm)) + [one, far]
        return stack_rows(rows), None
    for c in range(3):
        hi, mid, lo = split3(-2.0 * v[c])
        rows += [hi, hi, mid, mid, hi, lo]
    rows += list(split3(norm)) + [one, one, one] + [far, one]
    row = lax.broadcasted_iota(jnp.int32, (8, 128), 0)
    rq = (jnp.where(row == 0, jnp.broadcast_to(v[0], (8, 128)), 0.0)
          + jnp.where(row == 1, jnp.broadcast_to(v[1], (8, 128)), 0.0)
          + jnp.where(row == 2, jnp.broadcast_to(v[2], (8, 128)), 0.0) + jnp.where(row == 3, 1.0, 0.0))
    return stack_rows(rows), rq


def side_rows(x):
    row = lax.broadcasted_iota(jnp.int32, (8, 128), 0)
    return (jnp.where(row == 0, jnp.broadcast_to(x[0:1], (8, 128)), 0.0)
            + jnp.where(row == 1, jnp.broadcast_to(x[1:2], (8, 128)), 0.0)
            + jnp.where(row == 2, jnp.broadcast_to(x[2:3], (8, 128)), 0.0) + jnp.where(row == 3, 1.0, 0.0))


def piece_sums(rows, w_hi, w_lo, axis):
    hi, mid, lo = split3(rows)
    count = rows.shape[0]
    dims = (((1,), (axis,)), ((), ()))
    by_hi = lax.dot_general(
        jnp.concatenate([hi, mid, lo], axis=0), w_hi, dims, preferred_element_type=jnp.float32
    )
    by_lo = lax.dot_general(
        jnp.concatenate([hi, mid], axis=0), w_lo, dims, preferred_element_type=jnp.float32
    )
    return (by_hi[0:count] + by_hi[count:2 * count] + by_hi[2 * count:]) + (
        by_lo[0:count] + by_lo[count:]
    )


def tile_two(m_a, m_b, s_a, s_b, rd_a, rd_b, rq_a, rq_b):
    zero = jnp.zeros(m_a.shape, jnp.float32)
    mine = jnp.concatenate(
        [jnp.concatenate([m_a, zero], axis=1), jnp.concatenate([zero, m_b], axis=1)], axis=0
    )
    dist = lax.dot_general(
        jnp.concatenate([rd_a, rd_b], axis=0), mine, (((0,), (0,)), ((), ())),
        preferred_element_type=jnp.float32,
    )
    w = jnp.exp(-dist)
    zero = jnp.zeros((8, 128), jnp.float32)
    side = jnp.concatenate(
        [jnp.concatenate([s_a, zero], axis=1), jnp.concatenate([zero, s_b], axis=1)], axis=0
    )
    w_hi = w.astype(jnp.bfloat16).astype(jnp.float32)
    w_lo = (w - w_hi).astype(jnp.bfloat16).astype(jnp.float32)
    f1 = piece_sums(jnp.concatenate([rq_a, rq_b], axis=0), w_hi, w_lo, 0)
    f2 = piece_sums(side, w_hi, w_lo, 1)
    f1 = f1 * contact_stiff
    f2 = f2 * contact_stiff
    out = []
    for m, rq, g1, g2 in ((s_a, rq_a, f1[0:8, 0:128], f2[0:8]), (s_b, rq_b, f1[8:16, 128:256], f2[8:16])):
        out.append((m * g1[3:4, :] - g1, (rq * g2[3:4, :] - g2)[0:3, :]))
    return out


def peer_row(slot, rows, cap):
    return (slot // cap) * rows * cap + slot % cap


def pack_kernel(anc_ref, seg_ref, mine_ref, their_ref, cnt_ref, disp_ref, rows_ref, lent_ref):
    peers = cnt_ref.shape[0]
    cap = mine_ref.shape[0] // peers
    blocks = rows_ref.shape[0]
    row = lax.broadcasted_iota(jnp.int32, (4, 128), 0)
    lane = lax.broadcasted_iota(jnp.int32, (4, 128), 1)
    height = lax.broadcasted_iota(jnp.int32, (1, 128), 1).astype(jnp.float32) * spacing

    def block(g, carry):
        for k in range(slot_step):
            b = g * slot_step + k
            x = jnp.where((row == 3) & (lane == 0), seg_ref[b].astype(jnp.float32), 0.0)
            for c in range(3):
                v = disp_ref[c, pl.ds(b, 1), :] + anc_ref[c * blocks + b]
                if c == 2:
                    v = v + height
                x = jnp.where(row == c, jnp.broadcast_to(v, (4, 128)), x)
            rows_ref[b] = x
        return carry

    lax.fori_loop(0, blocks // slot_step, block, 0)

    lent_ref[...] = jnp.zeros(lent_ref.shape, lent_ref.dtype)

    def peer(d, carry):
        live = cnt_ref[d]

        sent = jnp.clip(live, 1, cap)

        def step(g, carry):
            for k in range(slot_step):
                c = jnp.minimum(g * slot_step + k, sent - 1)
                s = d * cap + c
                x = rows_ref[jnp.clip(mine_ref[s], 0, blocks - 1)]
                x = jnp.where((row == 3) & (lane == 1), their_ref[s].astype(jnp.float32), x)
                x = jnp.where((row == 3) & (lane == 2), live.astype(jnp.float32), x)
                lent_ref[pl.ds(d * 4 * cap + c, 4, stride=cap), :] = x
            return carry

        return lax.fori_loop(0, (sent + slot_step - 1) // slot_step, step, carry)

    lax.fori_loop(0, peers, peer, 0)


def pair_kernel(cnt_ref, req_ref, m_ref, rem_ref, low_ref, high_ref, f1_ref, f2_ref, lb_ref, ls_ref):
    f1_ref[...] = jnp.zeros(f1_ref.shape, f1_ref.dtype)
    f2_ref[...] = jnp.zeros(f2_ref.shape, f2_ref.dtype)
    peers = cnt_ref.shape[0]
    cap = req_ref.shape[0] // peers
    blocks = m_ref.shape[0]

    def listed(d, n):
        live = jnp.clip(cnt_ref[d], 0, cap)

        def held(g, n):
            for k in range(slot_step):
                c = jnp.minimum(g * slot_step + k, cap - 1)
                lb_ref[n + k] = jnp.clip(req_ref[d * cap + c], 0, blocks - 1)
                ls_ref[n + k] = d * cap + c
            return n + jnp.minimum(slot_step, live - g * slot_step)

        return lax.fori_loop(0, (live + slot_step - 1) // slot_step, held, n)

    total = lax.fori_loop(0, peers, listed, 0)
    last = jnp.maximum(total - 1, 0)

    def group(g, carry):
        done = []
        for k in range(0, tile_group, 2):
            picked = []
            for t in (g * tile_group + k, g * tile_group + k + 1):
                at = jnp.minimum(t, last)
                picked.append((t, lb_ref[at], ls_ref[at]))
            (t_a, b_a, s_a), (t_b, b_b, s_b) = picked
            rd_a, rq_a = rows_of(rem_ref[pl.ds(peer_row(s_a, 4, cap), 4, stride=cap), :], False)
            rd_b, rq_b = rows_of(rem_ref[pl.ds(peer_row(s_b, 4, cap), 4, stride=cap), :], False)
            x_a = m_ref[b_a]
            x_b = m_ref[b_b]
            pair = tile_two(
                rows_of(x_a, True)[0], rows_of(x_b, True)[0], side_rows(x_a), side_rows(x_b),
                rd_a, rd_b, rq_a, rq_b,
            )
            for (t, b, slot), (on_first, on_second) in zip(picked, pair):
                done.append((b, slot, jnp.where(t < total, on_first, 0.0), on_second))
        for b, slot, on_first, on_second in done:
            f1_ref[b] = f1_ref[b] + on_first
            f2_ref[pl.ds(peer_row(slot, 3, cap), 3, stride=cap), :] = on_second
        return carry

    lax.fori_loop(0, (total + tile_group - 1) // tile_group, group, 0)


def back_kernel(cap, mine_ref, cnt_ref, f1_ref, ret_ref, vel_ref, disp_ref, beam_ref, nv_ref, nd_ref, acc_ref):
    acc_ref[...] = f1_ref[...]
    blocks = vel_ref.shape[1]

    def peer(d, carry):
        live = jnp.clip(cnt_ref[d], 0, cap)

        def step(g, carry):
            for k in range(slot_step):
                c = g * slot_step + k
                at = jnp.minimum(c, live - 1)
                b = jnp.clip(mine_ref[d * cap + at], 0, blocks - 1)
                start = pl.multiple_of(b * 8, 8)
                got = ret_ref[pl.ds(d * 3 * cap + at, 3, stride=cap), :]
                acc_ref[pl.ds(start, 3), :] = acc_ref[pl.ds(start, 3), :] + jnp.where(c < live, got, 0.0)
            return carry

        return lax.fori_loop(0, (live + slot_step - 1) // slot_step, step, carry)

    lax.fori_loop(0, cnt_ref.shape[0], peer, 0)
    for c in range(3):
        contact = acc_ref[pl.ds(c, blocks, stride=8), :]
        new_velocity = damping * vel_ref[c] + time_step * (beam_ref[c] + contact)
        nv_ref[c] = new_velocity
        nd_ref[c] = disp_ref[c] + time_step * new_velocity


def local(displacement, velocity, anchors, seg_live, pair_blocks, pair_count):
    seg_len = displacement.shape[2]
    fibre_count = displacement.shape[1]
    per_fibre = seg_len // 128
    block_total = fibre_count * per_fibre
    peer_total = pair_blocks.shape[2]
    slot_cap = pair_blocks.shape[3]
    slot_total = peer_total * slot_cap
    halo_low, halo_high = halos(displacement, "len", 2, 2)
    beam = chain_force(jnp.concatenate([halo_low, displacement, halo_high], axis=2))

    mine_flat = pair_blocks[0, 0, :, :, 0].reshape(slot_total)
    their_flat = pair_blocks[0, 0, :, :, 1].reshape(slot_total)
    smem = pl.BlockSpec(memory_space=pltpu.SMEM)
    vmem = pl.BlockSpec(memory_space=pltpu.VMEM)
    my_rows, lent = pl.pallas_call(
        pack_kernel,
        out_shape=(
            jax.ShapeDtypeStruct((block_total, 4, 128), jnp.float32),
            jax.ShapeDtypeStruct((peer_total * 4 * slot_cap, 128), jnp.float32),
        ),
        in_specs=[smem, smem, smem, smem, smem, vmem],
        out_specs=(vmem, vmem),
    )(anchors.reshape(3 * block_total), seg_live.reshape(block_total), mine_flat, their_flat,
      pair_count[0, 0], displacement)
    remote = lax.all_to_all(
        lent.reshape(peer_total, 4, slot_cap, 128), ("xa", "xb"), split_axis=0, concat_axis=0, tiled=True
    )
    req_ids = remote[:, 3, :, 1].astype(jnp.int32).reshape(slot_total)
    live_from = remote[:, 3, 0, 2].astype(jnp.int32)

    f1, f2 = pl.pallas_call(
        pair_kernel,
        out_shape=(
            jax.ShapeDtypeStruct((block_total, 8, 128), jnp.float32),
            jax.ShapeDtypeStruct((peer_total * 3 * slot_cap, 128), jnp.float32),
        ),
        in_specs=[smem, smem, vmem, vmem, vmem, vmem],
        out_specs=(vmem, vmem),
        scratch_shapes=[pltpu.SMEM((slot_total + slot_step,), jnp.int32)] * 2,
    )(live_from, req_ids, my_rows, remote.reshape(peer_total * 4 * slot_cap, 128), halo_low, halo_high)

    returned = lax.all_to_all(
        f2.reshape(peer_total, 3, slot_cap, 128), ("xa", "xb"), split_axis=0, concat_axis=0, tiled=True
    )
    new_velocity, new_displacement = pl.pallas_call(
        functools.partial(back_kernel, slot_cap),
        out_shape=(
            jax.ShapeDtypeStruct(velocity.shape, jnp.float32),
            jax.ShapeDtypeStruct(displacement.shape, jnp.float32),
        ),
        in_specs=[smem, smem, vmem, vmem, vmem, vmem, vmem],
        out_specs=(vmem, vmem),
        scratch_shapes=[pltpu.VMEM((block_total * 8, 128), jnp.float32)],
    )(mine_flat, pair_count[0, 0], f1.reshape(block_total * 8, 128), returned.reshape(peer_total * 3 * slot_cap, 128),
      velocity, displacement, beam)
    return (new_velocity, new_displacement)


def solution(mesh):
    in_specs = (
        P(None, ("xa", "xb"), "len"),
        P(None, ("xa", "xb"), "len"),
        P(None, ("xa", "xb")),
        P(("xa", "xb"), "len"),
        P("len", ("xa", "xb"), None, None, None),
        P("len", ("xa", "xb"), None),
    )
    out_specs = (P(None, ("xa", "xb"), "len"), P(None, ("xa", "xb"), "len"))
    return jax.shard_map(local, mesh=mesh, in_specs=in_specs, out_specs=out_specs, check_vma=False)
```

```python
import functools

import jax
import jax.numpy as jnp
from jax import lax
from jax.experimental import pallas as pl
from jax.experimental.pallas import tpu as pltpu
from jax.sharding import PartitionSpec as P

spacing = 1.0 / 128.0
axial_stiff = 1.0
bend_stiff = 0.25
contact_stiff = 1.0 / 16.0
time_step = 0.2
damping = 0.9
masked_far = 1.0e4
HIGH = lax.Precision.HIGH
tile_group = 32
slot_step = 8


def halos(block, axis, dim, width):
    count = lax.axis_size(axis)
    forward = [(i, i + 1) for i in range(count - 1)]
    backward = [(target, source) for source, target in forward]
    low = lax.ppermute(
        lax.slice_in_dim(block, block.shape[dim] - width, None, axis=dim), axis, forward
    )
    high = lax.ppermute(lax.slice_in_dim(block, 0, width, axis=dim), axis, backward)
    return low, high


def chain_force(padded):
    center = padded[:, :, 2:-2]
    next_one = padded[:, :, 3:-1]
    prev_one = padded[:, :, 1:-3]
    next_two = padded[:, :, 4:]
    prev_two = padded[:, :, :-4]
    axial = next_one - 2.0 * center + prev_one
    bending = next_two - 4.0 * next_one + 6.0 * center - 4.0 * prev_one + prev_two
    return axial_stiff * axial - bend_stiff * bending


def split3(v):
    hi = v.astype(jnp.bfloat16).astype(jnp.float32)
    rest = v - hi
    mid = rest.astype(jnp.bfloat16).astype(jnp.float32)
    lo = (rest - mid).astype(jnp.bfloat16).astype(jnp.float32)
    return hi, mid, lo


def stack_rows(rows):
    row = lax.broadcasted_iota(jnp.int32, (8, 128), 0)
    groups = []
    for g in range(4):
        acc = jnp.zeros((8, 128), jnp.float32)
        for r, v in enumerate(rows[8 * g:8 * g + 8]):
            acc = acc + jnp.where(row == r, jnp.broadcast_to(v, (8, 128)), 0.0)
        groups.append(acc)
    return jnp.concatenate(groups, axis=0)


def rows_of(x, near):
    lane = lax.broadcasted_iota(jnp.int32, (1, 128), 1).astype(jnp.float32)
    v = [x[0:1], x[1:2], x[2:3]]
    on = jnp.where(lane < x[3:4, 0:1], 1.0, 0.0)
    norm = v[0] * v[0] + v[1] * v[1] + v[2] * v[2]
    far = masked_far * (1.0 - on)
    one = jnp.ones((1, 128), jnp.float32)
    rows = []
    if near:
        for c in range(3):
            hi, mid, lo = split3(v[c])
            rows += [hi, mid, hi, mid, lo, hi]
        rows += [one, one, one] + list(split3(norm)) + [one, far]
        return stack_rows(rows), None
    for c in range(3):
        hi, mid, lo = split3(-2.0 * v[c])
        rows += [hi, hi, mid, mid, hi, lo]
    rows += list(split3(norm)) + [one, one, one] + [far, one]
    row = lax.broadcasted_iota(jnp.int32, (8, 128), 0)
    rq = (jnp.where(row == 0, jnp.broadcast_to(v[0], (8, 128)), 0.0)
          + jnp.where(row == 1, jnp.broadcast_to(v[1], (8, 128)), 0.0)
          + jnp.where(row == 2, jnp.broadcast_to(v[2], (8, 128)), 0.0) + jnp.where(row == 3, 1.0, 0.0))
    return stack_rows(rows), rq


def side_rows(x):
    row = lax.broadcasted_iota(jnp.int32, (8, 128), 0)
    return (jnp.where(row == 0, jnp.broadcast_to(x[0:1], (8, 128)), 0.0)
            + jnp.where(row == 1, jnp.broadcast_to(x[1:2], (8, 128)), 0.0)
            + jnp.where(row == 2, jnp.broadcast_to(x[2:3], (8, 128)), 0.0) + jnp.where(row == 3, 1.0, 0.0))


def piece_sums(rows, w_hi, w_lo, axis):
    hi, mid, lo = split3(rows)
    count = rows.shape[0]
    dims = (((1,), (axis,)), ((), ()))
    by_hi = lax.dot_general(
        jnp.concatenate([hi, mid, lo], axis=0), w_hi, dims, preferred_element_type=jnp.float32
    )
    by_lo = lax.dot_general(
        jnp.concatenate([hi, mid], axis=0), w_lo, dims, preferred_element_type=jnp.float32
    )
    return (by_hi[0:count] + by_hi[count:2 * count] + by_hi[2 * count:]) + (
        by_lo[0:count] + by_lo[count:]
    )


def tile_two(m_a, m_b, s_a, s_b, rd_a, rd_b, rq_a, rq_b):
    zero = jnp.zeros(m_a.shape, jnp.float32)
    mine = jnp.concatenate(
        [jnp.concatenate([m_a, zero], axis=1), jnp.concatenate([zero, m_b], axis=1)], axis=0
    )
    dist = lax.dot_general(
        jnp.concatenate([rd_a, rd_b], axis=0), mine, (((0,), (0,)), ((), ())),
        preferred_element_type=jnp.float32,
    )
    w = jnp.exp(-dist)
    zero = jnp.zeros((8, 128), jnp.float32)
    side = jnp.concatenate(
        [jnp.concatenate([s_a, zero], axis=1), jnp.concatenate([zero, s_b], axis=1)], axis=0
    )
    w_hi = w.astype(jnp.bfloat16).astype(jnp.float32)
    w_lo = (w - w_hi).astype(jnp.bfloat16).astype(jnp.float32)
    f1 = piece_sums(jnp.concatenate([rq_a, rq_b], axis=0), w_hi, w_lo, 0)
    f2 = piece_sums(side, w_hi, w_lo, 1)
    f1 = f1 * contact_stiff
    f2 = f2 * contact_stiff
    out = []
    for m, rq, g1, g2 in ((s_a, rq_a, f1[0:8, 0:128], f2[0:8]), (s_b, rq_b, f1[8:16, 128:256], f2[8:16])):
        out.append((m * g1[3:4, :] - g1, (rq * g2[3:4, :] - g2)[0:3, :]))
    return out


def peer_row(slot, rows, cap):
    return (slot // cap) * rows * cap + slot % cap


def pack_kernel(anc_ref, seg_ref, mine_ref, their_ref, cnt_ref, disp_ref, rows_ref, lent_ref):
    peers = cnt_ref.shape[0]
    cap = mine_ref.shape[0] // peers
    blocks = rows_ref.shape[0]
    row = lax.broadcasted_iota(jnp.int32, (4, 128), 0)
    lane = lax.broadcasted_iota(jnp.int32, (4, 128), 1)
    height = lax.broadcasted_iota(jnp.int32, (1, 128), 1).astype(jnp.float32) * spacing

    def block(g, carry):
        for k in range(slot_step):
            b = g * slot_step + k
            x = jnp.where((row == 3) & (lane == 0), seg_ref[b].astype(jnp.float32), 0.0)
            for c in range(3):
                v = disp_ref[c, pl.ds(b, 1), :] + anc_ref[c * blocks + b]
                if c == 2:
                    v = v + height
                x = jnp.where(row == c, jnp.broadcast_to(v, (4, 128)), x)
            rows_ref[b] = x
        return carry

    lax.fori_loop(0, blocks // slot_step, block, 0)

    lent_ref[...] = jnp.zeros(lent_ref.shape, lent_ref.dtype)

    def peer(d, carry):
        live = cnt_ref[d]

        sent = jnp.clip(live, 1, cap)

        def step(g, carry):
            for k in range(slot_step):
                c = jnp.minimum(g * slot_step + k, sent - 1)
                s = d * cap + c
                x = rows_ref[jnp.clip(mine_ref[s], 0, blocks - 1)]
                x = jnp.where((row == 3) & (lane == 1), their_ref[s].astype(jnp.float32), x)
                x = jnp.where((row == 3) & (lane == 2), live.astype(jnp.float32), x)
                lent_ref[pl.ds(d * 4 * cap + c, 4, stride=cap), :] = x
            return carry

        return lax.fori_loop(0, (sent + slot_step - 1) // slot_step, step, carry)

    lax.fori_loop(0, peers, peer, 0)


def pair_kernel(cnt_ref, req_ref, m_ref, rem_ref, low_ref, high_ref, f1_ref, f2_ref, lb_ref, ls_ref):
    f1_ref[...] = jnp.zeros(f1_ref.shape, f1_ref.dtype)
    f2_ref[...] = jnp.zeros(f2_ref.shape, f2_ref.dtype)
    peers = cnt_ref.shape[0]
    cap = req_ref.shape[0] // peers
    blocks = m_ref.shape[0]

    def listed(d, n):
        live = jnp.clip(cnt_ref[d], 0, cap)

        def held(g, n):
            for k in range(slot_step):
                c = jnp.minimum(g * slot_step + k, cap - 1)
                lb_ref[n + k] = jnp.clip(req_ref[d * cap + c], 0, blocks - 1)
                ls_ref[n + k] = d * cap + c
            return n + jnp.minimum(slot_step, live - g * slot_step)

        return lax.fori_loop(0, (live + slot_step - 1) // slot_step, held, n)

    total = lax.fori_loop(0, peers, listed, 0)
    last = jnp.maximum(total - 1, 0)

    def group(g, carry):
        done = []
        for k in range(0, tile_group, 2):
            picked = []
            for t in (g * tile_group + k, g * tile_group + k + 1):
                at = jnp.minimum(t, last)
                picked.append((t, lb_ref[at], ls_ref[at]))
            (t_a, b_a, s_a), (t_b, b_b, s_b) = picked
            rd_a, rq_a = rows_of(rem_ref[pl.ds(peer_row(s_a, 4, cap), 4, stride=cap), :], False)
            rd_b, rq_b = rows_of(rem_ref[pl.ds(peer_row(s_b, 4, cap), 4, stride=cap), :], False)
            x_a = m_ref[b_a]
            x_b = m_ref[b_b]
            pair = tile_two(
                rows_of(x_a, True)[0], rows_of(x_b, True)[0], side_rows(x_a), side_rows(x_b),
                rd_a, rd_b, rq_a, rq_b,
            )
            for (t, b, slot), (on_first, on_second) in zip(picked, pair):
                done.append((b, slot, jnp.where(t < total, on_first, 0.0), on_second))
        for b, slot, on_first, on_second in done:
            f1_ref[b] = f1_ref[b] + on_first
            f2_ref[pl.ds(peer_row(slot, 3, cap), 3, stride=cap), :] = on_second
        return carry

    lax.fori_loop(0, (total + tile_group - 1) // tile_group, group, 0)


def back_kernel(cap, mine_ref, cnt_ref, f1_ref, ret_ref, vel_ref, disp_ref, beam_ref, nv_ref, nd_ref, acc_ref):
    acc_ref[...] = f1_ref[...]
    blocks = vel_ref.shape[1]

    def peer(d, carry):
        live = jnp.clip(cnt_ref[d], 0, cap)

        def step(g, carry):
            for k in range(slot_step):
                c = g * slot_step + k
                at = jnp.minimum(c, live - 1)
                b = jnp.clip(mine_ref[d * cap + at], 0, blocks - 1)
                start = pl.multiple_of(b * 8, 8)
                got = ret_ref[pl.ds(d * 3 * cap + at, 3, stride=cap), :]
                acc_ref[pl.ds(start, 3), :] = acc_ref[pl.ds(start, 3), :] + jnp.where(c < live, got, 0.0)
            return carry

        return lax.fori_loop(0, (live + slot_step - 1) // slot_step, step, carry)

    lax.fori_loop(0, cnt_ref.shape[0], peer, 0)
    for c in range(3):
        contact = acc_ref[pl.ds(c, blocks, stride=8), :]
        new_velocity = damping * vel_ref[c] + time_step * (beam_ref[c] + contact)
        nv_ref[c] = new_velocity
        nd_ref[c] = disp_ref[c] + time_step * new_velocity


def local(displacement, velocity, anchors, seg_live, pair_blocks, pair_count):
    seg_len = displacement.shape[2]
    fibre_count = displacement.shape[1]
    per_fibre = seg_len // 128
    block_total = fibre_count * per_fibre
    peer_total = pair_blocks.shape[2]
    slot_cap = pair_blocks.shape[3]
    slot_total = peer_total * slot_cap
    halo_low, halo_high = halos(displacement, "len", 2, 2)
    beam = chain_force(jnp.concatenate([halo_low, displacement, halo_high], axis=2))

    mine_flat = pair_blocks[0, 0, :, :, 0].reshape(slot_total)
    their_flat = pair_blocks[0, 0, :, :, 1].reshape(slot_total)
    smem = pl.BlockSpec(memory_space=pltpu.SMEM)
    vmem = pl.BlockSpec(memory_space=pltpu.VMEM)
    my_rows, lent = pl.pallas_call(
        pack_kernel,
        out_shape=(
            jax.ShapeDtypeStruct((block_total, 4, 128), jnp.float32),
            jax.ShapeDtypeStruct((peer_total * 4 * slot_cap, 128), jnp.float32),
        ),
        in_specs=[smem, smem, smem, smem, smem, vmem],
        out_specs=(vmem, vmem),
    )(anchors.reshape(3 * block_total), seg_live.reshape(block_total), mine_flat, their_flat,
      pair_count[0, 0], displacement)
    remote = lax.all_to_all(
        lent.reshape(peer_total, 4, slot_cap, 128), ("xa", "xb"), split_axis=0, concat_axis=0, tiled=True
    )
    req_ids = remote[:, 3, :, 1].astype(jnp.int32).reshape(slot_total)
    live_from = remote[:, 3, 0, 2].astype(jnp.int32)

    f1, f2 = pl.pallas_call(
        pair_kernel,
        out_shape=(
            jax.ShapeDtypeStruct((block_total, 8, 128), jnp.float32),
            jax.ShapeDtypeStruct((peer_total * 3 * slot_cap, 128), jnp.float32),
        ),
        in_specs=[smem, smem, vmem, vmem, vmem, vmem],
        out_specs=(vmem, vmem),
        scratch_shapes=[pltpu.SMEM((slot_total + slot_step,), jnp.int32)] * 2,
    )(live_from, req_ids, my_rows, remote.reshape(peer_total * 4 * slot_cap, 128), halo_low, halo_high)

    returned = lax.all_to_all(
        f2.reshape(peer_total, 3, slot_cap, 128), ("xa", "xb"), split_axis=0, concat_axis=0, tiled=True
    )
    new_velocity, new_displacement = pl.pallas_call(
        functools.partial(back_kernel, slot_cap),
        out_shape=(
            jax.ShapeDtypeStruct(velocity.shape, jnp.float32),
            jax.ShapeDtypeStruct(displacement.shape, jnp.float32),
        ),
        in_specs=[smem, smem, vmem, vmem, vmem, vmem, vmem],
        out_specs=(vmem, vmem),
        scratch_shapes=[pltpu.VMEM((block_total * 8, 128), jnp.float32)],
    )(mine_flat, pair_count[0, 0], f1.reshape(block_total * 8, 128), returned.reshape(peer_total * 3 * slot_cap, 128),
      velocity, displacement, beam)
    return (new_velocity, new_displacement)


def solution(mesh):
    in_specs = (
        P(None, ("xa", "xb"), "len"),
        P(None, ("xa", "xb"), "len"),
        P(None, ("xa", "xb")),
        P(("xa", "xb"), "len"),
        P("len", ("xa", "xb"), None, None, None),
        P("len", ("xa", "xb"), None),
    )
    out_specs = (P(None, ("xa", "xb"), "len"), P(None, ("xa", "xb"), "len"))
    return jax.shard_map(local, mesh=mesh, in_specs=in_specs, out_specs=out_specs, check_vma=False)
```

```python
import functools

import jax
import jax.numpy as jnp
from jax import lax
from jax.experimental import pallas as pl
from jax.experimental.pallas import tpu as pltpu
from jax.sharding import PartitionSpec as P

spacing = 1.0 / 128.0
axial_stiff = 1.0
bend_stiff = 0.25
contact_stiff = 1.0 / 16.0
time_step = 0.2
damping = 0.9
masked_far = 1.0e4
HIGH = lax.Precision.HIGH
tile_group = 64
slot_step = 8


def halos(block, axis, dim, width):
    count = lax.axis_size(axis)
    forward = [(i, i + 1) for i in range(count - 1)]
    backward = [(target, source) for source, target in forward]
    low = lax.ppermute(
        lax.slice_in_dim(block, block.shape[dim] - width, None, axis=dim), axis, forward
    )
    high = lax.ppermute(lax.slice_in_dim(block, 0, width, axis=dim), axis, backward)
    return low, high


def chain_force(padded):
    center = padded[:, :, 2:-2]
    next_one = padded[:, :, 3:-1]
    prev_one = padded[:, :, 1:-3]
    next_two = padded[:, :, 4:]
    prev_two = padded[:, :, :-4]
    axial = next_one - 2.0 * center + prev_one
    bending = next_two - 4.0 * next_one + 6.0 * center - 4.0 * prev_one + prev_two
    return axial_stiff * axial - bend_stiff * bending


def split3(v):
    hi = v.astype(jnp.bfloat16).astype(jnp.float32)
    rest = v - hi
    mid = rest.astype(jnp.bfloat16).astype(jnp.float32)
    lo = (rest - mid).astype(jnp.bfloat16).astype(jnp.float32)
    return hi, mid, lo


def stack_rows(rows):
    row = lax.broadcasted_iota(jnp.int32, (8, 128), 0)
    groups = []
    for g in range(4):
        acc = jnp.zeros((8, 128), jnp.float32)
        for r, v in enumerate(rows[8 * g:8 * g + 8]):
            acc = acc + jnp.where(row == r, jnp.broadcast_to(v, (8, 128)), 0.0)
        groups.append(acc)
    return jnp.concatenate(groups, axis=0)


def rows_of(x, near):
    lane = lax.broadcasted_iota(jnp.int32, (1, 128), 1).astype(jnp.float32)
    v = [x[0:1], x[1:2], x[2:3]]
    on = jnp.where(lane < x[3:4, 0:1], 1.0, 0.0)
    norm = v[0] * v[0] + v[1] * v[1] + v[2] * v[2]
    far = masked_far * (1.0 - on)
    one = jnp.ones((1, 128), jnp.float32)
    rows = []
    if near:
        for c in range(3):
            hi, mid, lo = split3(v[c])
            rows += [hi, mid, hi, mid, lo, hi]
        rows += [one, one, one] + list(split3(norm)) + [one, far]
        return stack_rows(rows), None
    for c in range(3):
        hi, mid, lo = split3(-2.0 * v[c])
        rows += [hi, hi, mid, mid, hi, lo]
    rows += list(split3(norm)) + [one, one, one] + [far, one]
    row = lax.broadcasted_iota(jnp.int32, (8, 128), 0)
    rq = (jnp.where(row == 0, jnp.broadcast_to(v[0], (8, 128)), 0.0)
          + jnp.where(row == 1, jnp.broadcast_to(v[1], (8, 128)), 0.0)
          + jnp.where(row == 2, jnp.broadcast_to(v[2], (8, 128)), 0.0) + jnp.where(row == 3, 1.0, 0.0))
    return stack_rows(rows), rq


def side_rows(x):
    row = lax.broadcasted_iota(jnp.int32, (8, 128), 0)
    return (jnp.where(row == 0, jnp.broadcast_to(x[0:1], (8, 128)), 0.0)
            + jnp.where(row == 1, jnp.broadcast_to(x[1:2], (8, 128)), 0.0)
            + jnp.where(row == 2, jnp.broadcast_to(x[2:3], (8, 128)), 0.0) + jnp.where(row == 3, 1.0, 0.0))


def piece_sums(rows, w_hi, w_lo, axis):
    hi, mid, lo = split3(rows)
    count = rows.shape[0]
    dims = (((1,), (axis,)), ((), ()))
    by_hi = lax.dot_general(
        jnp.concatenate([hi, mid, lo], axis=0), w_hi, dims, preferred_element_type=jnp.float32
    )
    by_lo = lax.dot_general(
        jnp.concatenate([hi, mid], axis=0), w_lo, dims, preferred_element_type=jnp.float32
    )
    return (by_hi[0:count] + by_hi[count:2 * count] + by_hi[2 * count:]) + (
        by_lo[0:count] + by_lo[count:]
    )


def tile_two(m_a, m_b, s_a, s_b, rd_a, rd_b, rq_a, rq_b):
    zero = jnp.zeros(m_a.shape, jnp.float32)
    mine = jnp.concatenate(
        [jnp.concatenate([m_a, zero], axis=1), jnp.concatenate([zero, m_b], axis=1)], axis=0
    )
    dist = lax.dot_general(
        jnp.concatenate([rd_a, rd_b], axis=0), mine, (((0,), (0,)), ((), ())),
        preferred_element_type=jnp.float32,
    )
    w = jnp.exp(-dist)
    zero = jnp.zeros((8, 128), jnp.float32)
    side = jnp.concatenate(
        [jnp.concatenate([s_a, zero], axis=1), jnp.concatenate([zero, s_b], axis=1)], axis=0
    )
    w_hi = w.astype(jnp.bfloat16).astype(jnp.float32)
    w_lo = (w - w_hi).astype(jnp.bfloat16).astype(jnp.float32)
    f1 = piece_sums(jnp.concatenate([rq_a, rq_b], axis=0), w_hi, w_lo, 0)
    f2 = piece_sums(side, w_hi, w_lo, 1)
    f1 = f1 * contact_stiff
    f2 = f2 * contact_stiff
    out = []
    for m, rq, g1, g2 in ((s_a, rq_a, f1[0:8, 0:128], f2[0:8]), (s_b, rq_b, f1[8:16, 128:256], f2[8:16])):
        out.append((m * g1[3:4, :] - g1, (rq * g2[3:4, :] - g2)[0:3, :]))
    return out


def peer_row(slot, rows, cap):
    return (slot // cap) * rows * cap + slot % cap


def pack_kernel(anc_ref, seg_ref, mine_ref, their_ref, cnt_ref, disp_ref, rows_ref, lent_ref):
    peers = cnt_ref.shape[0]
    cap = mine_ref.shape[0] // peers
    blocks = rows_ref.shape[0]
    row = lax.broadcasted_iota(jnp.int32, (4, 128), 0)
    lane = lax.broadcasted_iota(jnp.int32, (4, 128), 1)
    height = lax.broadcasted_iota(jnp.int32, (1, 128), 1).astype(jnp.float32) * spacing

    def block(g, carry):
        for k in range(slot_step):
            b = g * slot_step + k
            x = jnp.where((row == 3) & (lane == 0), seg_ref[b].astype(jnp.float32), 0.0)
            for c in range(3):
                v = disp_ref[c, pl.ds(b, 1), :] + anc_ref[c * blocks + b]
                if c == 2:
                    v = v + height
                x = jnp.where(row == c, jnp.broadcast_to(v, (4, 128)), x)
            rows_ref[b] = x
        return carry

    lax.fori_loop(0, blocks // slot_step, block, 0)

    lent_ref[...] = jnp.zeros(lent_ref.shape, lent_ref.dtype)

    def peer(d, carry):
        live = cnt_ref[d]

        sent = jnp.clip(live, 1, cap)

        def step(g, carry):
            for k in range(slot_step):
                c = jnp.minimum(g * slot_step + k, sent - 1)
                s = d * cap + c
                x = rows_ref[jnp.clip(mine_ref[s], 0, blocks - 1)]
                x = jnp.where((row == 3) & (lane == 1), their_ref[s].astype(jnp.float32), x)
                x = jnp.where((row == 3) & (lane == 2), live.astype(jnp.float32), x)
                lent_ref[pl.ds(d * 4 * cap + c, 4, stride=cap), :] = x
            return carry

        return lax.fori_loop(0, (sent + slot_step - 1) // slot_step, step, carry)

    lax.fori_loop(0, peers, peer, 0)


def pair_kernel(cnt_ref, req_ref, m_ref, rem_ref, low_ref, high_ref, f1_ref, f2_ref, lb_ref, ls_ref):
    f1_ref[...] = jnp.zeros(f1_ref.shape, f1_ref.dtype)
    f2_ref[...] = jnp.zeros(f2_ref.shape, f2_ref.dtype)
    peers = cnt_ref.shape[0]
    cap = req_ref.shape[0] // peers
    blocks = m_ref.shape[0]

    def listed(d, n):
        live = jnp.clip(cnt_ref[d], 0, cap)

        def held(g, n):
            for k in range(slot_step):
                c = jnp.minimum(g * slot_step + k, cap - 1)
                lb_ref[n + k] = jnp.clip(req_ref[d * cap + c], 0, blocks - 1)
                ls_ref[n + k] = d * cap + c
            return n + jnp.minimum(slot_step, live - g * slot_step)

        return lax.fori_loop(0, (live + slot_step - 1) // slot_step, held, n)

    total = lax.fori_loop(0, peers, listed, 0)
    last = jnp.maximum(total - 1, 0)

    def group(g, carry):
        done = []
        for k in range(0, tile_group, 2):
            picked = []
            for t in (g * tile_group + k, g * tile_group + k + 1):
                at = jnp.minimum(t, last)
                picked.append((t, lb_ref[at], ls_ref[at]))
            (t_a, b_a, s_a), (t_b, b_b, s_b) = picked
            rd_a, rq_a = rows_of(rem_ref[pl.ds(peer_row(s_a, 4, cap), 4, stride=cap), :], False)
            rd_b, rq_b = rows_of(rem_ref[pl.ds(peer_row(s_b, 4, cap), 4, stride=cap), :], False)
            x_a = m_ref[b_a]
            x_b = m_ref[b_b]
            pair = tile_two(
                rows_of(x_a, True)[0], rows_of(x_b, True)[0], side_rows(x_a), side_rows(x_b),
                rd_a, rd_b, rq_a, rq_b,
            )
            for (t, b, slot), (on_first, on_second) in zip(picked, pair):
                done.append((b, slot, jnp.where(t < total, on_first, 0.0), on_second))
        for b, slot, on_first, on_second in done:
            f1_ref[b] = f1_ref[b] + on_first
            f2_ref[pl.ds(peer_row(slot, 3, cap), 3, stride=cap), :] = on_second
        return carry

    lax.fori_loop(0, (total + tile_group - 1) // tile_group, group, 0)


def back_kernel(cap, mine_ref, cnt_ref, f1_ref, ret_ref, vel_ref, disp_ref, beam_ref, nv_ref, nd_ref, acc_ref):
    acc_ref[...] = f1_ref[...]
    blocks = vel_ref.shape[1]

    def peer(d, carry):
        live = jnp.clip(cnt_ref[d], 0, cap)

        def step(g, carry):
            for k in range(slot_step):
                c = g * slot_step + k
                at = jnp.minimum(c, live - 1)
                b = jnp.clip(mine_ref[d * cap + at], 0, blocks - 1)
                start = pl.multiple_of(b * 8, 8)
                got = ret_ref[pl.ds(d * 3 * cap + at, 3, stride=cap), :]
                acc_ref[pl.ds(start, 3), :] = acc_ref[pl.ds(start, 3), :] + jnp.where(c < live, got, 0.0)
            return carry

        return lax.fori_loop(0, (live + slot_step - 1) // slot_step, step, carry)

    lax.fori_loop(0, cnt_ref.shape[0], peer, 0)
    for c in range(3):
        contact = acc_ref[pl.ds(c, blocks, stride=8), :]
        new_velocity = damping * vel_ref[c] + time_step * (beam_ref[c] + contact)
        nv_ref[c] = new_velocity
        nd_ref[c] = disp_ref[c] + time_step * new_velocity


def local(displacement, velocity, anchors, seg_live, pair_blocks, pair_count):
    seg_len = displacement.shape[2]
    fibre_count = displacement.shape[1]
    per_fibre = seg_len // 128
    block_total = fibre_count * per_fibre
    peer_total = pair_blocks.shape[2]
    slot_cap = pair_blocks.shape[3]
    slot_total = peer_total * slot_cap
    halo_low, halo_high = halos(displacement, "len", 2, 2)
    beam = chain_force(jnp.concatenate([halo_low, displacement, halo_high], axis=2))

    mine_flat = pair_blocks[0, 0, :, :, 0].reshape(slot_total)
    their_flat = pair_blocks[0, 0, :, :, 1].reshape(slot_total)
    smem = pl.BlockSpec(memory_space=pltpu.SMEM)
    vmem = pl.BlockSpec(memory_space=pltpu.VMEM)
    my_rows, lent = pl.pallas_call(
        pack_kernel,
        out_shape=(
            jax.ShapeDtypeStruct((block_total, 4, 128), jnp.float32),
            jax.ShapeDtypeStruct((peer_total * 4 * slot_cap, 128), jnp.float32),
        ),
        in_specs=[smem, smem, smem, smem, smem, vmem],
        out_specs=(vmem, vmem),
    )(anchors.reshape(3 * block_total), seg_live.reshape(block_total), mine_flat, their_flat,
      pair_count[0, 0], displacement)
    remote = lax.all_to_all(
        lent.reshape(peer_total, 4, slot_cap, 128), ("xa", "xb"), split_axis=0, concat_axis=0, tiled=True
    )
    req_ids = remote[:, 3, :, 1].astype(jnp.int32).reshape(slot_total)
    live_from = remote[:, 3, 0, 2].astype(jnp.int32)

    f1, f2 = pl.pallas_call(
        pair_kernel,
        out_shape=(
            jax.ShapeDtypeStruct((block_total, 8, 128), jnp.float32),
            jax.ShapeDtypeStruct((peer_total * 3 * slot_cap, 128), jnp.float32),
        ),
        in_specs=[smem, smem, vmem, vmem, vmem, vmem],
        out_specs=(vmem, vmem),
        scratch_shapes=[pltpu.SMEM((slot_total + slot_step,), jnp.int32)] * 2,
    )(live_from, req_ids, my_rows, remote.reshape(peer_total * 4 * slot_cap, 128), halo_low, halo_high)

    returned = lax.all_to_all(
        f2.reshape(peer_total, 3, slot_cap, 128), ("xa", "xb"), split_axis=0, concat_axis=0, tiled=True
    )
    new_velocity, new_displacement = pl.pallas_call(
        functools.partial(back_kernel, slot_cap),
        out_shape=(
            jax.ShapeDtypeStruct(velocity.shape, jnp.float32),
            jax.ShapeDtypeStruct(displacement.shape, jnp.float32),
        ),
        in_specs=[smem, smem, vmem, vmem, vmem, vmem, vmem],
        out_specs=(vmem, vmem),
        scratch_shapes=[pltpu.VMEM((block_total * 8, 128), jnp.float32)],
    )(mine_flat, pair_count[0, 0], f1.reshape(block_total * 8, 128), returned.reshape(peer_total * 3 * slot_cap, 128),
      velocity, displacement, beam)
    return (new_velocity, new_displacement)


def solution(mesh):
    in_specs = (
        P(None, ("xa", "xb"), "len"),
        P(None, ("xa", "xb"), "len"),
        P(None, ("xa", "xb")),
        P(("xa", "xb"), "len"),
        P("len", ("xa", "xb"), None, None, None),
        P("len", ("xa", "xb"), None),
    )
    out_specs = (P(None, ("xa", "xb"), "len"), P(None, ("xa", "xb"), "len"))
    return jax.shard_map(local, mesh=mesh, in_specs=in_specs, out_specs=out_specs, check_vma=False)
```

```python
import functools

import jax
import jax.numpy as jnp
from jax import lax
from jax.experimental import pallas as pl
from jax.experimental.pallas import tpu as pltpu
from jax.sharding import PartitionSpec as P

spacing = 1.0 / 128.0
axial_stiff = 1.0
bend_stiff = 0.25
contact_stiff = 1.0 / 16.0
time_step = 0.2
damping = 0.9
masked_far = 1.0e4
HIGH = lax.Precision.HIGH
tile_group = 32
slot_step = 8


def halos(block, axis, dim, width):
    count = lax.axis_size(axis)
    forward = [(i, i + 1) for i in range(count - 1)]
    backward = [(target, source) for source, target in forward]
    low = lax.ppermute(
        lax.slice_in_dim(block, block.shape[dim] - width, None, axis=dim), axis, forward
    )
    high = lax.ppermute(lax.slice_in_dim(block, 0, width, axis=dim), axis, backward)
    return low, high


def chain_force(padded):
    center = padded[:, :, 2:-2]
    next_one = padded[:, :, 3:-1]
    prev_one = padded[:, :, 1:-3]
    next_two = padded[:, :, 4:]
    prev_two = padded[:, :, :-4]
    axial = next_one - 2.0 * center + prev_one
    bending = next_two - 4.0 * next_one + 6.0 * center - 4.0 * prev_one + prev_two
    return axial_stiff * axial - bend_stiff * bending


def split3(v):
    hi = v.astype(jnp.bfloat16).astype(jnp.float32)
    rest = v - hi
    mid = rest.astype(jnp.bfloat16).astype(jnp.float32)
    lo = (rest - mid).astype(jnp.bfloat16).astype(jnp.float32)
    return hi, mid, lo


def stack_rows(rows):
    row = lax.broadcasted_iota(jnp.int32, (8, 128), 0)
    groups = []
    for g in range(4):
        acc = jnp.zeros((8, 128), jnp.float32)
        for r, v in enumerate(rows[8 * g:8 * g + 8]):
            acc = acc + jnp.where(row == r, jnp.broadcast_to(v, (8, 128)), 0.0)
        groups.append(acc)
    return jnp.concatenate(groups, axis=0)


def rows_of(x, near):
    lane = lax.broadcasted_iota(jnp.int32, (1, 128), 1).astype(jnp.float32)
    v = [x[0:1], x[1:2], x[2:3]]
    on = jnp.where(lane < x[3:4, 0:1], 1.0, 0.0)
    norm = v[0] * v[0] + v[1] * v[1] + v[2] * v[2]
    far = masked_far * (1.0 - on)
    one = jnp.ones((1, 128), jnp.float32)
    rows = []
    if near:
        for c in range(3):
            hi, mid, lo = split3(v[c])
            rows += [hi, mid, hi, mid, lo, hi]
        rows += [one, one, one] + list(split3(norm)) + [one, far]
        return stack_rows(rows), None
    for c in range(3):
        hi, mid, lo = split3(-2.0 * v[c])
        rows += [hi, hi, mid, mid, hi, lo]
    rows += list(split3(norm)) + [one, one, one] + [far, one]
    row = lax.broadcasted_iota(jnp.int32, (8, 128), 0)
    rq = (jnp.where(row == 0, jnp.broadcast_to(v[0], (8, 128)), 0.0)
          + jnp.where(row == 1, jnp.broadcast_to(v[1], (8, 128)), 0.0)
          + jnp.where(row == 2, jnp.broadcast_to(v[2], (8, 128)), 0.0) + jnp.where(row == 3, 1.0, 0.0))
    return stack_rows(rows), rq


def side_rows(x):
    row = lax.broadcasted_iota(jnp.int32, (8, 128), 0)
    return (jnp.where(row == 0, jnp.broadcast_to(x[0:1], (8, 128)), 0.0)
            + jnp.where(row == 1, jnp.broadcast_to(x[1:2], (8, 128)), 0.0)
            + jnp.where(row == 2, jnp.broadcast_to(x[2:3], (8, 128)), 0.0) + jnp.where(row == 3, 1.0, 0.0))


def piece_sums(rows, w_hi, w_lo, axis):
    hi, mid, lo = split3(rows)
    count = rows.shape[0]
    dims = (((1,), (axis,)), ((), ()))
    by_hi = lax.dot_general(
        jnp.concatenate([hi, mid, lo], axis=0), w_hi, dims, preferred_element_type=jnp.float32
    )
    by_lo = lax.dot_general(
        jnp.concatenate([hi, mid], axis=0), w_lo, dims, preferred_element_type=jnp.float32
    )
    return (by_hi[0:count] + by_hi[count:2 * count] + by_hi[2 * count:]) + (
        by_lo[0:count] + by_lo[count:]
    )


def tile_two(m_a, m_b, s_a, s_b, rd_a, rd_b, rq_a, rq_b):
    zero = jnp.zeros(m_a.shape, jnp.float32)
    mine = jnp.concatenate(
        [jnp.concatenate([m_a, zero], axis=1), jnp.concatenate([zero, m_b], axis=1)], axis=0
    )
    dist = lax.dot_general(
        jnp.concatenate([rd_a, rd_b], axis=0), mine, (((0,), (0,)), ((), ())),
        preferred_element_type=jnp.float32,
    )
    w = jnp.exp(-dist)
    zero = jnp.zeros((8, 128), jnp.float32)
    side = jnp.concatenate(
        [jnp.concatenate([s_a, zero], axis=1), jnp.concatenate([zero, s_b], axis=1)], axis=0
    )
    w_hi = w.astype(jnp.bfloat16).astype(jnp.float32)
    w_lo = (w - w_hi).astype(jnp.bfloat16).astype(jnp.float32)
    f1 = piece_sums(jnp.concatenate([rq_a, rq_b], axis=0), w_hi, w_lo, 0)
    f2 = piece_sums(side, w_hi, w_lo, 1)
    f1 = f1 * contact_stiff
    f2 = f2 * contact_stiff
    out = []
    for m, rq, g1, g2 in ((s_a, rq_a, f1[0:8, 0:128], f2[0:8]), (s_b, rq_b, f1[8:16, 128:256], f2[8:16])):
        out.append((m * g1[3:4, :] - g1, (rq * g2[3:4, :] - g2)[0:3, :]))
    return out


def peer_row(slot, rows, cap):
    return (slot // cap) * rows * cap + slot % cap


def pack_kernel(anc_ref, seg_ref, mine_ref, their_ref, cnt_ref, disp_ref, rows_ref, lent_ref):
    peers = cnt_ref.shape[0]
    cap = mine_ref.shape[0] // peers
    blocks = rows_ref.shape[0]
    row = lax.broadcasted_iota(jnp.int32, (4, 128), 0)
    lane = lax.broadcasted_iota(jnp.int32, (4, 128), 1)
    height = lax.broadcasted_iota(jnp.int32, (1, 128), 1).astype(jnp.float32) * spacing

    def block(g, carry):
        for k in range(slot_step):
            b = g * slot_step + k
            x = jnp.where((row == 3) & (lane == 0), seg_ref[b].astype(jnp.float32), 0.0)
            for c in range(3):
                v = disp_ref[c, pl.ds(b, 1), :] + anc_ref[c * blocks + b]
                if c == 2:
                    v = v + height
                x = jnp.where(row == c, jnp.broadcast_to(v, (4, 128)), x)
            rows_ref[b] = x
        return carry

    lax.fori_loop(0, blocks // slot_step, block, 0)

    def peer(d, carry):
        live = cnt_ref[d]

        sent = jnp.clip(live, 1, cap)

        def step(g, carry):
            for k in range(slot_step):
                c = jnp.minimum(g * slot_step + k, sent - 1)
                s = d * cap + c
                x = rows_ref[jnp.clip(mine_ref[s], 0, blocks - 1)]
                x = jnp.where((row == 3) & (lane == 1), their_ref[s].astype(jnp.float32), x)
                x = jnp.where((row == 3) & (lane == 2), live.astype(jnp.float32), x)
                lent_ref[pl.ds(d * 4 * cap + c, 4, stride=cap), :] = x
            return carry

        return lax.fori_loop(0, (sent + slot_step - 1) // slot_step, step, carry)

    lax.fori_loop(0, peers, peer, 0)


def pair_kernel(cnt_ref, req_ref, m_ref, rem_ref, low_ref, high_ref, f1_ref, f2_ref, lb_ref, ls_ref):
    f1_ref[...] = jnp.zeros(f1_ref.shape, f1_ref.dtype)
    peers = cnt_ref.shape[0]
    cap = req_ref.shape[0] // peers
    blocks = m_ref.shape[0]

    def listed(d, n):
        live = jnp.clip(cnt_ref[d], 0, cap)

        def held(g, n):
            for k in range(slot_step):
                c = jnp.minimum(g * slot_step + k, cap - 1)
                lb_ref[n + k] = jnp.clip(req_ref[d * cap + c], 0, blocks - 1)
                ls_ref[n + k] = d * cap + c
            return n + jnp.minimum(slot_step, live - g * slot_step)

        return lax.fori_loop(0, (live + slot_step - 1) // slot_step, held, n)

    total = lax.fori_loop(0, peers, listed, 0)
    last = jnp.maximum(total - 1, 0)

    def group(g, carry):
        done = []
        for k in range(0, tile_group, 2):
            picked = []
            for t in (g * tile_group + k, g * tile_group + k + 1):
                at = jnp.minimum(t, last)
                picked.append((t, lb_ref[at], ls_ref[at]))
            (t_a, b_a, s_a), (t_b, b_b, s_b) = picked
            rd_a, rq_a = rows_of(rem_ref[pl.ds(peer_row(s_a, 4, cap), 4, stride=cap), :], False)
            rd_b, rq_b = rows_of(rem_ref[pl.ds(peer_row(s_b, 4, cap), 4, stride=cap), :], False)
            x_a = m_ref[b_a]
            x_b = m_ref[b_b]
            pair = tile_two(
                rows_of(x_a, True)[0], rows_of(x_b, True)[0], side_rows(x_a), side_rows(x_b),
                rd_a, rd_b, rq_a, rq_b,
            )
            for (t, b, slot), (on_first, on_second) in zip(picked, pair):
                done.append((b, slot, jnp.where(t < total, on_first, 0.0), on_second))
        for b, slot, on_first, on_second in done:
            f1_ref[b] = f1_ref[b] + on_first
            f2_ref[pl.ds(peer_row(slot, 3, cap), 3, stride=cap), :] = on_second
        return carry

    lax.fori_loop(0, (total + tile_group - 1) // tile_group, group, 0)


def back_kernel(cap, mine_ref, cnt_ref, f1_ref, ret_ref, vel_ref, disp_ref, beam_ref, nv_ref, nd_ref, acc_ref):
    acc_ref[...] = f1_ref[...]
    blocks = vel_ref.shape[1]

    def peer(d, carry):
        live = jnp.clip(cnt_ref[d], 0, cap)

        def step(g, carry):
            for k in range(slot_step):
                c = g * slot_step + k
                at = jnp.minimum(c, live - 1)
                b = jnp.clip(mine_ref[d * cap + at], 0, blocks - 1)
                start = pl.multiple_of(b * 8, 8)
                got = ret_ref[pl.ds(d * 3 * cap + at, 3, stride=cap), :]
                acc_ref[pl.ds(start, 3), :] = acc_ref[pl.ds(start, 3), :] + jnp.where(c < live, got, 0.0)
            return carry

        return lax.fori_loop(0, (live + slot_step - 1) // slot_step, step, carry)

    lax.fori_loop(0, cnt_ref.shape[0], peer, 0)
    for c in range(3):
        contact = acc_ref[pl.ds(c, blocks, stride=8), :]
        new_velocity = damping * vel_ref[c] + time_step * (beam_ref[c] + contact)
        nv_ref[c] = new_velocity
        nd_ref[c] = disp_ref[c] + time_step * new_velocity


def local(displacement, velocity, anchors, seg_live, pair_blocks, pair_count):
    seg_len = displacement.shape[2]
    fibre_count = displacement.shape[1]
    per_fibre = seg_len // 128
    block_total = fibre_count * per_fibre
    peer_total = pair_blocks.shape[2]
    slot_cap = pair_blocks.shape[3]
    slot_total = peer_total * slot_cap
    halo_low, halo_high = halos(displacement, "len", 2, 2)
    beam = chain_force(jnp.concatenate([halo_low, displacement, halo_high], axis=2))

    mine_flat = pair_blocks[0, 0, :, :, 0].reshape(slot_total)
    their_flat = pair_blocks[0, 0, :, :, 1].reshape(slot_total)
    smem = pl.BlockSpec(memory_space=pltpu.SMEM)
    vmem = pl.BlockSpec(memory_space=pltpu.VMEM)
    my_rows, lent = pl.pallas_call(
        pack_kernel,
        out_shape=(
            jax.ShapeDtypeStruct((block_total, 4, 128), jnp.float32),
            jax.ShapeDtypeStruct((peer_total * 4 * slot_cap, 128), jnp.float32),
        ),
        in_specs=[smem, smem, smem, smem, smem, vmem],
        out_specs=(vmem, vmem),
    )(anchors.reshape(3 * block_total), seg_live.reshape(block_total), mine_flat, their_flat,
      pair_count[0, 0], displacement)
    remote = lax.all_to_all(
        lent.reshape(peer_total, 4, slot_cap, 128), ("xa", "xb"), split_axis=0, concat_axis=0, tiled=True
    )
    req_ids = remote[:, 3, :, 1].astype(jnp.int32).reshape(slot_total)
    live_from = remote[:, 3, 0, 2].astype(jnp.int32)

    f1, f2 = pl.pallas_call(
        pair_kernel,
        out_shape=(
            jax.ShapeDtypeStruct((block_total, 8, 128), jnp.float32),
            jax.ShapeDtypeStruct((peer_total * 3 * slot_cap, 128), jnp.float32),
        ),
        in_specs=[smem, smem, vmem, vmem, vmem, vmem],
        out_specs=(vmem, vmem),
        scratch_shapes=[pltpu.SMEM((slot_total + slot_step,), jnp.int32)] * 2,
    )(live_from, req_ids, my_rows, remote.reshape(peer_total * 4 * slot_cap, 128), halo_low, halo_high)

    returned = lax.all_to_all(
        f2.reshape(peer_total, 3, slot_cap, 128), ("xa", "xb"), split_axis=0, concat_axis=0, tiled=True
    )
    new_velocity, new_displacement = pl.pallas_call(
        functools.partial(back_kernel, slot_cap),
        out_shape=(
            jax.ShapeDtypeStruct(velocity.shape, jnp.float32),
            jax.ShapeDtypeStruct(displacement.shape, jnp.float32),
        ),
        in_specs=[smem, smem, vmem, vmem, vmem, vmem, vmem],
        out_specs=(vmem, vmem),
        scratch_shapes=[pltpu.VMEM((block_total * 8, 128), jnp.float32)],
    )(mine_flat, pair_count[0, 0], f1.reshape(block_total * 8, 128), returned.reshape(peer_total * 3 * slot_cap, 128),
      velocity, displacement, beam)
    return (new_velocity, new_displacement)


def solution(mesh):
    in_specs = (
        P(None, ("xa", "xb"), "len"),
        P(None, ("xa", "xb"), "len"),
        P(None, ("xa", "xb")),
        P(("xa", "xb"), "len"),
        P("len", ("xa", "xb"), None, None, None),
        P("len", ("xa", "xb"), None),
    )
    out_specs = (P(None, ("xa", "xb"), "len"), P(None, ("xa", "xb"), "len"))
    return jax.shard_map(local, mesh=mesh, in_specs=in_specs, out_specs=out_specs, check_vma=False)
```

```python
import functools

import jax
import jax.numpy as jnp
from jax import lax
from jax.experimental import pallas as pl
from jax.experimental.pallas import tpu as pltpu
from jax.sharding import PartitionSpec as P

spacing = 1.0 / 128.0
axial_stiff = 1.0
bend_stiff = 0.25
contact_stiff = 1.0 / 16.0
time_step = 0.2
damping = 0.9
masked_far = 1.0e4
HIGH = lax.Precision.HIGH
tile_group = 32
slot_step = 16


def halos(block, axis, dim, width):
    count = lax.axis_size(axis)
    forward = [(i, i + 1) for i in range(count - 1)]
    backward = [(target, source) for source, target in forward]
    low = lax.ppermute(
        lax.slice_in_dim(block, block.shape[dim] - width, None, axis=dim), axis, forward
    )
    high = lax.ppermute(lax.slice_in_dim(block, 0, width, axis=dim), axis, backward)
    return low, high


def chain_force(padded):
    center = padded[:, :, 2:-2]
    next_one = padded[:, :, 3:-1]
    prev_one = padded[:, :, 1:-3]
    next_two = padded[:, :, 4:]
    prev_two = padded[:, :, :-4]
    axial = next_one - 2.0 * center + prev_one
    bending = next_two - 4.0 * next_one + 6.0 * center - 4.0 * prev_one + prev_two
    return axial_stiff * axial - bend_stiff * bending


def split3(v):
    hi = v.astype(jnp.bfloat16).astype(jnp.float32)
    rest = v - hi
    mid = rest.astype(jnp.bfloat16).astype(jnp.float32)
    lo = (rest - mid).astype(jnp.bfloat16).astype(jnp.float32)
    return hi, mid, lo


def stack_rows(rows):
    row = lax.broadcasted_iota(jnp.int32, (8, 128), 0)
    groups = []
    for g in range(4):
        acc = jnp.zeros((8, 128), jnp.float32)
        for r, v in enumerate(rows[8 * g:8 * g + 8]):
            acc = acc + jnp.where(row == r, jnp.broadcast_to(v, (8, 128)), 0.0)
        groups.append(acc)
    return jnp.concatenate(groups, axis=0)


def rows_of(x, near):
    lane = lax.broadcasted_iota(jnp.int32, (1, 128), 1).astype(jnp.float32)
    v = [x[0:1], x[1:2], x[2:3]]
    on = jnp.where(lane < x[3:4, 0:1], 1.0, 0.0)
    norm = v[0] * v[0] + v[1] * v[1] + v[2] * v[2]
    far = masked_far * (1.0 - on)
    one = jnp.ones((1, 128), jnp.float32)
    rows = []
    if near:
        for c in range(3):
            hi, mid, lo = split3(v[c])
            rows += [hi, mid, hi, mid, lo, hi]
        rows += [one, one, one] + list(split3(norm)) + [one, far]
        return stack_rows(rows), None
    for c in range(3):
        hi, mid, lo = split3(-2.0 * v[c])
        rows += [hi, hi, mid, mid, hi, lo]
    rows += list(split3(norm)) + [one, one, one] + [far, one]
    row = lax.broadcasted_iota(jnp.int32, (8, 128), 0)
    rq = (jnp.where(row == 0, jnp.broadcast_to(v[0], (8, 128)), 0.0)
          + jnp.where(row == 1, jnp.broadcast_to(v[1], (8, 128)), 0.0)
          + jnp.where(row == 2, jnp.broadcast_to(v[2], (8, 128)), 0.0) + jnp.where(row == 3, 1.0, 0.0))
    return stack_rows(rows), rq


def side_rows(x):
    row = lax.broadcasted_iota(jnp.int32, (8, 128), 0)
    return (jnp.where(row == 0, jnp.broadcast_to(x[0:1], (8, 128)), 0.0)
            + jnp.where(row == 1, jnp.broadcast_to(x[1:2], (8, 128)), 0.0)
            + jnp.where(row == 2, jnp.broadcast_to(x[2:3], (8, 128)), 0.0) + jnp.where(row == 3, 1.0, 0.0))


def piece_sums(rows, w_hi, w_lo, axis):
    hi, mid, lo = split3(rows)
    count = rows.shape[0]
    dims = (((1,), (axis,)), ((), ()))
    by_hi = lax.dot_general(
        jnp.concatenate([hi, mid, lo], axis=0), w_hi, dims, preferred_element_type=jnp.float32
    )
    by_lo = lax.dot_general(
        jnp.concatenate([hi, mid], axis=0), w_lo, dims, preferred_element_type=jnp.float32
    )
    return (by_hi[0:count] + by_hi[count:2 * count] + by_hi[2 * count:]) + (
        by_lo[0:count] + by_lo[count:]
    )


def tile_two(m_a, m_b, s_a, s_b, rd_a, rd_b, rq_a, rq_b):
    zero = jnp.zeros(m_a.shape, jnp.float32)
    mine = jnp.concatenate(
        [jnp.concatenate([m_a, zero], axis=1), jnp.concatenate([zero, m_b], axis=1)], axis=0
    )
    dist = lax.dot_general(
        jnp.concatenate([rd_a, rd_b], axis=0), mine, (((0,), (0,)), ((), ())),
        preferred_element_type=jnp.float32,
    )
    w = jnp.exp(-dist)
    zero = jnp.zeros((8, 128), jnp.float32)
    side = jnp.concatenate(
        [jnp.concatenate([s_a, zero], axis=1), jnp.concatenate([zero, s_b], axis=1)], axis=0
    )
    w_hi = w.astype(jnp.bfloat16).astype(jnp.float32)
    w_lo = (w - w_hi).astype(jnp.bfloat16).astype(jnp.float32)
    f1 = piece_sums(jnp.concatenate([rq_a, rq_b], axis=0), w_hi, w_lo, 0)
    f2 = piece_sums(side, w_hi, w_lo, 1)
    f1 = f1 * contact_stiff
    f2 = f2 * contact_stiff
    out = []
    for m, rq, g1, g2 in ((s_a, rq_a, f1[0:8, 0:128], f2[0:8]), (s_b, rq_b, f1[8:16, 128:256], f2[8:16])):
        out.append((m * g1[3:4, :] - g1, (rq * g2[3:4, :] - g2)[0:3, :]))
    return out


def peer_row(slot, rows, cap):
    return (slot // cap) * rows * cap + slot % cap


def pack_kernel(anc_ref, seg_ref, mine_ref, their_ref, cnt_ref, disp_ref, rows_ref, lent_ref):
    peers = cnt_ref.shape[0]
    cap = mine_ref.shape[0] // peers
    blocks = rows_ref.shape[0]
    row = lax.broadcasted_iota(jnp.int32, (4, 128), 0)
    lane = lax.broadcasted_iota(jnp.int32, (4, 128), 1)
    height = lax.broadcasted_iota(jnp.int32, (1, 128), 1).astype(jnp.float32) * spacing

    def block(g, carry):
        for k in range(slot_step):
            b = g * slot_step + k
            x = jnp.where((row == 3) & (lane == 0), seg_ref[b].astype(jnp.float32), 0.0)
            for c in range(3):
                v = disp_ref[c, pl.ds(b, 1), :] + anc_ref[c * blocks + b]
                if c == 2:
                    v = v + height
                x = jnp.where(row == c, jnp.broadcast_to(v, (4, 128)), x)
            rows_ref[b] = x
        return carry

    lax.fori_loop(0, blocks // slot_step, block, 0)

    lent_ref[...] = jnp.zeros(lent_ref.shape, lent_ref.dtype)

    def peer(d, carry):
        live = cnt_ref[d]

        sent = jnp.clip(live, 1, cap)

        def step(g, carry):
            for k in range(slot_step):
                c = jnp.minimum(g * slot_step + k, sent - 1)
                s = d * cap + c
                x = rows_ref[jnp.clip(mine_ref[s], 0, blocks - 1)]
                x = jnp.where((row == 3) & (lane == 1), their_ref[s].astype(jnp.float32), x)
                x = jnp.where((row == 3) & (lane == 2), live.astype(jnp.float32), x)
                lent_ref[pl.ds(d * 4 * cap + c, 4, stride=cap), :] = x
            return carry

        return lax.fori_loop(0, (sent + slot_step - 1) // slot_step, step, carry)

    lax.fori_loop(0, peers, peer, 0)


def pair_kernel(cnt_ref, req_ref, m_ref, rem_ref, low_ref, high_ref, f1_ref, f2_ref, lb_ref, ls_ref):
    f1_ref[...] = jnp.zeros(f1_ref.shape, f1_ref.dtype)
    f2_ref[...] = jnp.zeros(f2_ref.shape, f2_ref.dtype)
    peers = cnt_ref.shape[0]
    cap = req_ref.shape[0] // peers
    blocks = m_ref.shape[0]

    def listed(d, n):
        live = jnp.clip(cnt_ref[d], 0, cap)

        def held(g, n):
            for k in range(slot_step):
                c = jnp.minimum(g * slot_step + k, cap - 1)
                lb_ref[n + k] = jnp.clip(req_ref[d * cap + c], 0, blocks - 1)
                ls_ref[n + k] = d * cap + c
            return n + jnp.minimum(slot_step, live - g * slot_step)

        return lax.fori_loop(0, (live + slot_step - 1) // slot_step, held, n)

    total = lax.fori_loop(0, peers, listed, 0)
    last = jnp.maximum(total - 1, 0)

    def group(g, carry):
        done = []
        for k in range(0, tile_group, 2):
            picked = []
            for t in (g * tile_group + k, g * tile_group + k + 1):
                at = jnp.minimum(t, last)
                picked.append((t, lb_ref[at], ls_ref[at]))
            (t_a, b_a, s_a), (t_b, b_b, s_b) = picked
            rd_a, rq_a = rows_of(rem_ref[pl.ds(peer_row(s_a, 4, cap), 4, stride=cap), :], False)
            rd_b, rq_b = rows_of(rem_ref[pl.ds(peer_row(s_b, 4, cap), 4, stride=cap), :], False)
            x_a = m_ref[b_a]
            x_b = m_ref[b_b]
            pair = tile_two(
                rows_of(x_a, True)[0], rows_of(x_b, True)[0], side_rows(x_a), side_rows(x_b),
                rd_a, rd_b, rq_a, rq_b,
            )
            for (t, b, slot), (on_first, on_second) in zip(picked, pair):
                done.append((b, slot, jnp.where(t < total, on_first, 0.0), on_second))
        for b, slot, on_first, on_second in done:
            f1_ref[b] = f1_ref[b] + on_first
            f2_ref[pl.ds(peer_row(slot, 3, cap), 3, stride=cap), :] = on_second
        return carry

    lax.fori_loop(0, (total + tile_group - 1) // tile_group, group, 0)


def back_kernel(cap, mine_ref, cnt_ref, f1_ref, ret_ref, vel_ref, disp_ref, beam_ref, nv_ref, nd_ref, acc_ref):
    acc_ref[...] = f1_ref[...]
    blocks = vel_ref.shape[1]

    def peer(d, carry):
        live = jnp.clip(cnt_ref[d], 0, cap)

        def step(g, carry):
            for k in range(slot_step):
                c = g * slot_step + k
                at = jnp.minimum(c, live - 1)
                b = jnp.clip(mine_ref[d * cap + at], 0, blocks - 1)
                start = pl.multiple_of(b * 8, 8)
                got = ret_ref[pl.ds(d * 3 * cap + at, 3, stride=cap), :]
                acc_ref[pl.ds(start, 3), :] = acc_ref[pl.ds(start, 3), :] + jnp.where(c < live, got, 0.0)
            return carry

        return lax.fori_loop(0, (live + slot_step - 1) // slot_step, step, carry)

    lax.fori_loop(0, cnt_ref.shape[0], peer, 0)
    for c in range(3):
        contact = acc_ref[pl.ds(c, blocks, stride=8), :]
        new_velocity = damping * vel_ref[c] + time_step * (beam_ref[c] + contact)
        nv_ref[c] = new_velocity
        nd_ref[c] = disp_ref[c] + time_step * new_velocity


def local(displacement, velocity, anchors, seg_live, pair_blocks, pair_count):
    seg_len = displacement.shape[2]
    fibre_count = displacement.shape[1]
    per_fibre = seg_len // 128
    block_total = fibre_count * per_fibre
    peer_total = pair_blocks.shape[2]
    slot_cap = pair_blocks.shape[3]
    slot_total = peer_total * slot_cap
    halo_low, halo_high = halos(displacement, "len", 2, 2)
    beam = chain_force(jnp.concatenate([halo_low, displacement, halo_high], axis=2))

    mine_flat = pair_blocks[0, 0, :, :, 0].reshape(slot_total)
    their_flat = pair_blocks[0, 0, :, :, 1].reshape(slot_total)
    smem = pl.BlockSpec(memory_space=pltpu.SMEM)
    vmem = pl.BlockSpec(memory_space=pltpu.VMEM)
    my_rows, lent = pl.pallas_call(
        pack_kernel,
        out_shape=(
            jax.ShapeDtypeStruct((block_total, 4, 128), jnp.float32),
            jax.ShapeDtypeStruct((peer_total * 4 * slot_cap, 128), jnp.float32),
        ),
        in_specs=[smem, smem, smem, smem, smem, vmem],
        out_specs=(vmem, vmem),
    )(anchors.reshape(3 * block_total), seg_live.reshape(block_total), mine_flat, their_flat,
      pair_count[0, 0], displacement)
    remote = lax.all_to_all(
        lent.reshape(peer_total, 4, slot_cap, 128), ("xa", "xb"), split_axis=0, concat_axis=0, tiled=True
    )
    req_ids = remote[:, 3, :, 1].astype(jnp.int32).reshape(slot_total)
    live_from = remote[:, 3, 0, 2].astype(jnp.int32)

    f1, f2 = pl.pallas_call(
        pair_kernel,
        out_shape=(
            jax.ShapeDtypeStruct((block_total, 8, 128), jnp.float32),
            jax.ShapeDtypeStruct((peer_total * 3 * slot_cap, 128), jnp.float32),
        ),
        in_specs=[smem, smem, vmem, vmem, vmem, vmem],
        out_specs=(vmem, vmem),
        scratch_shapes=[pltpu.SMEM((slot_total + slot_step,), jnp.int32)] * 2,
    )(live_from, req_ids, my_rows, remote.reshape(peer_total * 4 * slot_cap, 128), halo_low, halo_high)

    returned = lax.all_to_all(
        f2.reshape(peer_total, 3, slot_cap, 128), ("xa", "xb"), split_axis=0, concat_axis=0, tiled=True
    )
    new_velocity, new_displacement = pl.pallas_call(
        functools.partial(back_kernel, slot_cap),
        out_shape=(
            jax.ShapeDtypeStruct(velocity.shape, jnp.float32),
            jax.ShapeDtypeStruct(displacement.shape, jnp.float32),
        ),
        in_specs=[smem, smem, vmem, vmem, vmem, vmem, vmem],
        out_specs=(vmem, vmem),
        scratch_shapes=[pltpu.VMEM((block_total * 8, 128), jnp.float32)],
    )(mine_flat, pair_count[0, 0], f1.reshape(block_total * 8, 128), returned.reshape(peer_total * 3 * slot_cap, 128),
      velocity, displacement, beam)
    return (new_velocity, new_displacement)


def solution(mesh):
    in_specs = (
        P(None, ("xa", "xb"), "len"),
        P(None, ("xa", "xb"), "len"),
        P(None, ("xa", "xb")),
        P(("xa", "xb"), "len"),
        P("len", ("xa", "xb"), None, None, None),
        P("len", ("xa", "xb"), None),
    )
    out_specs = (P(None, ("xa", "xb"), "len"), P(None, ("xa", "xb"), "len"))
    return jax.shard_map(local, mesh=mesh, in_specs=in_specs, out_specs=out_specs, check_vma=False)
```
